32 devices in a mesh: src: 8 (over z, core), tgt: 4 (over y, x).
Axes of the slice: x: 2, y: 2, z: 4, core: 2. Of those that a mesh axis runs over, the one named last changes fastest.
Arguments:
- samples: bfloat16 [512, 128, 512], P(('src', 'tgt')), may hold values from -6 to 6
- echoes: bfloat16 [512, 128, 512], P(('src', 'tgt')), may hold values from -6 to 6
- leaf_maps: bfloat16 [512, 64, 128], P(('src', 'tgt')), may hold values from -0.5 to 0.5
- local_blocks: bfloat16 [4, 512, 64, 256], P(None, ('src', 'tgt')), may hold values from -0.375 to 0.375
- cross_blocks: bfloat16 [2, 512, 64, 256], P(None, 'src'), may hold values from -0.375 to 0.375
- outer_blocks: bfloat16 [3, 512, 64, 256], P(None, ('src', 'tgt')), may hold values from -0.375 to 0.375
- spread_maps: bfloat16 [512, 64, 128], P(('src', 'tgt')), may hold values from -0.5 to 0.5
Outputs:
- image_field: bfloat16 [512, 128, 512], P(('src', 'tgt'))
- aperture_field: bfloat16 [512, 128, 512], P(('src', 'tgt'))
The draws below stay inside these ranges and needn't reach their ends.
All inputs are finite; a program needn't handle non-finite values.
Results may differ from the reference program's by a relative error of at most 0.018.
Values may be sent and summed in bfloat16 or wider, within the bound.
No kernel may reach another device: no remote copies, remote signals or barrier semaphores. Data moves between devices by JAX's collectives and lax.ppermute only.
A program may use at most 128 MiB of HBM per device.

```python
import jax
import jax.numpy as jnp

RANK = 64
LEAF = 64
NRHS = 512
LOCAL = 4
TBITS = 2
SBITS = 3
BOXES = 512


def level_of(rng, dims, shards, smallest, largest):
    level = 1.0
    for dim, shards_of in shards:
        steps = jax.random.uniform(jax.random.fold_in(jax.random.fold_in(rng, 6), dim), (shards_of,), jnp.float32, smallest / len(shards), largest / len(shards))
        level = level * jnp.repeat(jnp.exp(steps), dims[dim] // shards_of).reshape((-1,) + (1,) * (len(dims) - 1 - dim))
    return level


def centred(stream_key, shape, width, bound, split=(), dtype=jnp.bfloat16):
    factor_of = level_of(stream_key, shape, split, -0.22, 0.18) if split else 1.0
    drawn = jax.random.normal(stream_key, shape, jnp.float32) * width * factor_of
    return jnp.minimum(jnp.maximum(drawn, -bound), bound).astype(dtype)


def setup_inputs(seed: int = 0) -> dict:
    streams_of = jax.random.split(jax.random.key(seed), 8)
    samples = centred(streams_of[0], (BOXES, 2 * LEAF, NRHS), 1.0, 6.0, ((0, 32),))
    echoes = centred(streams_of[1], (BOXES, 2 * LEAF, NRHS), 1.0, 6.0, ((0, 32),))
    leaf_maps = centred(streams_of[2], (BOXES, RANK, 2 * LEAF), (2 * LEAF) ** -0.5, 0.5, ((0, 32),))
    local_blocks = centred(streams_of[3], (LOCAL, BOXES, RANK, 4 * RANK), (4 * RANK) ** -0.5, 0.375, ((1, 32),))
    cross_blocks = centred(streams_of[4], (TBITS, BOXES, RANK, 4 * RANK), (4 * RANK) ** -0.5, 0.375, ((1, 8),))
    outer_blocks = centred(streams_of[5], (SBITS, BOXES, RANK, 4 * RANK), (4 * RANK) ** -0.5, 0.375, ((1, 32),))
    spread_maps = centred(streams_of[6], (BOXES, LEAF, 2 * RANK), (2 * RANK) ** -0.5, 0.5, ((0, 32),))
    return dict(samples=samples, echoes=echoes, leaf_maps=leaf_maps, local_blocks=local_blocks, cross_blocks=cross_blocks, outer_blocks=outer_blocks, spread_maps=spread_maps)


def complex_embed(stored):
    half_width = stored.shape[-1] // 2
    real_part = stored[..., :half_width].astype(jnp.float32)
    imag_part = stored[..., half_width:].astype(jnp.float32)
    top_rows = jnp.concatenate([real_part, -imag_part], axis=-1)
    bottom_rows = jnp.concatenate([imag_part, real_part], axis=-1)
    return jnp.concatenate([top_rows, bottom_rows], axis=-2)


def swap_bits(values, upper_bit, lower_bit):
    if upper_bit == lower_bit:
        return values
    shaped = values.reshape((-1, 2, 2 ** (upper_bit - lower_bit - 1), 2, 2 ** lower_bit) + values.shape[1:])
    return jnp.swapaxes(shaped, 1, 3).reshape(values.shape)


def block_weights(blocks, block_side, lower_bit):
    block_width = blocks.shape[-1] // 2
    embedded = complex_embed(blocks[..., block_side * block_width:(block_side + 1) * block_width])
    return embedded.reshape((-1, 2, 2 ** lower_bit) + embedded.shape[1:])


def level_forward(coefficients, blocks, upper_bit, lower_bit):
    permuted = swap_bits(coefficients, upper_bit, lower_bit).astype(jnp.float32)
    grouped = permuted.reshape((-1, 2, 2 ** lower_bit) + permuted.shape[1:])
    updated = jnp.einsum("hjlik,hlkn->hjlin", block_weights(blocks, 0, lower_bit), grouped[:, 0])
    updated = updated + jnp.einsum("hjlik,hlkn->hjlin", block_weights(blocks, 1, lower_bit), grouped[:, 1])
    return updated.reshape(coefficients.shape).astype(jnp.bfloat16)


def level_adjoint(adjoint, blocks, upper_bit, lower_bit):
    grouped = adjoint.astype(jnp.float32).reshape((-1, 2, 2 ** lower_bit) + adjoint.shape[1:])
    back_first = jnp.einsum("hjlik,hjlin->hlkn", block_weights(blocks, 0, lower_bit), grouped)
    back_second = jnp.einsum("hjlik,hjlin->hlkn", block_weights(blocks, 1, lower_bit), grouped)
    permuted = jnp.stack([back_first, back_second], axis=1).reshape(adjoint.shape).astype(jnp.bfloat16)
    return swap_bits(permuted, upper_bit, lower_bit)


def reference(samples, echoes, leaf_maps, local_blocks, cross_blocks, outer_blocks, spread_maps):
    level_plan = [(local_blocks[section_index], section_index, section_index) for section_index in range(LOCAL)]
    level_plan += [(cross_blocks[section_index], LOCAL + section_index, section_index) for section_index in range(TBITS)]
    level_plan += [(outer_blocks[section_index], LOCAL + TBITS + section_index, section_index) for section_index in range(SBITS)]
    leaf_weights = complex_embed(leaf_maps)
    spread_weights = complex_embed(spread_maps)
    coefficients = jnp.einsum("pik,pkn->pin", leaf_weights, samples.astype(jnp.float32)).astype(jnp.bfloat16)
    for blocks, upper_bit, lower_bit in level_plan:
        coefficients = level_forward(coefficients, blocks, upper_bit, lower_bit)
    image_field = jnp.einsum("pik,pkn->pin", spread_weights, coefficients.astype(jnp.float32)).astype(jnp.bfloat16)
    adjoint = jnp.einsum("pki,pkn->pin", spread_weights, echoes.astype(jnp.float32)).astype(jnp.bfloat16)
    for blocks, upper_bit, lower_bit in reversed(level_plan):
        adjoint = level_adjoint(adjoint, blocks, upper_bit, lower_bit)
    aperture_field = jnp.einsum("pki,pkn->pin", leaf_weights, adjoint.astype(jnp.float32)).astype(jnp.bfloat16)
    return image_field, aperture_field
```

```python
import functools

import jax
import jax.numpy as jnp
from jax import lax
from jax.experimental import pallas as pl
from jax.experimental.pallas import tpu as pltpu
from jax.sharding import PartitionSpec as P

CHUNKS = 4


def from_partner(x, axis, apart):
    return lax.ppermute(x, axis, [(i, i ^ 1 << apart) for i in range(lax.axis_size(axis))])


def complex_embed(stored):
    half_width = stored.shape[-1] // 2
    real_part = stored[..., :half_width]
    imag_part = stored[..., half_width:]
    top_rows = jnp.concatenate([real_part, -imag_part], axis=-1)
    bottom_rows = jnp.concatenate([imag_part, real_part], axis=-1)
    return jnp.concatenate([top_rows, bottom_rows], axis=-2)


def pair_embed(blocks):
    return jnp.concatenate([complex_embed(blocks[..., :blocks.shape[-1] // 2]),
                            complex_embed(blocks[..., blocks.shape[-1] // 2:])], axis=-1)


def swap_halves(w):
    half = w.shape[-1] // 2
    return jnp.concatenate([w[..., half:], w[..., :half]], axis=-1)


def adjoint_weights(w, bit):
    count, rows = w.shape[0], w.shape[1]
    low = 2**bit
    shaped = w.reshape(count // (2 * low), 2, low, rows, 2, rows)
    moved = jnp.transpose(shaped, (0, 2, 4, 5, 1, 3))
    return moved.reshape(count // 2, 2, rows, 2 * rows)


def expand(r, bit, j):
    return ((r >> bit) << (bit + 1)) | (j << bit) | (r & ((1 << bit) - 1))


def compress(p, bit):
    return ((p >> (bit + 1)) << bit) | (p & ((1 << bit) - 1))


def mm(w, x):
    return jnp.dot(w, x, preferred_element_type=jnp.float32).astype(jnp.bfloat16)


def write_split(value_of, count, bit, own, stay_ref, leave_ref):
    for p in range(count):
        r = compress(p, bit)
        here = ((p >> bit) & 1) == own

        @pl.when(here)
        def _():
            stay_ref[r] = value_of(p)

        @pl.when(jnp.logical_not(here))
        def _():
            leave_ref[r] = value_of(p)


def read_split(kept_ref, arrived_ref, bit, own):
    def value_of(p):
        r = compress(p, bit)
        return jnp.where(((p >> bit) & 1) == own, kept_ref[r], arrived_ref[r])

    return value_of


def forward_local_kernel(own_ref, samples_ref, leaf_ref, local_ref, stay_ref, leave_ref, buf_a, buf_b,
                         *, count, levels, next_bit):
    for p in range(count):
        buf_a[p] = mm(leaf_ref[p], samples_ref[p])
    src, dst = buf_a, buf_b
    for level in range(levels):
        for r in range(count // 2):
            p0, p1 = expand(r, level, 0), expand(r, level, 1)
            stacked = jnp.concatenate([src[p0], src[p1]], axis=0)
            dst[p0] = mm(local_ref[level, p0], stacked)
            dst[p1] = mm(local_ref[level, p1], stacked)
        src, dst = dst, src
    write_split(lambda p: src[p], count, next_bit, own_ref[0], stay_ref, leave_ref)


def forward_cross_kernel(own_ref, kept_ref, arrived_ref, weight_ref, *rest, count, bit, next_bit, last):
    if last:
        spread_ref, out_ref, buf = rest
    else:
        stay_ref, leave_ref, buf = rest
    for r in range(count // 2):
        stacked = jnp.concatenate([kept_ref[r], arrived_ref[r]], axis=0)
        for j in range(2):
            p = expand(r, bit, j)
            buf[p] = mm(weight_ref[p], stacked)
    if last:
        for p in range(count):
            out_ref[p] = mm(spread_ref[p], buf[p])
    else:
        write_split(lambda p: buf[p], count, next_bit, own_ref[0], stay_ref, leave_ref)


def adjoint_first_kernel(own_ref, echoes_ref, spread_t_ref, weight_ref, kept_ref, leave_ref, buf, *, count, bit):
    for p in range(count):
        buf[p] = mm(spread_t_ref[p], echoes_ref[p])
    for r in range(count // 2):
        stacked = jnp.concatenate([buf[expand(r, bit, 0)], buf[expand(r, bit, 1)]], axis=0)
        kept_ref[r] = mm(weight_ref[r, 0], stacked)
        leave_ref[r] = mm(weight_ref[r, 1], stacked)


def adjoint_cross_kernel(own_ref, prev_kept_ref, prev_arrived_ref, weight_ref, kept_ref, leave_ref,
                         *, count, bit, prev_bit):
    value_of = read_split(prev_kept_ref, prev_arrived_ref, prev_bit, own_ref[0])
    for r in range(count // 2):
        stacked = jnp.concatenate([value_of(expand(r, bit, 0)), value_of(expand(r, bit, 1))], axis=0)
        kept_ref[r] = mm(weight_ref[r, 0], stacked)
        leave_ref[r] = mm(weight_ref[r, 1], stacked)


def adjoint_local_kernel(own_ref, prev_kept_ref, prev_arrived_ref, local_ref, leaf_t_ref, out_ref, buf_a, buf_b,
                         *, count, levels, prev_bit):
    value_of = read_split(prev_kept_ref, prev_arrived_ref, prev_bit, own_ref[0])
    for p in range(count):
        buf_a[p] = value_of(p)
    src, dst = buf_a, buf_b
    for level in reversed(range(levels)):
        for r in range(count // 2):
            stacked = jnp.concatenate([src[expand(r, level, 0)], src[expand(r, level, 1)]], axis=0)
            for b in range(2):
                dst[expand(r, level, b)] = mm(local_ref[level, r, b], stacked)
        src, dst = dst, src
    for p in range(count):
        out_ref[p] = mm(leaf_t_ref[p], src[p])


def whole(shape):
    return pl.BlockSpec(shape, lambda i, own, n=len(shape): (0,) * n)


def column_block(shape, chunk):
    return pl.BlockSpec(shape, lambda i, own, c=chunk: (0, 0, c))


def call(kernel, own, inputs, in_specs, out_shapes, scratch):
    grid_spec = pltpu.PrefetchScalarGridSpec(
        num_scalar_prefetch=1,
        grid=(1,),
        in_specs=in_specs,
        out_specs=[whole(s.shape) for s in out_shapes],
        scratch_shapes=scratch,
    )
    return pl.pallas_call(
        kernel,
        grid_spec=grid_spec,
        out_shape=out_shapes,
        compiler_params=pltpu.CompilerParams(vmem_limit_bytes=48 * 1024 * 1024),
    )(own, *inputs)


def per_device(samples, echoes, leaf_maps, local_blocks, cross_blocks, outer_blocks, spread_maps):
    levels_local = local_blocks.shape[0]
    inner_bits = cross_blocks.shape[0]
    outer_bits = outer_blocks.shape[0]
    count, rows, columns = samples.shape
    width = columns // CHUNKS
    tgt_index = lax.axis_index("tgt")
    src_index = lax.axis_index("src")
    own_group = lax.dynamic_slice_in_dim(cross_blocks, tgt_index * count, count, 1)

    crossing = []
    for bit_number in range(inner_bits):
        crossing.append((own_group[bit_number], bit_number, "tgt", tgt_index >> bit_number & 1))
    for bit_number in range(outer_bits):
        crossing.append((outer_blocks[bit_number], bit_number, "src", src_index >> bit_number & 1))
    owns = [jnp.reshape(own, (1,)).astype(jnp.int32) for _, _, _, own in crossing]

    leaf_weights = complex_embed(leaf_maps)
    spread_weights = complex_embed(spread_maps)
    leaf_t = jnp.swapaxes(leaf_weights, 1, 2)
    spread_t = jnp.swapaxes(spread_weights, 1, 2)
    local_weights = jnp.stack([pair_embed(local_blocks[i]) for i in range(levels_local)])
    local_t = jnp.stack([adjoint_weights(local_weights[i], i) for i in range(levels_local)])
    cross_fwd, cross_adj = [], []
    for blocks, bit, _, own in crossing:
        w = pair_embed(blocks)
        cross_fwd.append(jnp.where(own == 0, w, swap_halves(w)))
        wt = adjoint_weights(w, bit)
        cross_adj.append(jnp.where(own == 0, wt, wt[:, ::-1]))

    block = jax.ShapeDtypeStruct((count, rows, width), jnp.bfloat16)
    half = jax.ShapeDtypeStruct((count // 2, rows, width), jnp.bfloat16)
    half_spec = whole(half.shape)
    n_cross = len(crossing)

    image_parts, aperture_parts = [], []
    for chunk in range(CHUNKS):
        stay, leave = call(
            functools.partial(forward_local_kernel, count=count, levels=levels_local, next_bit=crossing[0][1]),
            owns[0],
            [samples, leaf_weights, local_weights],
            [column_block((count, rows, width), chunk), whole(leaf_weights.shape), whole(local_weights.shape)],
            [half, half],
            [pltpu.VMEM(block.shape, jnp.bfloat16), pltpu.VMEM(block.shape, jnp.bfloat16)],
        )
        for index, (_, bit, axis, _) in enumerate(crossing):
            arrived = from_partner(leave, axis, bit)
            last = index == n_cross - 1
            next_bit = 0 if last else crossing[index + 1][1]
            inputs = [stay, arrived, cross_fwd[index]]
            specs = [half_spec, half_spec, whole(cross_fwd[index].shape)]
            if last:
                inputs.append(spread_weights)
                specs.append(whole(spread_weights.shape))
            result = call(
                functools.partial(forward_cross_kernel, count=count, bit=bit, next_bit=next_bit, last=last),
                owns[index] if last else owns[index + 1],
                inputs,
                specs,
                [block] if last else [half, half],
                [pltpu.VMEM(block.shape, jnp.bfloat16)],
            )
            if last:
                image_parts.append(result[0])
            else:
                stay, leave = result

        top = n_cross - 1
        kept, leave = call(
            functools.partial(adjoint_first_kernel, count=count, bit=crossing[top][1]),
            owns[top],
            [echoes, spread_t, cross_adj[top]],
            [column_block((count, rows, width), chunk), whole(spread_t.shape), whole(cross_adj[top].shape)],
            [half, half],
            [pltpu.VMEM(block.shape, jnp.bfloat16)],
        )
        arrived = from_partner(leave, crossing[top][2], crossing[top][1])
        for index in reversed(range(top)):
            prev_bit = crossing[index + 1][1]
            kept, leave = call(
                functools.partial(adjoint_cross_kernel, count=count, bit=crossing[index][1], prev_bit=prev_bit),
                owns[index + 1],
                [kept, arrived, cross_adj[index]],
                [half_spec, half_spec, whole(cross_adj[index].shape)],
                [half, half],
                [],
            )
            arrived = from_partner(leave, crossing[index][2], crossing[index][1])
        (aperture,) = call(
            functools.partial(adjoint_local_kernel, count=count, levels=levels_local, prev_bit=crossing[0][1]),
            owns[0],
            [kept, arrived, local_t, leaf_t],
            [half_spec, half_spec, whole(local_t.shape), whole(leaf_t.shape)],
            [block],
            [pltpu.VMEM(block.shape, jnp.bfloat16), pltpu.VMEM(block.shape, jnp.bfloat16)],
        )
        aperture_parts.append(aperture)
    image_field = jnp.concatenate(image_parts, axis=-1)
    aperture_field = jnp.concatenate(aperture_parts, axis=-1)
    return (image_field, aperture_field)


def solution(mesh):
    return jax.shard_map(
        per_device,
        mesh=mesh,
        in_specs=(
            P(("src", "tgt"), None, None),
            P(("src", "tgt"), None, None),
            P(("src", "tgt"), None, None),
            P(None, ("src", "tgt"), None, None),
            P(None, "src", None, None),
            P(None, ("src", "tgt"), None, None),
            P(("src", "tgt"), None, None),
        ),
        out_specs=(P(("src", "tgt"), None, None), P(("src", "tgt"), None, None)),
        check_vma=False,
    )
```

```python
import functools

import jax
import jax.numpy as jnp
from jax import lax
from jax.experimental import pallas as pl
from jax.experimental.pallas import tpu as pltpu
from jax.sharding import PartitionSpec as P

CHUNKS = 4


def from_partner(x, axis, apart):
    return lax.ppermute(x, axis, [(i, i ^ 1 << apart) for i in range(lax.axis_size(axis))])


def complex_embed(stored):
    half_width = stored.shape[-1] // 2
    real_part = stored[..., :half_width]
    imag_part = stored[..., half_width:]
    top_rows = jnp.concatenate([real_part, -imag_part], axis=-1)
    bottom_rows = jnp.concatenate([imag_part, real_part], axis=-1)
    return jnp.concatenate([top_rows, bottom_rows], axis=-2)


def expand(r, bit, j):
    return ((r >> bit) << (bit + 1)) | (j << bit) | (r & ((1 << bit) - 1))


def compress(p, bit):
    return ((p >> (bit + 1)) << bit) | (p & ((1 << bit) - 1))


def mm(w, x):
    return jnp.dot(w, x, preferred_element_type=jnp.float32).astype(jnp.bfloat16)


def write_split(value_of, count, bit, own, stay_ref, leave_ref):
    for p in range(count):
        r = compress(p, bit)
        here = ((p >> bit) & 1) == own

        @pl.when(here)
        def _():
            stay_ref[r] = value_of(p)

        @pl.when(jnp.logical_not(here))
        def _():
            leave_ref[r] = value_of(p)


def read_split(kept_ref, arrived_ref, bit, own):
    def value_of(p):
        r = compress(p, bit)
        return jnp.where(((p >> bit) & 1) == own, kept_ref[r], arrived_ref[r])

    return value_of


def forward_local_kernel(own_ref, samples_ref, leaf_ref, local_ref, stay_ref, leave_ref, buf_a, buf_b,
                         *, count, levels, next_bit):
    for p in range(count):
        buf_a[p] = mm(leaf_ref[p], samples_ref[p])
    src, dst = buf_a, buf_b
    for level in range(levels):
        for r in range(count // 2):
            p0, p1 = expand(r, level, 0), expand(r, level, 1)
            stacked = jnp.concatenate([src[p0], src[p1]], axis=0)
            dst[p0] = mm(local_ref[level, p0], stacked)
            dst[p1] = mm(local_ref[level, p1], stacked)
        src, dst = dst, src
    write_split(lambda p: src[p], count, next_bit, own_ref[0], stay_ref, leave_ref)


def forward_cross_kernel(own_ref, kept_ref, arrived_ref, weight_ref, *rest, count, bit, next_bit, last):
    if last:
        spread_ref, out_ref, buf = rest
    else:
        stay_ref, leave_ref, buf = rest
    for r in range(count // 2):
        stacked = jnp.concatenate([kept_ref[r], arrived_ref[r]], axis=0)
        for j in range(2):
            p = expand(r, bit, j)
            buf[p] = mm(weight_ref[p], stacked)
    if last:
        for p in range(count):
            out_ref[p] = mm(spread_ref[p], buf[p])
    else:
        write_split(lambda p: buf[p], count, next_bit, own_ref[0], stay_ref, leave_ref)


def adjoint_first_kernel(own_ref, echoes_ref, spread_t_ref, weight_ref, kept_ref, leave_ref, buf, *, count, bit):
    for p in range(count):
        buf[p] = mm(spread_t_ref[p], echoes_ref[p])
    for r in range(count // 2):
        stacked = jnp.concatenate([buf[expand(r, bit, 0)], buf[expand(r, bit, 1)]], axis=0)
        kept_ref[r] = mm(weight_ref[r, 0], stacked)
        leave_ref[r] = mm(weight_ref[r, 1], stacked)


def adjoint_cross_kernel(own_ref, prev_kept_ref, prev_arrived_ref, weight_ref, kept_ref, leave_ref,
                         *, count, bit, prev_bit):
    value_of = read_split(prev_kept_ref, prev_arrived_ref, prev_bit, own_ref[0])
    for r in range(count // 2):
        stacked = jnp.concatenate([value_of(expand(r, bit, 0)), value_of(expand(r, bit, 1))], axis=0)
        kept_ref[r] = mm(weight_ref[r, 0], stacked)
        leave_ref[r] = mm(weight_ref[r, 1], stacked)


def adjoint_local_kernel(own_ref, prev_kept_ref, prev_arrived_ref, local_ref, leaf_t_ref, out_ref, buf_a, buf_b,
                         *, count, levels, prev_bit):
    value_of = read_split(prev_kept_ref, prev_arrived_ref, prev_bit, own_ref[0])
    for p in range(count):
        buf_a[p] = value_of(p)
    src, dst = buf_a, buf_b
    for level in reversed(range(levels)):
        for r in range(count // 2):
            stacked = jnp.concatenate([src[expand(r, level, 0)], src[expand(r, level, 1)]], axis=0)
            for b in range(2):
                dst[expand(r, level, b)] = mm(local_ref[level, r, b], stacked)
        src, dst = dst, src
    for p in range(count):
        out_ref[p] = mm(leaf_t_ref[p], src[p])


def embed_tile(stored):
    half = stored.shape[-1] // 2
    lane = lax.broadcasted_iota(jnp.int32, stored.shape, 1)
    top = jnp.where(lane < half, stored, -stored)
    bottom = pltpu.roll(stored, half, 1)
    return jnp.concatenate([top, bottom], axis=0)


def transpose_tile(tile):
    return tile.astype(jnp.float32).T.astype(jnp.bfloat16)


def prep_level_kernel(own_ref, blocks_ref, fwd_ref, adj_ref, *, count, bits, flip):
    width = blocks_ref.shape[-1] // 2
    size = 2 * blocks_ref.shape[-2]
    for level, bit in enumerate(bits):
        own = own_ref[level] if flip else 0
        for p in range(count):
            first = embed_tile(blocks_ref[level, p, :, :width])
            second = embed_tile(blocks_ref[level, p, :, width:])
            fwd_ref[level, p, :, :size] = jnp.where(own == 0, first, second)
            fwd_ref[level, p, :, size:] = jnp.where(own == 0, second, first)
        for r in range(count // 2):
            for j in range(2):
                p = expand(r, bit, j)
                first = transpose_tile(embed_tile(blocks_ref[level, p, :, :width]))
                second = transpose_tile(embed_tile(blocks_ref[level, p, :, width:]))
                adj_ref[level, r, 0, :, j * size:(j + 1) * size] = jnp.where(own == 0, first, second)
                adj_ref[level, r, 1, :, j * size:(j + 1) * size] = jnp.where(own == 0, second, first)


def prep_map_kernel(maps_ref, fwd_ref, adj_ref, *, count):
    for p in range(count):
        tile = embed_tile(maps_ref[p])
        fwd_ref[p] = tile
        adj_ref[p] = transpose_tile(tile)


def prep_levels(blocks, scalars, bits, count, group, flip):
    levels, _, rank, width = blocks.shape
    block_spec = pl.BlockSpec((levels, count, rank, width), lambda i, sc: (0, sc[group], 0, 0))
    return pl.pallas_call(
        functools.partial(prep_level_kernel, count=count, bits=bits, flip=flip),
        grid_spec=pltpu.PrefetchScalarGridSpec(
            num_scalar_prefetch=1, grid=(1,),
            in_specs=[block_spec],
            out_specs=[whole((levels, count, 2 * rank, width)), whole((levels, count // 2, 2, 2 * rank, width))],
        ),
        out_shape=[jax.ShapeDtypeStruct((levels, count, 2 * rank, width), jnp.bfloat16),
                   jax.ShapeDtypeStruct((levels, count // 2, 2, 2 * rank, width), jnp.bfloat16)],
    )(scalars, blocks)


def level_block(shape, level):
    return pl.BlockSpec((None,) + tuple(shape[1:]), lambda i, own, n=len(shape) - 1, v=level: (v,) + (0,) * n)


def prep_map(maps):
    count, rank, width = maps.shape
    spec = pl.BlockSpec((count, rank, width), lambda i: (0, 0, 0))
    out = pl.BlockSpec((count, width, width), lambda i: (0, 0, 0))
    return pl.pallas_call(
        functools.partial(prep_map_kernel, count=count),
        grid=(1,),
        in_specs=[spec],
        out_specs=[out, out],
        out_shape=[jax.ShapeDtypeStruct((count, width, width), jnp.bfloat16)] * 2,
    )(maps)


def whole(shape):
    return pl.BlockSpec(shape, lambda i, own, n=len(shape): (0,) * n)


def column_block(shape, chunk):
    return pl.BlockSpec(shape, lambda i, own, c=chunk: (0, 0, c))


def call(kernel, own, inputs, in_specs, out_shapes, scratch):
    grid_spec = pltpu.PrefetchScalarGridSpec(
        num_scalar_prefetch=1,
        grid=(1,),
        in_specs=in_specs,
        out_specs=[whole(s.shape) for s in out_shapes],
        scratch_shapes=scratch,
    )
    return pl.pallas_call(
        kernel,
        grid_spec=grid_spec,
        out_shape=out_shapes,
        compiler_params=pltpu.CompilerParams(vmem_limit_bytes=48 * 1024 * 1024),
    )(own, *inputs)


def per_device(samples, echoes, leaf_maps, local_blocks, cross_blocks, outer_blocks, spread_maps):
    levels_local = local_blocks.shape[0]
    inner_bits = cross_blocks.shape[0]
    outer_bits = outer_blocks.shape[0]
    count, rows, columns = samples.shape
    width = columns // CHUNKS
    tgt_index = lax.axis_index("tgt")
    src_index = lax.axis_index("src")
    bits = [m for m in range(inner_bits)] + [m for m in range(outer_bits)]
    axes = ["tgt"] * inner_bits + ["src"] * outer_bits
    own_bits = [tgt_index >> m & 1 for m in range(inner_bits)] + [src_index >> m & 1 for m in range(outer_bits)]
    owns = [jnp.reshape(own, (1,)).astype(jnp.int32) for own in own_bits]
    n_cross = len(bits)

    leaf_weights, leaf_t = prep_map(leaf_maps)
    spread_weights, spread_t = prep_map(spread_maps)
    local_weights, local_t = prep_levels(
        local_blocks, jnp.zeros((1,), jnp.int32), tuple(range(levels_local)), count, 0, False)
    tgt_scalars = jnp.stack(own_bits[:inner_bits] + [tgt_index]).astype(jnp.int32)
    inner_fwd, inner_adj = prep_levels(cross_blocks, tgt_scalars, tuple(bits[:inner_bits]), count, inner_bits, True)
    src_scalars = jnp.stack(own_bits[inner_bits:] + [src_index * 0]).astype(jnp.int32)
    outer_fwd, outer_adj = prep_levels(outer_blocks, src_scalars, tuple(bits[inner_bits:]), count, outer_bits, True)
    cross_fwd = [(inner_fwd, m) for m in range(inner_bits)] + [(outer_fwd, m) for m in range(outer_bits)]
    cross_adj = [(inner_adj, m) for m in range(inner_bits)] + [(outer_adj, m) for m in range(outer_bits)]

    block = jax.ShapeDtypeStruct((count, rows, width), jnp.bfloat16)
    half = jax.ShapeDtypeStruct((count // 2, rows, width), jnp.bfloat16)
    half_spec = whole(half.shape)

    image_parts, aperture_parts = [], []
    for chunk in range(CHUNKS):
        stay, leave = call(
            functools.partial(forward_local_kernel, count=count, levels=levels_local, next_bit=bits[0]),
            owns[0],
            [samples, leaf_weights, local_weights],
            [column_block((count, rows, width), chunk), whole(leaf_weights.shape), whole(local_weights.shape)],
            [half, half],
            [pltpu.VMEM(block.shape, jnp.bfloat16), pltpu.VMEM(block.shape, jnp.bfloat16)],
        )
        for index in range(n_cross):
            bit, axis = bits[index], axes[index]
            arrived = from_partner(leave, axis, bit)
            last = index == n_cross - 1
            next_bit = 0 if last else bits[index + 1]
            weights, level = cross_fwd[index]
            inputs = [stay, arrived, weights]
            specs = [half_spec, half_spec, level_block(weights.shape, level)]
            if last:
                inputs.append(spread_weights)
                specs.append(whole(spread_weights.shape))
            result = call(
                functools.partial(forward_cross_kernel, count=count, bit=bit, next_bit=next_bit, last=last),
                owns[index] if last else owns[index + 1],
                inputs,
                specs,
                [block] if last else [half, half],
                [pltpu.VMEM(block.shape, jnp.bfloat16)],
            )
            if last:
                image_parts.append(result[0])
            else:
                stay, leave = result

        top = n_cross - 1
        kept, leave = call(
            functools.partial(adjoint_first_kernel, count=count, bit=bits[top]),
            owns[top],
            [echoes, spread_t, cross_adj[top][0]],
            [column_block((count, rows, width), chunk), whole(spread_t.shape),
             level_block(cross_adj[top][0].shape, cross_adj[top][1])],
            [half, half],
            [pltpu.VMEM(block.shape, jnp.bfloat16)],
        )
        arrived = from_partner(leave, axes[top], bits[top])
        for index in reversed(range(top)):
            prev_bit = bits[index + 1]
            weights, level = cross_adj[index]
            kept, leave = call(
                functools.partial(adjoint_cross_kernel, count=count, bit=bits[index], prev_bit=prev_bit),
                owns[index + 1],
                [kept, arrived, weights],
                [half_spec, half_spec, level_block(weights.shape, level)],
                [half, half],
                [],
            )
            arrived = from_partner(leave, axes[index], bits[index])
        (aperture,) = call(
            functools.partial(adjoint_local_kernel, count=count, levels=levels_local, prev_bit=bits[0]),
            owns[0],
            [kept, arrived, local_t, leaf_t],
            [half_spec, half_spec, whole(local_t.shape), whole(leaf_t.shape)],
            [block],
            [pltpu.VMEM(block.shape, jnp.bfloat16), pltpu.VMEM(block.shape, jnp.bfloat16)],
        )
        aperture_parts.append(aperture)
    image_field = jnp.concatenate(image_parts, axis=-1)
    aperture_field = jnp.concatenate(aperture_parts, axis=-1)
    return (image_field, aperture_field)


def solution(mesh):
    return jax.shard_map(
        per_device,
        mesh=mesh,
        in_specs=(
            P(("src", "tgt"), None, None),
            P(("src", "tgt"), None, None),
            P(("src", "tgt"), None, None),
            P(None, ("src", "tgt"), None, None),
            P(None, "src", None, None),
            P(None, ("src", "tgt"), None, None),
            P(("src", "tgt"), None, None),
        ),
        out_specs=(P(("src", "tgt"), None, None), P(("src", "tgt"), None, None)),
        check_vma=False,
    )
```

```python
import functools

import jax
import jax.numpy as jnp
from jax import lax
from jax.experimental import pallas as pl
from jax.experimental.pallas import tpu as pltpu
from jax.sharding import PartitionSpec as P

CHUNKS = 2


def from_partner(x, axis, apart):
    return lax.ppermute(x, axis, [(i, i ^ 1 << apart) for i in range(lax.axis_size(axis))])


def complex_embed(stored):
    half_width = stored.shape[-1] // 2
    real_part = stored[..., :half_width]
    imag_part = stored[..., half_width:]
    top_rows = jnp.concatenate([real_part, -imag_part], axis=-1)
    bottom_rows = jnp.concatenate([imag_part, real_part], axis=-1)
    return jnp.concatenate([top_rows, bottom_rows], axis=-2)


def expand(r, bit, j):
    return ((r >> bit) << (bit + 1)) | (j << bit) | (r & ((1 << bit) - 1))


def compress(p, bit):
    return ((p >> (bit + 1)) << bit) | (p & ((1 << bit) - 1))


def mm(w, x):
    return jnp.dot(w, x, preferred_element_type=jnp.float32).astype(jnp.bfloat16)


def write_split(value_of, count, bit, own, stay_ref, leave_ref):
    for p in range(count):
        r = compress(p, bit)
        here = ((p >> bit) & 1) == own

        @pl.when(here)
        def _():
            stay_ref[r] = value_of(p)

        @pl.when(jnp.logical_not(here))
        def _():
            leave_ref[r] = value_of(p)


def read_split(kept_ref, arrived_ref, bit, own):
    def value_of(p):
        r = compress(p, bit)
        return jnp.where(((p >> bit) & 1) == own, kept_ref[r], arrived_ref[r])

    return value_of


def forward_local_kernel(own_ref, samples_ref, leaf_ref, local_ref, stay_ref, leave_ref, buf_a, buf_b,
                         *, count, levels, next_bit):
    for p in range(count):
        buf_a[p] = mm(leaf_ref[p], samples_ref[p])
    src, dst = buf_a, buf_b
    for level in range(levels):
        for r in range(count // 2):
            p0, p1 = expand(r, level, 0), expand(r, level, 1)
            stacked = jnp.concatenate([src[p0], src[p1]], axis=0)
            dst[p0] = mm(local_ref[level, p0], stacked)
            dst[p1] = mm(local_ref[level, p1], stacked)
        src, dst = dst, src
    write_split(lambda p: src[p], count, next_bit, own_ref[0], stay_ref, leave_ref)


def forward_cross_kernel(own_ref, kept_ref, arrived_ref, weight_ref, *rest, count, bit, next_bit, last):
    if last:
        spread_ref, out_ref, buf = rest
    else:
        stay_ref, leave_ref, buf = rest
    for r in range(count // 2):
        stacked = jnp.concatenate([kept_ref[r], arrived_ref[r]], axis=0)
        for j in range(2):
            p = expand(r, bit, j)
            buf[p] = mm(weight_ref[p], stacked)
    if last:
        for p in range(count):
            out_ref[p] = mm(spread_ref[p], buf[p])
    else:
        write_split(lambda p: buf[p], count, next_bit, own_ref[0], stay_ref, leave_ref)


def adjoint_first_kernel(own_ref, echoes_ref, spread_t_ref, weight_ref, kept_ref, leave_ref, buf, *, count, bit):
    for p in range(count):
        buf[p] = mm(spread_t_ref[p], echoes_ref[p])
    for r in range(count // 2):
        stacked = jnp.concatenate([buf[expand(r, bit, 0)], buf[expand(r, bit, 1)]], axis=0)
        kept_ref[r] = mm(weight_ref[r, 0], stacked)
        leave_ref[r] = mm(weight_ref[r, 1], stacked)


def adjoint_cross_kernel(own_ref, prev_kept_ref, prev_arrived_ref, weight_ref, kept_ref, leave_ref,
                         *, count, bit, prev_bit):
    value_of = read_split(prev_kept_ref, prev_arrived_ref, prev_bit, own_ref[0])
    for r in range(count // 2):
        stacked = jnp.concatenate([value_of(expand(r, bit, 0)), value_of(expand(r, bit, 1))], axis=0)
        kept_ref[r] = mm(weight_ref[r, 0], stacked)
        leave_ref[r] = mm(weight_ref[r, 1], stacked)


def adjoint_local_kernel(own_ref, prev_kept_ref, prev_arrived_ref, local_ref, leaf_t_ref, out_ref, buf_a, buf_b,
                         *, count, levels, prev_bit):
    value_of = read_split(prev_kept_ref, prev_arrived_ref, prev_bit, own_ref[0])
    for p in range(count):
        buf_a[p] = value_of(p)
    src, dst = buf_a, buf_b
    for level in reversed(range(levels)):
        for r in range(count // 2):
            stacked = jnp.concatenate([src[expand(r, level, 0)], src[expand(r, level, 1)]], axis=0)
            for b in range(2):
                dst[expand(r, level, b)] = mm(local_ref[level, r, b], stacked)
        src, dst = dst, src
    for p in range(count):
        out_ref[p] = mm(leaf_t_ref[p], src[p])


def embed_tile(stored):
    half = stored.shape[-1] // 2
    lane = lax.broadcasted_iota(jnp.int32, stored.shape, 1)
    top = jnp.where(lane < half, stored, -stored)
    bottom = pltpu.roll(stored, half, 1)
    return jnp.concatenate([top, bottom], axis=0)


def transpose_tile(tile):
    return tile.astype(jnp.float32).T.astype(jnp.bfloat16)


def prep_level_kernel(own_ref, blocks_ref, fwd_ref, adj_ref, *, count, bits, flip):
    width = blocks_ref.shape[-1] // 2
    size = 2 * blocks_ref.shape[-2]
    for level, bit in enumerate(bits):
        own = own_ref[level] if flip else 0
        for p in range(count):
            first = embed_tile(blocks_ref[level, p, :, :width])
            second = embed_tile(blocks_ref[level, p, :, width:])
            fwd_ref[level, p, :, :size] = jnp.where(own == 0, first, second)
            fwd_ref[level, p, :, size:] = jnp.where(own == 0, second, first)
        for r in range(count // 2):
            for j in range(2):
                p = expand(r, bit, j)
                first = transpose_tile(embed_tile(blocks_ref[level, p, :, :width]))
                second = transpose_tile(embed_tile(blocks_ref[level, p, :, width:]))
                adj_ref[level, r, 0, :, j * size:(j + 1) * size] = jnp.where(own == 0, first, second)
                adj_ref[level, r, 1, :, j * size:(j + 1) * size] = jnp.where(own == 0, second, first)


def prep_map_kernel(maps_ref, fwd_ref, adj_ref, *, count):
    for p in range(count):
        tile = embed_tile(maps_ref[p])
        fwd_ref[p] = tile
        adj_ref[p] = transpose_tile(tile)


def prep_levels(blocks, scalars, bits, count, group, flip):
    levels, _, rank, width = blocks.shape
    block_spec = pl.BlockSpec((levels, count, rank, width), lambda i, sc: (0, sc[group], 0, 0))
    return pl.pallas_call(
        functools.partial(prep_level_kernel, count=count, bits=bits, flip=flip),
        grid_spec=pltpu.PrefetchScalarGridSpec(
            num_scalar_prefetch=1, grid=(1,),
            in_specs=[block_spec],
            out_specs=[whole((levels, count, 2 * rank, width)), whole((levels, count // 2, 2, 2 * rank, width))],
        ),
        out_shape=[jax.ShapeDtypeStruct((levels, count, 2 * rank, width), jnp.bfloat16),
                   jax.ShapeDtypeStruct((levels, count // 2, 2, 2 * rank, width), jnp.bfloat16)],
    )(scalars, blocks)


def level_block(shape, level):
    return pl.BlockSpec((None,) + tuple(shape[1:]), lambda i, own, n=len(shape) - 1, v=level: (v,) + (0,) * n)


def prep_map(maps):
    count, rank, width = maps.shape
    spec = pl.BlockSpec((count, rank, width), lambda i: (0, 0, 0))
    out = pl.BlockSpec((count, width, width), lambda i: (0, 0, 0))
    return pl.pallas_call(
        functools.partial(prep_map_kernel, count=count),
        grid=(1,),
        in_specs=[spec],
        out_specs=[out, out],
        out_shape=[jax.ShapeDtypeStruct((count, width, width), jnp.bfloat16)] * 2,
    )(maps)


def whole(shape):
    return pl.BlockSpec(shape, lambda i, own, n=len(shape): (0,) * n)


def column_block(shape, chunk):
    return pl.BlockSpec(shape, lambda i, own, c=chunk: (0, 0, c))


def call(kernel, own, inputs, in_specs, out_shapes, scratch):
    grid_spec = pltpu.PrefetchScalarGridSpec(
        num_scalar_prefetch=1,
        grid=(1,),
        in_specs=in_specs,
        out_specs=[whole(s.shape) for s in out_shapes],
        scratch_shapes=scratch,
    )
    return pl.pallas_call(
        kernel,
        grid_spec=grid_spec,
        out_shape=out_shapes,
        compiler_params=pltpu.CompilerParams(vmem_limit_bytes=48 * 1024 * 1024),
    )(own, *inputs)


def per_device(samples, echoes, leaf_maps, local_blocks, cross_blocks, outer_blocks, spread_maps):
    levels_local = local_blocks.shape[0]
    inner_bits = cross_blocks.shape[0]
    outer_bits = outer_blocks.shape[0]
    count, rows, columns = samples.shape
    width = columns // CHUNKS
    tgt_index = lax.axis_index("tgt")
    src_index = lax.axis_index("src")
    bits = [m for m in range(inner_bits)] + [m for m in range(outer_bits)]
    axes = ["tgt"] * inner_bits + ["src"] * outer_bits
    own_bits = [tgt_index >> m & 1 for m in range(inner_bits)] + [src_index >> m & 1 for m in range(outer_bits)]
    owns = [jnp.reshape(own, (1,)).astype(jnp.int32) for own in own_bits]
    n_cross = len(bits)

    leaf_weights, leaf_t = prep_map(leaf_maps)
    spread_weights, spread_t = prep_map(spread_maps)
    local_weights, local_t = prep_levels(
        local_blocks, jnp.zeros((1,), jnp.int32), tuple(range(levels_local)), count, 0, False)
    tgt_scalars = jnp.stack(own_bits[:inner_bits] + [tgt_index]).astype(jnp.int32)
    inner_fwd, inner_adj = prep_levels(cross_blocks, tgt_scalars, tuple(bits[:inner_bits]), count, inner_bits, True)
    src_scalars = jnp.stack(own_bits[inner_bits:] + [src_index * 0]).astype(jnp.int32)
    outer_fwd, outer_adj = prep_levels(outer_blocks, src_scalars, tuple(bits[inner_bits:]), count, outer_bits, True)
    cross_fwd = [(inner_fwd, m) for m in range(inner_bits)] + [(outer_fwd, m) for m in range(outer_bits)]
    cross_adj = [(inner_adj, m) for m in range(inner_bits)] + [(outer_adj, m) for m in range(outer_bits)]

    block = jax.ShapeDtypeStruct((count, rows, width), jnp.bfloat16)
    half = jax.ShapeDtypeStruct((count // 2, rows, width), jnp.bfloat16)
    half_spec = whole(half.shape)

    image_parts, aperture_parts = [], []
    for chunk in range(CHUNKS):
        stay, leave = call(
            functools.partial(forward_local_kernel, count=count, levels=levels_local, next_bit=bits[0]),
            owns[0],
            [samples, leaf_weights, local_weights],
            [column_block((count, rows, width), chunk), whole(leaf_weights.shape), whole(local_weights.shape)],
            [half, half],
            [pltpu.VMEM(block.shape, jnp.bfloat16), pltpu.VMEM(block.shape, jnp.bfloat16)],
        )
        for index in range(n_cross):
            bit, axis = bits[index], axes[index]
            arrived = from_partner(leave, axis, bit)
            last = index == n_cross - 1
            next_bit = 0 if last else bits[index + 1]
            weights, level = cross_fwd[index]
            inputs = [stay, arrived, weights]
            specs = [half_spec, half_spec, level_block(weights.shape, level)]
            if last:
                inputs.append(spread_weights)
                specs.append(whole(spread_weights.shape))
            result = call(
                functools.partial(forward_cross_kernel, count=count, bit=bit, next_bit=next_bit, last=last),
                owns[index] if last else owns[index + 1],
                inputs,
                specs,
                [block] if last else [half, half],
                [pltpu.VMEM(block.shape, jnp.bfloat16)],
            )
            if last:
                image_parts.append(result[0])
            else:
                stay, leave = result

        top = n_cross - 1
        kept, leave = call(
            functools.partial(adjoint_first_kernel, count=count, bit=bits[top]),
            owns[top],
            [echoes, spread_t, cross_adj[top][0]],
            [column_block((count, rows, width), chunk), whole(spread_t.shape),
             level_block(cross_adj[top][0].shape, cross_adj[top][1])],
            [half, half],
            [pltpu.VMEM(block.shape, jnp.bfloat16)],
        )
        arrived = from_partner(leave, axes[top], bits[top])
        for index in reversed(range(top)):
            prev_bit = bits[index + 1]
            weights, level = cross_adj[index]
            kept, leave = call(
                functools.partial(adjoint_cross_kernel, count=count, bit=bits[index], prev_bit=prev_bit),
                owns[index + 1],
                [kept, arrived, weights],
                [half_spec, half_spec, level_block(weights.shape, level)],
                [half, half],
                [],
            )
            arrived = from_partner(leave, axes[index], bits[index])
        (aperture,) = call(
            functools.partial(adjoint_local_kernel, count=count, levels=levels_local, prev_bit=bits[0]),
            owns[0],
            [kept, arrived, local_t, leaf_t],
            [half_spec, half_spec, whole(local_t.shape), whole(leaf_t.shape)],
            [block],
            [pltpu.VMEM(block.shape, jnp.bfloat16), pltpu.VMEM(block.shape, jnp.bfloat16)],
        )
        aperture_parts.append(aperture)
    image_field = jnp.concatenate(image_parts, axis=-1)
    aperture_field = jnp.concatenate(aperture_parts, axis=-1)
    return (image_field, aperture_field)


def solution(mesh):
    return jax.shard_map(
        per_device,
        mesh=mesh,
        in_specs=(
            P(("src", "tgt"), None, None),
            P(("src", "tgt"), None, None),
            P(("src", "tgt"), None, None),
            P(None, ("src", "tgt"), None, None),
            P(None, "src", None, None),
            P(None, ("src", "tgt"), None, None),
            P(("src", "tgt"), None, None),
        ),
        out_specs=(P(("src", "tgt"), None, None), P(("src", "tgt"), None, None)),
        check_vma=False,
    )
```

```python
import functools

import jax
import jax.numpy as jnp
from jax import lax
from jax.experimental import pallas as pl
from jax.experimental.pallas import tpu as pltpu
from jax.sharding import PartitionSpec as P

CHUNKS = 2


def from_partner(x, axis, apart):
    return lax.ppermute(x, axis, [(i, i ^ 1 << apart) for i in range(lax.axis_size(axis))])


def expand(r, bit, j):
    return ((r >> bit) << (bit + 1)) | (j << bit) | (r & ((1 << bit) - 1))


def compress(p, bit):
    return ((p >> (bit + 1)) << bit) | (p & ((1 << bit) - 1))


def mm(w, x):
    return jnp.dot(w, x, preferred_element_type=jnp.float32).astype(jnp.bfloat16)


def mm_t(w, x):
    product = lax.dot_general(w, x, (((0,), (0,)), ((), ())), preferred_element_type=jnp.float32)
    return product.astype(jnp.bfloat16)


def embed_tile(stored):
    half = stored.shape[-1] // 2
    lane = lax.broadcasted_iota(jnp.int32, stored.shape, 1)
    top = jnp.where(lane < half, stored, -stored)
    bottom = pltpu.roll(stored, half, 1)
    return jnp.concatenate([top, bottom], axis=0)


def block_pair(stored, own):
    width = stored.shape[-1] // 2
    first = embed_tile(stored[:, :width])
    second = embed_tile(stored[:, width:])
    if isinstance(own, int) and own == 0:
        return first, second
    return jnp.where(own == 0, first, second), jnp.where(own == 0, second, first)


def forward_weight(stored, own):
    first, second = block_pair(stored, own)
    return jnp.concatenate([first, second], axis=1)


def write_split(value_of, count, bit, own, stay_ref, leave_ref):
    for p in range(count):
        r = compress(p, bit)
        here = ((p >> bit) & 1) == own

        @pl.when(here)
        def _():
            stay_ref[r] = value_of(p)

        @pl.when(jnp.logical_not(here))
        def _():
            leave_ref[r] = value_of(p)


def read_split(kept_ref, arrived_ref, bit, own):
    def value_of(p):
        r = compress(p, bit)
        return jnp.where(((p >> bit) & 1) == own, kept_ref[r], arrived_ref[r])

    return value_of


def adjoint_pair(value_of, blocks_ref, bit, r, own):
    lower, upper = expand(r, bit, 0), expand(r, bit, 1)
    stacked = jnp.concatenate([value_of(lower), value_of(upper)], axis=0)
    first_lower, second_lower = block_pair(blocks_ref[lower], own)
    first_upper, second_upper = block_pair(blocks_ref[upper], own)
    kept = mm_t(jnp.concatenate([first_lower, first_upper], axis=0), stacked)
    leave = mm_t(jnp.concatenate([second_lower, second_upper], axis=0), stacked)
    return kept, leave


def forward_local_kernel(sc_ref, samples_ref, leaf_ref, local_ref, stay_ref, leave_ref, buf_a, buf_b,
                         *, count, levels, next_bit):
    for p in range(count):
        buf_a[p] = mm(embed_tile(leaf_ref[p]), samples_ref[p])
    src, dst = buf_a, buf_b
    for level in range(levels):
        for r in range(count // 2):
            p0, p1 = expand(r, level, 0), expand(r, level, 1)
            stacked = jnp.concatenate([src[p0], src[p1]], axis=0)
            dst[p0] = mm(forward_weight(local_ref[level, p0], 0), stacked)
            dst[p1] = mm(forward_weight(local_ref[level, p1], 0), stacked)
        src, dst = dst, src
    write_split(lambda p: src[p], count, next_bit, sc_ref[1], stay_ref, leave_ref)


def forward_cross_kernel(sc_ref, kept_ref, arrived_ref, blocks_ref, *rest, count, bit, next_bit, last):
    if last:
        spread_ref, out_ref, buf = rest
    else:
        stay_ref, leave_ref, buf = rest
    own = sc_ref[0]
    for r in range(count // 2):
        stacked = jnp.concatenate([kept_ref[r], arrived_ref[r]], axis=0)
        for j in range(2):
            p = expand(r, bit, j)
            buf[p] = mm(forward_weight(blocks_ref[p], own), stacked)
    if last:
        for p in range(count):
            out_ref[p] = mm(embed_tile(spread_ref[p]), buf[p])
    else:
        write_split(lambda p: buf[p], count, next_bit, sc_ref[1], stay_ref, leave_ref)


def adjoint_first_kernel(sc_ref, echoes_ref, spread_ref, blocks_ref, kept_ref, leave_ref, buf, *, count, bit):
    for p in range(count):
        buf[p] = mm_t(embed_tile(spread_ref[p]), echoes_ref[p])
    own = sc_ref[0]
    for r in range(count // 2):
        kept_ref[r], leave_ref[r] = adjoint_pair(lambda p: buf[p], blocks_ref, bit, r, own)


def adjoint_cross_kernel(sc_ref, prev_kept_ref, prev_arrived_ref, blocks_ref, kept_ref, leave_ref,
                         *, count, bit, prev_bit):
    value_of = read_split(prev_kept_ref, prev_arrived_ref, prev_bit, sc_ref[1])
    own = sc_ref[0]
    for r in range(count // 2):
        kept_ref[r], leave_ref[r] = adjoint_pair(value_of, blocks_ref, bit, r, own)


def adjoint_local_kernel(sc_ref, prev_kept_ref, prev_arrived_ref, local_ref, leaf_ref, out_ref, buf_a, buf_b,
                         *, count, levels, prev_bit):
    value_of = read_split(prev_kept_ref, prev_arrived_ref, prev_bit, sc_ref[1])
    for p in range(count):
        buf_a[p] = value_of(p)
    src, dst = buf_a, buf_b
    for level in reversed(range(levels)):
        for r in range(count // 2):
            first, second = adjoint_pair(lambda p: src[p], local_ref.at[level], level, r, 0)
            dst[expand(r, level, 0)] = first
            dst[expand(r, level, 1)] = second
        src, dst = dst, src
    for p in range(count):
        out_ref[p] = mm_t(embed_tile(leaf_ref[p]), src[p])


def whole(shape):
    return pl.BlockSpec(shape, lambda i, sc, n=len(shape): (0,) * n)


def column_block(shape, chunk):
    return pl.BlockSpec(shape, lambda i, sc, c=chunk: (0, 0, c))


def level_block(shape, level, count, grouped):
    if grouped:
        return pl.BlockSpec((None, count) + tuple(shape[2:]), lambda i, sc, v=level: (v, sc[2], 0, 0))
    return pl.BlockSpec((None, count) + tuple(shape[2:]), lambda i, sc, v=level: (v, 0, 0, 0))


def call(kernel, scalars, inputs, in_specs, out_shapes, scratch):
    grid_spec = pltpu.PrefetchScalarGridSpec(
        num_scalar_prefetch=1,
        grid=(1,),
        in_specs=in_specs,
        out_specs=[whole(s.shape) for s in out_shapes],
        scratch_shapes=scratch,
    )
    return pl.pallas_call(
        kernel,
        grid_spec=grid_spec,
        out_shape=out_shapes,
        compiler_params=pltpu.CompilerParams(vmem_limit_bytes=48 * 1024 * 1024),
    )(scalars, *inputs)


def per_device(samples, echoes, leaf_maps, local_blocks, cross_blocks, outer_blocks, spread_maps):
    levels_local = local_blocks.shape[0]
    inner_bits = cross_blocks.shape[0]
    outer_bits = outer_blocks.shape[0]
    count, rows, columns = samples.shape
    width = columns // CHUNKS
    tgt_index = lax.axis_index("tgt")
    src_index = lax.axis_index("src")
    bits = [m for m in range(inner_bits)] + [m for m in range(outer_bits)]
    axes = ["tgt"] * inner_bits + ["src"] * outer_bits
    own_bits = [tgt_index >> m & 1 for m in range(inner_bits)] + [src_index >> m & 1 for m in range(outer_bits)]
    sources = [(cross_blocks, m, True) for m in range(inner_bits)] + [(outer_blocks, m, False) for m in range(outer_bits)]
    n_cross = len(bits)

    def scalars(first, second):
        return jnp.stack([first, second, tgt_index]).astype(jnp.int32)

    def blocks_spec(index):
        array, level, grouped = sources[index]
        return level_block(array.shape, level, count, grouped)

    block = jax.ShapeDtypeStruct((count, rows, width), jnp.bfloat16)
    half = jax.ShapeDtypeStruct((count // 2, rows, width), jnp.bfloat16)
    half_spec = whole(half.shape)
    zero = tgt_index * 0

    image_parts, aperture_parts = [], []
    for chunk in range(CHUNKS):
        stay, leave = call(
            functools.partial(forward_local_kernel, count=count, levels=levels_local, next_bit=bits[0]),
            scalars(zero, own_bits[0]),
            [samples, leaf_maps, local_blocks],
            [column_block((count, rows, width), chunk), whole(leaf_maps.shape), whole(local_blocks.shape)],
            [half, half],
            [pltpu.VMEM(block.shape, jnp.bfloat16), pltpu.VMEM(block.shape, jnp.bfloat16)],
        )
        for index in range(n_cross):
            bit, axis = bits[index], axes[index]
            arrived = from_partner(leave, axis, bit)
            last = index == n_cross - 1
            next_bit = 0 if last else bits[index + 1]
            inputs = [stay, arrived, sources[index][0]]
            specs = [half_spec, half_spec, blocks_spec(index)]
            if last:
                inputs.append(spread_maps)
                specs.append(whole(spread_maps.shape))
            result = call(
                functools.partial(forward_cross_kernel, count=count, bit=bit, next_bit=next_bit, last=last),
                scalars(own_bits[index], zero if last else own_bits[index + 1]),
                inputs,
                specs,
                [block] if last else [half, half],
                [pltpu.VMEM(block.shape, jnp.bfloat16)],
            )
            if last:
                image_parts.append(result[0])
            else:
                stay, leave = result

        top = n_cross - 1
        kept, leave = call(
            functools.partial(adjoint_first_kernel, count=count, bit=bits[top]),
            scalars(own_bits[top], zero),
            [echoes, spread_maps, sources[top][0]],
            [column_block((count, rows, width), chunk), whole(spread_maps.shape), blocks_spec(top)],
            [half, half],
            [pltpu.VMEM(block.shape, jnp.bfloat16)],
        )
        arrived = from_partner(leave, axes[top], bits[top])
        for index in reversed(range(top)):
            kept, leave = call(
                functools.partial(adjoint_cross_kernel, count=count, bit=bits[index], prev_bit=bits[index + 1]),
                scalars(own_bits[index], own_bits[index + 1]),
                [kept, arrived, sources[index][0]],
                [half_spec, half_spec, blocks_spec(index)],
                [half, half],
                [],
            )
            arrived = from_partner(leave, axes[index], bits[index])
        (aperture,) = call(
            functools.partial(adjoint_local_kernel, count=count, levels=levels_local, prev_bit=bits[0]),
            scalars(zero, own_bits[0]),
            [kept, arrived, local_blocks, leaf_maps],
            [half_spec, half_spec, whole(local_blocks.shape), whole(leaf_maps.shape)],
            [block],
            [pltpu.VMEM(block.shape, jnp.bfloat16), pltpu.VMEM(block.shape, jnp.bfloat16)],
        )
        aperture_parts.append(aperture)
    image_field = jnp.concatenate(image_parts, axis=-1)
    aperture_field = jnp.concatenate(aperture_parts, axis=-1)
    return (image_field, aperture_field)


def solution(mesh):
    return jax.shard_map(
        per_device,
        mesh=mesh,
        in_specs=(
            P(("src", "tgt"), None, None),
            P(("src", "tgt"), None, None),
            P(("src", "tgt"), None, None),
            P(None, ("src", "tgt"), None, None),
            P(None, "src", None, None),
            P(None, ("src", "tgt"), None, None),
            P(("src", "tgt"), None, None),
        ),
        out_specs=(P(("src", "tgt"), None, None), P(("src", "tgt"), None, None)),
        check_vma=False,
    )
```

```python
import functools

import jax
import jax.numpy as jnp
from jax import lax
from jax.experimental import pallas as pl
from jax.experimental.pallas import tpu as pltpu
from jax.sharding import PartitionSpec as P

CHUNKS = 4


def from_partner(x, axis, apart):
    return lax.ppermute(x, axis, [(i, i ^ 1 << apart) for i in range(lax.axis_size(axis))])


def expand(r, bit, j):
    return ((r >> bit) << (bit + 1)) | (j << bit) | (r & ((1 << bit) - 1))


def compress(p, bit):
    return ((p >> (bit + 1)) << bit) | (p & ((1 << bit) - 1))


def mm(w, x):
    return jnp.dot(w, x, preferred_element_type=jnp.float32).astype(jnp.bfloat16)


def mm_t(w, x):
    product = lax.dot_general(w, x, (((0,), (0,)), ((), ())), preferred_element_type=jnp.float32)
    return product.astype(jnp.bfloat16)


def embed_tile(stored):
    half = stored.shape[-1] // 2
    lane = lax.broadcasted_iota(jnp.int32, stored.shape, 1)
    top = jnp.where(lane < half, stored, -stored)
    bottom = pltpu.roll(stored, half, 1)
    return jnp.concatenate([top, bottom], axis=0)


def block_pair(stored, own):
    width = stored.shape[-1] // 2
    first = embed_tile(stored[:, :width])
    second = embed_tile(stored[:, width:])
    if isinstance(own, int) and own == 0:
        return first, second
    return jnp.where(own == 0, first, second), jnp.where(own == 0, second, first)


def forward_weight(stored, own):
    first, second = block_pair(stored, own)
    return jnp.concatenate([first, second], axis=1)


def write_split(value_of, count, bit, own, stay_ref, leave_ref):
    for p in range(count):
        r = compress(p, bit)
        here = ((p >> bit) & 1) == own

        @pl.when(here)
        def _():
            stay_ref[r] = value_of(p)

        @pl.when(jnp.logical_not(here))
        def _():
            leave_ref[r] = value_of(p)


def read_split(kept_ref, arrived_ref, bit, own):
    def value_of(p):
        r = compress(p, bit)
        return jnp.where(((p >> bit) & 1) == own, kept_ref[r], arrived_ref[r])

    return value_of


def adjoint_pair(value_of, blocks_ref, bit, r, own):
    lower, upper = expand(r, bit, 0), expand(r, bit, 1)
    stacked = jnp.concatenate([value_of(lower), value_of(upper)], axis=0)
    first_lower, second_lower = block_pair(blocks_ref[lower], own)
    first_upper, second_upper = block_pair(blocks_ref[upper], own)
    kept = mm_t(jnp.concatenate([first_lower, first_upper], axis=0), stacked)
    leave = mm_t(jnp.concatenate([second_lower, second_upper], axis=0), stacked)
    return kept, leave


def forward_local_kernel(sc_ref, samples_ref, leaf_ref, local_ref, stay_ref, leave_ref, buf_a, buf_b,
                         *, count, levels, next_bit):
    for p in range(count):
        buf_a[p] = mm(embed_tile(leaf_ref[p]), samples_ref[p])
    src, dst = buf_a, buf_b
    for level in range(levels):
        for r in range(count // 2):
            p0, p1 = expand(r, level, 0), expand(r, level, 1)
            stacked = jnp.concatenate([src[p0], src[p1]], axis=0)
            dst[p0] = mm(forward_weight(local_ref[level, p0], 0), stacked)
            dst[p1] = mm(forward_weight(local_ref[level, p1], 0), stacked)
        src, dst = dst, src
    write_split(lambda p: src[p], count, next_bit, sc_ref[1], stay_ref, leave_ref)


def forward_cross_kernel(sc_ref, kept_ref, arrived_ref, blocks_ref, *rest, count, bit, next_bit, last):
    if last:
        spread_ref, out_ref, buf = rest
    else:
        stay_ref, leave_ref, buf = rest
    own = sc_ref[0]
    for r in range(count // 2):
        stacked = jnp.concatenate([kept_ref[r], arrived_ref[r]], axis=0)
        for j in range(2):
            p = expand(r, bit, j)
            buf[p] = mm(forward_weight(blocks_ref[p], own), stacked)
    if last:
        for p in range(count):
            out_ref[p] = mm(embed_tile(spread_ref[p]), buf[p])
    else:
        write_split(lambda p: buf[p], count, next_bit, sc_ref[1], stay_ref, leave_ref)


def adjoint_first_kernel(sc_ref, echoes_ref, spread_ref, blocks_ref, kept_ref, leave_ref, buf, *, count, bit):
    for p in range(count):
        buf[p] = mm_t(embed_tile(spread_ref[p]), echoes_ref[p])
    own = sc_ref[0]
    for r in range(count // 2):
        kept_ref[r], leave_ref[r] = adjoint_pair(lambda p: buf[p], blocks_ref, bit, r, own)


def adjoint_cross_kernel(sc_ref, prev_kept_ref, prev_arrived_ref, blocks_ref, kept_ref, leave_ref,
                         *, count, bit, prev_bit):
    value_of = read_split(prev_kept_ref, prev_arrived_ref, prev_bit, sc_ref[1])
    own = sc_ref[0]
    for r in range(count // 2):
        kept_ref[r], leave_ref[r] = adjoint_pair(value_of, blocks_ref, bit, r, own)


def adjoint_local_kernel(sc_ref, prev_kept_ref, prev_arrived_ref, local_ref, leaf_ref, out_ref, buf_a, buf_b,
                         *, count, levels, prev_bit):
    value_of = read_split(prev_kept_ref, prev_arrived_ref, prev_bit, sc_ref[1])
    for p in range(count):
        buf_a[p] = value_of(p)
    src, dst = buf_a, buf_b
    for level in reversed(range(levels)):
        for r in range(count // 2):
            first, second = adjoint_pair(lambda p: src[p], local_ref.at[level], level, r, 0)
            dst[expand(r, level, 0)] = first
            dst[expand(r, level, 1)] = second
        src, dst = dst, src
    for p in range(count):
        out_ref[p] = mm_t(embed_tile(leaf_ref[p]), src[p])


def whole(shape):
    return pl.BlockSpec(shape, lambda i, sc, n=len(shape): (0,) * n)


def column_block(shape, chunk):
    return pl.BlockSpec(shape, lambda i, sc, c=chunk: (0, 0, c))


def level_block(shape, level, count, grouped):
    if grouped:
        return pl.BlockSpec((None, count) + tuple(shape[2:]), lambda i, sc, v=level: (v, sc[2], 0, 0))
    return pl.BlockSpec((None, count) + tuple(shape[2:]), lambda i, sc, v=level: (v, 0, 0, 0))


def call(kernel, scalars, inputs, in_specs, out_shapes, scratch):
    grid_spec = pltpu.PrefetchScalarGridSpec(
        num_scalar_prefetch=1,
        grid=(1,),
        in_specs=in_specs,
        out_specs=[whole(s.shape) for s in out_shapes],
        scratch_shapes=scratch,
    )
    return pl.pallas_call(
        kernel,
        grid_spec=grid_spec,
        out_shape=out_shapes,
        compiler_params=pltpu.CompilerParams(vmem_limit_bytes=48 * 1024 * 1024),
    )(scalars, *inputs)


def per_device(samples, echoes, leaf_maps, local_blocks, cross_blocks, outer_blocks, spread_maps):
    levels_local = local_blocks.shape[0]
    inner_bits = cross_blocks.shape[0]
    outer_bits = outer_blocks.shape[0]
    count, rows, columns = samples.shape
    width = columns // CHUNKS
    tgt_index = lax.axis_index("tgt")
    src_index = lax.axis_index("src")
    bits = [m for m in range(inner_bits)] + [m for m in range(outer_bits)]
    axes = ["tgt"] * inner_bits + ["src"] * outer_bits
    own_bits = [tgt_index >> m & 1 for m in range(inner_bits)] + [src_index >> m & 1 for m in range(outer_bits)]
    sources = [(cross_blocks, m, True) for m in range(inner_bits)] + [(outer_blocks, m, False) for m in range(outer_bits)]
    n_cross = len(bits)

    def scalars(first, second):
        return jnp.stack([first, second, tgt_index]).astype(jnp.int32)

    def blocks_spec(index):
        array, level, grouped = sources[index]
        return level_block(array.shape, level, count, grouped)

    block = jax.ShapeDtypeStruct((count, rows, width), jnp.bfloat16)
    half = jax.ShapeDtypeStruct((count // 2, rows, width), jnp.bfloat16)
    half_spec = whole(half.shape)
    zero = tgt_index * 0

    image_parts, aperture_parts = [], []
    for chunk in range(CHUNKS):
        stay, leave = call(
            functools.partial(forward_local_kernel, count=count, levels=levels_local, next_bit=bits[0]),
            scalars(zero, own_bits[0]),
            [samples, leaf_maps, local_blocks],
            [column_block((count, rows, width), chunk), whole(leaf_maps.shape), whole(local_blocks.shape)],
            [half, half],
            [pltpu.VMEM(block.shape, jnp.bfloat16), pltpu.VMEM(block.shape, jnp.bfloat16)],
        )
        for index in range(n_cross):
            bit, axis = bits[index], axes[index]
            arrived = from_partner(leave, axis, bit)
            last = index == n_cross - 1
            next_bit = 0 if last else bits[index + 1]
            inputs = [stay, arrived, sources[index][0]]
            specs = [half_spec, half_spec, blocks_spec(index)]
            if last:
                inputs.append(spread_maps)
                specs.append(whole(spread_maps.shape))
            result = call(
                functools.partial(forward_cross_kernel, count=count, bit=bit, next_bit=next_bit, last=last),
                scalars(own_bits[index], zero if last else own_bits[index + 1]),
                inputs,
                specs,
                [block] if last else [half, half],
                [pltpu.VMEM(block.shape, jnp.bfloat16)],
            )
            if last:
                image_parts.append(result[0])
            else:
                stay, leave = result

        top = n_cross - 1
        kept, leave = call(
            functools.partial(adjoint_first_kernel, count=count, bit=bits[top]),
            scalars(own_bits[top], zero),
            [echoes, spread_maps, sources[top][0]],
            [column_block((count, rows, width), chunk), whole(spread_maps.shape), blocks_spec(top)],
            [half, half],
            [pltpu.VMEM(block.shape, jnp.bfloat16)],
        )
        arrived = from_partner(leave, axes[top], bits[top])
        for index in reversed(range(top)):
            kept, leave = call(
                functools.partial(adjoint_cross_kernel, count=count, bit=bits[index], prev_bit=bits[index + 1]),
                scalars(own_bits[index], own_bits[index + 1]),
                [kept, arrived, sources[index][0]],
                [half_spec, half_spec, blocks_spec(index)],
                [half, half],
                [],
            )
            arrived = from_partner(leave, axes[index], bits[index])
        (aperture,) = call(
            functools.partial(adjoint_local_kernel, count=count, levels=levels_local, prev_bit=bits[0]),
            scalars(zero, own_bits[0]),
            [kept, arrived, local_blocks, leaf_maps],
            [half_spec, half_spec, whole(local_blocks.shape), whole(leaf_maps.shape)],
            [block],
            [pltpu.VMEM(block.shape, jnp.bfloat16), pltpu.VMEM(block.shape, jnp.bfloat16)],
        )
        aperture_parts.append(aperture)
    image_field = jnp.concatenate(image_parts, axis=-1)
    aperture_field = jnp.concatenate(aperture_parts, axis=-1)
    return (image_field, aperture_field)


def solution(mesh):
    return jax.shard_map(
        per_device,
        mesh=mesh,
        in_specs=(
            P(("src", "tgt"), None, None),
            P(("src", "tgt"), None, None),
            P(("src", "tgt"), None, None),
            P(None, ("src", "tgt"), None, None),
            P(None, "src", None, None),
            P(None, ("src", "tgt"), None, None),
            P(("src", "tgt"), None, None),
        ),
        out_specs=(P(("src", "tgt"), None, None), P(("src", "tgt"), None, None)),
        check_vma=False,
    )
```

```python
import functools

import jax
import jax.numpy as jnp
from jax import lax
from jax.experimental import pallas as pl
from jax.experimental.pallas import tpu as pltpu
from jax.sharding import PartitionSpec as P

CHUNKS = 2


def from_partner(x, axis, apart):
    return lax.ppermute(x, axis, [(i, i ^ 1 << apart) for i in range(lax.axis_size(axis))])


def expand(r, bit, j):
    return ((r >> bit) << (bit + 1)) | (j << bit) | (r & ((1 << bit) - 1))


def compress(p, bit):
    return ((p >> (bit + 1)) << bit) | (p & ((1 << bit) - 1))


def mm(w, x):
    return jnp.dot(w, x, preferred_element_type=jnp.float32).astype(jnp.bfloat16)


def mm_t(w, x):
    product = lax.dot_general(w, x, (((0,), (0,)), ((), ())), preferred_element_type=jnp.float32)
    return product.astype(jnp.bfloat16)


def embed_tile(stored):
    half = stored.shape[-1] // 2
    lane = lax.broadcasted_iota(jnp.int32, stored.shape, 1)
    top = jnp.where(lane < half, stored, -stored)
    bottom = pltpu.roll(stored, half, 1)
    return jnp.concatenate([top, bottom], axis=0)


def block_pair(stored, own):
    width = stored.shape[-1] // 2
    first = embed_tile(stored[:, :width])
    second = embed_tile(stored[:, width:])
    if isinstance(own, int) and own == 0:
        return first, second
    return jnp.where(own == 0, first, second), jnp.where(own == 0, second, first)


def forward_weight(stored, own):
    first, second = block_pair(stored, own)
    return jnp.concatenate([first, second], axis=1)


def write_split(value_of, count, bit, own, stay_ref, leave_ref):
    for p in range(count):
        r = compress(p, bit)
        here = ((p >> bit) & 1) == own

        @pl.when(here)
        def _():
            stay_ref[r] = value_of(p)

        @pl.when(jnp.logical_not(here))
        def _():
            leave_ref[r] = value_of(p)


def read_split(kept_ref, arrived_ref, bit, own):
    def value_of(p):
        r = compress(p, bit)
        return jnp.where(((p >> bit) & 1) == own, kept_ref[r], arrived_ref[r])

    return value_of


def adjoint_pair(value_of, blocks_ref, bit, r, own):
    lower, upper = expand(r, bit, 0), expand(r, bit, 1)
    stacked = jnp.concatenate([value_of(lower), value_of(upper)], axis=0)
    first_lower, second_lower = block_pair(blocks_ref[lower], own)
    first_upper, second_upper = block_pair(blocks_ref[upper], own)
    kept = mm_t(jnp.concatenate([first_lower, first_upper], axis=0), stacked)
    leave = mm_t(jnp.concatenate([second_lower, second_upper], axis=0), stacked)
    return kept, leave


def forward_local_kernel(sc_ref, samples_ref, leaf_ref, local_ref, stay_ref, leave_ref, buf_a, buf_b,
                         *, count, levels, next_bit):
    for p in range(count):
        buf_a[p] = mm(embed_tile(leaf_ref[p]), samples_ref[p])
    src, dst = buf_a, buf_b
    for level in range(levels):
        for r in range(count // 2):
            p0, p1 = expand(r, level, 0), expand(r, level, 1)
            stacked = jnp.concatenate([src[p0], src[p1]], axis=0)
            dst[p0] = mm(forward_weight(local_ref[level, p0], 0), stacked)
            dst[p1] = mm(forward_weight(local_ref[level, p1], 0), stacked)
        src, dst = dst, src
    write_split(lambda p: src[p], count, next_bit, sc_ref[1], stay_ref, leave_ref)


def forward_cross_kernel(sc_ref, kept_ref, arrived_ref, blocks_ref, *rest, count, bit, next_bit, last):
    if last:
        spread_ref, out_ref, buf = rest
    else:
        stay_ref, leave_ref, buf = rest
    own = sc_ref[0]
    for r in range(count // 2):
        stacked = jnp.concatenate([kept_ref[r], arrived_ref[r]], axis=0)
        for j in range(2):
            p = expand(r, bit, j)
            buf[p] = mm(forward_weight(blocks_ref[p], own), stacked)
    if last:
        for p in range(count):
            out_ref[p] = mm(embed_tile(spread_ref[p]), buf[p])
    else:
        write_split(lambda p: buf[p], count, next_bit, sc_ref[1], stay_ref, leave_ref)


def adjoint_first_kernel(sc_ref, echoes_ref, spread_ref, blocks_ref, kept_ref, leave_ref, buf, *, count, bit):
    for p in range(count):
        buf[p] = mm_t(embed_tile(spread_ref[p]), echoes_ref[p])
    own = sc_ref[0]
    for r in range(count // 2):
        kept_ref[r], leave_ref[r] = adjoint_pair(lambda p: buf[p], blocks_ref, bit, r, own)


def adjoint_cross_kernel(sc_ref, prev_kept_ref, prev_arrived_ref, blocks_ref, kept_ref, leave_ref,
                         *, count, bit, prev_bit):
    value_of = read_split(prev_kept_ref, prev_arrived_ref, prev_bit, sc_ref[1])
    own = sc_ref[0]
    for r in range(count // 2):
        kept_ref[r], leave_ref[r] = adjoint_pair(value_of, blocks_ref, bit, r, own)


def adjoint_local_kernel(sc_ref, prev_kept_ref, prev_arrived_ref, local_ref, leaf_ref, out_ref, buf_a, buf_b,
                         *, count, levels, prev_bit):
    value_of = read_split(prev_kept_ref, prev_arrived_ref, prev_bit, sc_ref[1])
    for p in range(count):
        buf_a[p] = value_of(p)
    src, dst = buf_a, buf_b
    for level in reversed(range(levels)):
        for r in range(count // 2):
            first, second = adjoint_pair(lambda p: src[p], local_ref.at[level], level, r, 0)
            dst[expand(r, level, 0)] = first
            dst[expand(r, level, 1)] = second
        src, dst = dst, src
    for p in range(count):
        out_ref[p] = mm_t(embed_tile(leaf_ref[p]), src[p])


def whole(shape):
    return pl.BlockSpec(shape, lambda i, sc, n=len(shape): (0,) * n)


def column_block(shape, chunk):
    return pl.BlockSpec(shape, lambda i, sc, c=chunk: (0, 0, c))


def level_block(shape, level, count, grouped):
    if grouped:
        return pl.BlockSpec((None, count) + tuple(shape[2:]), lambda i, sc, v=level: (v, sc[2], 0, 0))
    return pl.BlockSpec((None, count) + tuple(shape[2:]), lambda i, sc, v=level: (v, 0, 0, 0))


def call(kernel, scalars, inputs, in_specs, out_shapes, scratch):
    grid_spec = pltpu.PrefetchScalarGridSpec(
        num_scalar_prefetch=1,
        grid=(1,),
        in_specs=in_specs,
        out_specs=[whole(s.shape) for s in out_shapes],
        scratch_shapes=scratch,
    )
    return pl.pallas_call(
        kernel,
        grid_spec=grid_spec,
        out_shape=out_shapes,
        compiler_params=pltpu.CompilerParams(vmem_limit_bytes=48 * 1024 * 1024),
    )(scalars, *inputs)


def per_device(samples, echoes, leaf_maps, local_blocks, cross_blocks, outer_blocks, spread_maps):
    levels_local = local_blocks.shape[0]
    inner_bits = cross_blocks.shape[0]
    outer_bits = outer_blocks.shape[0]
    count, rows, columns = samples.shape
    width = columns // CHUNKS
    tgt_index = lax.axis_index("tgt")
    src_index = lax.axis_index("src")
    bits = [m for m in range(inner_bits)] + [m for m in range(outer_bits)]
    axes = ["tgt"] * inner_bits + ["src"] * outer_bits
    own_bits = [tgt_index >> m & 1 for m in range(inner_bits)] + [src_index >> m & 1 for m in range(outer_bits)]
    sources = [(cross_blocks, m, True) for m in range(inner_bits)] + [(outer_blocks, m, False) for m in range(outer_bits)]
    n_cross = len(bits)

    def scalars(first, second):
        return jnp.stack([first, second, tgt_index]).astype(jnp.int32)

    def blocks_spec(index):
        array, level, grouped = sources[index]
        return level_block(array.shape, level, count, grouped)

    block = jax.ShapeDtypeStruct((count, rows, width), jnp.bfloat16)
    half = jax.ShapeDtypeStruct((count // 2, rows, width), jnp.bfloat16)
    half_spec = whole(half.shape)
    zero = tgt_index * 0

    def in_order(leave, earlier):
        if earlier is None:
            return leave
        leave, _ = lax.optimization_barrier((leave, earlier))
        return leave

    fwd = []
    for chunk in range(CHUNKS):
        fwd.append(call(
            functools.partial(forward_local_kernel, count=count, levels=levels_local, next_bit=bits[0]),
            scalars(zero, own_bits[0]),
            [samples, leaf_maps, local_blocks],
            [column_block((count, rows, width), chunk), whole(leaf_maps.shape), whole(local_blocks.shape)],
            [half, half],
            [pltpu.VMEM(block.shape, jnp.bfloat16), pltpu.VMEM(block.shape, jnp.bfloat16)],
        ))
    top = n_cross - 1
    adj = []
    for chunk in range(CHUNKS):
        adj.append(call(
            functools.partial(adjoint_first_kernel, count=count, bit=bits[top]),
            scalars(own_bits[top], zero),
            [echoes, spread_maps, sources[top][0]],
            [column_block((count, rows, width), chunk), whole(spread_maps.shape), blocks_spec(top)],
            [half, half],
            [pltpu.VMEM(block.shape, jnp.bfloat16)],
        ))

    image_parts = [None] * CHUNKS
    for step in range(n_cross):
        index = step
        bit, axis = bits[index], axes[index]
        last = index == n_cross - 1
        next_bit = 0 if last else bits[index + 1]
        earlier = None
        for chunk in range(CHUNKS):
            stay, leave = fwd[chunk]
            arrived = from_partner(in_order(leave, earlier), axis, bit)
            earlier = arrived
            inputs = [stay, arrived, sources[index][0]]
            specs = [half_spec, half_spec, blocks_spec(index)]
            if last:
                inputs.append(spread_maps)
                specs.append(whole(spread_maps.shape))
            result = call(
                functools.partial(forward_cross_kernel, count=count, bit=bit, next_bit=next_bit, last=last),
                scalars(own_bits[index], zero if last else own_bits[index + 1]),
                inputs,
                specs,
                [block] if last else [half, half],
                [pltpu.VMEM(block.shape, jnp.bfloat16)],
            )
            if last:
                image_parts[chunk] = result[0]
            else:
                fwd[chunk] = tuple(result)

        index = top - step
        earlier = None
        for chunk in range(CHUNKS):
            kept, leave = adj[chunk]
            arrived = from_partner(in_order(leave, earlier), axes[index], bits[index])
            earlier = arrived
            if index > 0:
                adj[chunk] = tuple(call(
                    functools.partial(adjoint_cross_kernel, count=count, bit=bits[index - 1], prev_bit=bits[index]),
                    scalars(own_bits[index - 1], own_bits[index]),
                    [kept, arrived, sources[index - 1][0]],
                    [half_spec, half_spec, blocks_spec(index - 1)],
                    [half, half],
                    [],
                ))
            else:
                adj[chunk] = (kept, arrived)

    aperture_parts = []
    for chunk in range(CHUNKS):
        kept, arrived = adj[chunk]
        (aperture,) = call(
            functools.partial(adjoint_local_kernel, count=count, levels=levels_local, prev_bit=bits[0]),
            scalars(zero, own_bits[0]),
            [kept, arrived, local_blocks, leaf_maps],
            [half_spec, half_spec, whole(local_blocks.shape), whole(leaf_maps.shape)],
            [block],
            [pltpu.VMEM(block.shape, jnp.bfloat16), pltpu.VMEM(block.shape, jnp.bfloat16)],
        )
        aperture_parts.append(aperture)
    image_field = jnp.concatenate(image_parts, axis=-1)
    aperture_field = jnp.concatenate(aperture_parts, axis=-1)
    return (image_field, aperture_field)


def solution(mesh):
    return jax.shard_map(
        per_device,
        mesh=mesh,
        in_specs=(
            P(("src", "tgt"), None, None),
            P(("src", "tgt"), None, None),
            P(("src", "tgt"), None, None),
            P(None, ("src", "tgt"), None, None),
            P(None, "src", None, None),
            P(None, ("src", "tgt"), None, None),
            P(("src", "tgt"), None, None),
        ),
        out_specs=(P(("src", "tgt"), None, None), P(("src", "tgt"), None, None)),
        check_vma=False,
    )
```

```python
import functools

import jax
import jax.numpy as jnp
from jax import lax
from jax.experimental import pallas as pl
from jax.experimental.pallas import tpu as pltpu
from jax.sharding import PartitionSpec as P

CHUNKS = 4


def from_partner(x, axis, apart):
    return lax.ppermute(x, axis, [(i, i ^ 1 << apart) for i in range(lax.axis_size(axis))])


def expand(r, bit, j):
    return ((r >> bit) << (bit + 1)) | (j << bit) | (r & ((1 << bit) - 1))


def compress(p, bit):
    return ((p >> (bit + 1)) << bit) | (p & ((1 << bit) - 1))


def mm(w, x):
    return jnp.dot(w, x, preferred_element_type=jnp.float32).astype(jnp.bfloat16)


def mm_t(w, x):
    product = lax.dot_general(w, x, (((0,), (0,)), ((), ())), preferred_element_type=jnp.float32)
    return product.astype(jnp.bfloat16)


def embed_tile(stored):
    half = stored.shape[-1] // 2
    lane = lax.broadcasted_iota(jnp.int32, stored.shape, 1)
    top = jnp.where(lane < half, stored, -stored)
    bottom = pltpu.roll(stored, half, 1)
    return jnp.concatenate([top, bottom], axis=0)


def block_pair(stored, own):
    width = stored.shape[-1] // 2
    first = embed_tile(stored[:, :width])
    second = embed_tile(stored[:, width:])
    if isinstance(own, int) and own == 0:
        return first, second
    return jnp.where(own == 0, first, second), jnp.where(own == 0, second, first)


def forward_weight(stored, own):
    first, second = block_pair(stored, own)
    return jnp.concatenate([first, second], axis=1)


def write_split(value_of, count, bit, own, stay_ref, leave_ref):
    for p in range(count):
        r = compress(p, bit)
        here = ((p >> bit) & 1) == own

        @pl.when(here)
        def _():
            stay_ref[r] = value_of(p)

        @pl.when(jnp.logical_not(here))
        def _():
            leave_ref[r] = value_of(p)


def read_split(kept_ref, arrived_ref, bit, own):
    def value_of(p):
        r = compress(p, bit)
        return jnp.where(((p >> bit) & 1) == own, kept_ref[r], arrived_ref[r])

    return value_of


def adjoint_pair(value_of, blocks_ref, bit, r, own):
    lower, upper = expand(r, bit, 0), expand(r, bit, 1)
    stacked = jnp.concatenate([value_of(lower), value_of(upper)], axis=0)
    first_lower, second_lower = block_pair(blocks_ref[lower], own)
    first_upper, second_upper = block_pair(blocks_ref[upper], own)
    kept = mm_t(jnp.concatenate([first_lower, first_upper], axis=0), stacked)
    leave = mm_t(jnp.concatenate([second_lower, second_upper], axis=0), stacked)
    return kept, leave


def forward_local_kernel(sc_ref, samples_ref, leaf_ref, local_ref, stay_ref, leave_ref, buf_a, buf_b,
                         *, count, levels, next_bit):
    for p in range(count):
        buf_a[p] = mm(embed_tile(leaf_ref[p]), samples_ref[p])
    src, dst = buf_a, buf_b
    for level in range(levels):
        for r in range(count // 2):
            p0, p1 = expand(r, level, 0), expand(r, level, 1)
            stacked = jnp.concatenate([src[p0], src[p1]], axis=0)
            dst[p0] = mm(forward_weight(local_ref[level, p0], 0), stacked)
            dst[p1] = mm(forward_weight(local_ref[level, p1], 0), stacked)
        src, dst = dst, src
    write_split(lambda p: src[p], count, next_bit, sc_ref[1], stay_ref, leave_ref)


def forward_cross_kernel(sc_ref, kept_ref, arrived_ref, blocks_ref, *rest, count, bit, next_bit, last):
    if last:
        spread_ref, out_ref, buf = rest
    else:
        stay_ref, leave_ref, buf = rest
    own = sc_ref[0]
    for r in range(count // 2):
        stacked = jnp.concatenate([kept_ref[r], arrived_ref[r]], axis=0)
        for j in range(2):
            p = expand(r, bit, j)
            buf[p] = mm(forward_weight(blocks_ref[p], own), stacked)
    if last:
        for p in range(count):
            out_ref[p] = mm(embed_tile(spread_ref[p]), buf[p])
    else:
        write_split(lambda p: buf[p], count, next_bit, sc_ref[1], stay_ref, leave_ref)


def adjoint_first_kernel(sc_ref, echoes_ref, spread_ref, blocks_ref, kept_ref, leave_ref, buf, *, count, bit):
    for p in range(count):
        buf[p] = mm_t(embed_tile(spread_ref[p]), echoes_ref[p])
    own = sc_ref[0]
    for r in range(count // 2):
        kept_ref[r], leave_ref[r] = adjoint_pair(lambda p: buf[p], blocks_ref, bit, r, own)


def adjoint_cross_kernel(sc_ref, prev_kept_ref, prev_arrived_ref, blocks_ref, kept_ref, leave_ref,
                         *, count, bit, prev_bit):
    value_of = read_split(prev_kept_ref, prev_arrived_ref, prev_bit, sc_ref[1])
    own = sc_ref[0]
    for r in range(count // 2):
        kept_ref[r], leave_ref[r] = adjoint_pair(value_of, blocks_ref, bit, r, own)


def adjoint_local_kernel(sc_ref, prev_kept_ref, prev_arrived_ref, local_ref, leaf_ref, out_ref, buf_a, buf_b,
                         *, count, levels, prev_bit):
    value_of = read_split(prev_kept_ref, prev_arrived_ref, prev_bit, sc_ref[1])
    for p in range(count):
        buf_a[p] = value_of(p)
    src, dst = buf_a, buf_b
    for level in reversed(range(levels)):
        for r in range(count // 2):
            first, second = adjoint_pair(lambda p: src[p], local_ref.at[level], level, r, 0)
            dst[expand(r, level, 0)] = first
            dst[expand(r, level, 1)] = second
        src, dst = dst, src
    for p in range(count):
        out_ref[p] = mm_t(embed_tile(leaf_ref[p]), src[p])


def whole(shape):
    return pl.BlockSpec(shape, lambda i, sc, n=len(shape): (0,) * n)


def column_block(shape, chunk):
    return pl.BlockSpec(shape, lambda i, sc, c=chunk: (0, 0, c))


def level_block(shape, level, count, grouped):
    if grouped:
        return pl.BlockSpec((None, count) + tuple(shape[2:]), lambda i, sc, v=level: (v, sc[2], 0, 0))
    return pl.BlockSpec((None, count) + tuple(shape[2:]), lambda i, sc, v=level: (v, 0, 0, 0))


def call(kernel, scalars, inputs, in_specs, out_shapes, scratch):
    grid_spec = pltpu.PrefetchScalarGridSpec(
        num_scalar_prefetch=1,
        grid=(1,),
        in_specs=in_specs,
        out_specs=[whole(s.shape) for s in out_shapes],
        scratch_shapes=scratch,
    )
    return pl.pallas_call(
        kernel,
        grid_spec=grid_spec,
        out_shape=out_shapes,
        compiler_params=pltpu.CompilerParams(vmem_limit_bytes=48 * 1024 * 1024),
    )(scalars, *inputs)


def per_device(samples, echoes, leaf_maps, local_blocks, cross_blocks, outer_blocks, spread_maps):
    levels_local = local_blocks.shape[0]
    inner_bits = cross_blocks.shape[0]
    outer_bits = outer_blocks.shape[0]
    count, rows, columns = samples.shape
    width = columns // CHUNKS
    tgt_index = lax.axis_index("tgt")
    src_index = lax.axis_index("src")
    bits = [m for m in range(inner_bits)] + [m for m in range(outer_bits)]
    axes = ["tgt"] * inner_bits + ["src"] * outer_bits
    own_bits = [tgt_index >> m & 1 for m in range(inner_bits)] + [src_index >> m & 1 for m in range(outer_bits)]
    sources = [(cross_blocks, m, True) for m in range(inner_bits)] + [(outer_blocks, m, False) for m in range(outer_bits)]
    n_cross = len(bits)

    def scalars(first, second):
        return jnp.stack([first, second, tgt_index]).astype(jnp.int32)

    def blocks_spec(index):
        array, level, grouped = sources[index]
        return level_block(array.shape, level, count, grouped)

    block = jax.ShapeDtypeStruct((count, rows, width), jnp.bfloat16)
    half = jax.ShapeDtypeStruct((count // 2, rows, width), jnp.bfloat16)
    half_spec = whole(half.shape)
    zero = tgt_index * 0

    def in_order(leave, earlier):
        if earlier is None:
            return leave
        leave, _ = lax.optimization_barrier((leave, earlier))
        return leave

    fwd = []
    for chunk in range(CHUNKS):
        fwd.append(call(
            functools.partial(forward_local_kernel, count=count, levels=levels_local, next_bit=bits[0]),
            scalars(zero, own_bits[0]),
            [samples, leaf_maps, local_blocks],
            [column_block((count, rows, width), chunk), whole(leaf_maps.shape), whole(local_blocks.shape)],
            [half, half],
            [pltpu.VMEM(block.shape, jnp.bfloat16), pltpu.VMEM(block.shape, jnp.bfloat16)],
        ))
    top = n_cross - 1
    adj = []
    for chunk in range(CHUNKS):
        adj.append(call(
            functools.partial(adjoint_first_kernel, count=count, bit=bits[top]),
            scalars(own_bits[top], zero),
            [echoes, spread_maps, sources[top][0]],
            [column_block((count, rows, width), chunk), whole(spread_maps.shape), blocks_spec(top)],
            [half, half],
            [pltpu.VMEM(block.shape, jnp.bfloat16)],
        ))

    image_parts = [None] * CHUNKS
    for step in range(n_cross):
        index = step
        bit, axis = bits[index], axes[index]
        last = index == n_cross - 1
        next_bit = 0 if last else bits[index + 1]
        earlier = None
        for chunk in range(CHUNKS):
            stay, leave = fwd[chunk]
            arrived = from_partner(in_order(leave, earlier), axis, bit)
            earlier = arrived
            inputs = [stay, arrived, sources[index][0]]
            specs = [half_spec, half_spec, blocks_spec(index)]
            if last:
                inputs.append(spread_maps)
                specs.append(whole(spread_maps.shape))
            result = call(
                functools.partial(forward_cross_kernel, count=count, bit=bit, next_bit=next_bit, last=last),
                scalars(own_bits[index], zero if last else own_bits[index + 1]),
                inputs,
                specs,
                [block] if last else [half, half],
                [pltpu.VMEM(block.shape, jnp.bfloat16)],
            )
            if last:
                image_parts[chunk] = result[0]
            else:
                fwd[chunk] = tuple(result)

        index = top - step
        earlier = None
        for chunk in range(CHUNKS):
            kept, leave = adj[chunk]
            arrived = from_partner(in_order(leave, earlier), axes[index], bits[index])
            earlier = arrived
            if index > 0:
                adj[chunk] = tuple(call(
                    functools.partial(adjoint_cross_kernel, count=count, bit=bits[index - 1], prev_bit=bits[index]),
                    scalars(own_bits[index - 1], own_bits[index]),
                    [kept, arrived, sources[index - 1][0]],
                    [half_spec, half_spec, blocks_spec(index - 1)],
                    [half, half],
                    [],
                ))
            else:
                adj[chunk] = (kept, arrived)

    aperture_parts = []
    for chunk in range(CHUNKS):
        kept, arrived = adj[chunk]
        (aperture,) = call(
            functools.partial(adjoint_local_kernel, count=count, levels=levels_local, prev_bit=bits[0]),
            scalars(zero, own_bits[0]),
            [kept, arrived, local_blocks, leaf_maps],
            [half_spec, half_spec, whole(local_blocks.shape), whole(leaf_maps.shape)],
            [block],
            [pltpu.VMEM(block.shape, jnp.bfloat16), pltpu.VMEM(block.shape, jnp.bfloat16)],
        )
        aperture_parts.append(aperture)
    image_field = jnp.concatenate(image_parts, axis=-1)
    aperture_field = jnp.concatenate(aperture_parts, axis=-1)
    return (image_field, aperture_field)


def solution(mesh):
    return jax.shard_map(
        per_device,
        mesh=mesh,
        in_specs=(
            P(("src", "tgt"), None, None),
            P(("src", "tgt"), None, None),
            P(("src", "tgt"), None, None),
            P(None, ("src", "tgt"), None, None),
            P(None, "src", None, None),
            P(None, ("src", "tgt"), None, None),
            P(("src", "tgt"), None, None),
        ),
        out_specs=(P(("src", "tgt"), None, None), P(("src", "tgt"), None, None)),
        check_vma=False,
    )
```

```python
import functools

import jax
import jax.numpy as jnp
from jax import lax
from jax.experimental import pallas as pl
from jax.experimental.pallas import tpu as pltpu
from jax.sharding import PartitionSpec as P

CHUNKS = 2


def from_partner(x, axis, apart):
    return lax.ppermute(x, axis, [(i, i ^ 1 << apart) for i in range(lax.axis_size(axis))])


def expand(r, bit, j):
    return ((r >> bit) << (bit + 1)) | (j << bit) | (r & ((1 << bit) - 1))


def compress(p, bit):
    return ((p >> (bit + 1)) << bit) | (p & ((1 << bit) - 1))


def mm(w, x):
    return jnp.dot(w, x, preferred_element_type=jnp.float32).astype(jnp.bfloat16)


def mm_t(w, x):
    product = lax.dot_general(w, x, (((0,), (0,)), ((), ())), preferred_element_type=jnp.float32)
    return product.astype(jnp.bfloat16)


def embed_tile(stored):
    half = stored.shape[-1] // 2
    lane = lax.broadcasted_iota(jnp.int32, stored.shape, 1)
    top = jnp.where(lane < half, stored, -stored)
    bottom = pltpu.roll(stored, half, 1)
    return jnp.concatenate([top, bottom], axis=0)


def block_pair(stored, own):
    width = stored.shape[-1] // 2
    first = embed_tile(stored[:, :width])
    second = embed_tile(stored[:, width:])
    if isinstance(own, int) and own == 0:
        return first, second
    return jnp.where(own == 0, first, second), jnp.where(own == 0, second, first)


def forward_weight(stored, own):
    first, second = block_pair(stored, own)
    return jnp.concatenate([first, second], axis=1)


def write_split(value_of, count, bit, own, stay_ref, leave_ref):
    for p in range(count):
        r = compress(p, bit)
        here = ((p >> bit) & 1) == own

        @pl.when(here)
        def _():
            stay_ref[r] = value_of(p)

        @pl.when(jnp.logical_not(here))
        def _():
            leave_ref[r] = value_of(p)


def read_split(kept_ref, arrived_ref, bit, own):
    def value_of(p):
        r = compress(p, bit)
        return jnp.where(((p >> bit) & 1) == own, kept_ref[r], arrived_ref[r])

    return value_of


def adjoint_pair(value_of, blocks_ref, bit, r, own):
    lower, upper = expand(r, bit, 0), expand(r, bit, 1)
    stacked = jnp.concatenate([value_of(lower), value_of(upper)], axis=0)
    first_lower, second_lower = block_pair(blocks_ref[lower], own)
    first_upper, second_upper = block_pair(blocks_ref[upper], own)
    kept = mm_t(jnp.concatenate([first_lower, first_upper], axis=0), stacked)
    leave = mm_t(jnp.concatenate([second_lower, second_upper], axis=0), stacked)
    return kept, leave


def forward_local_kernel(sc_ref, samples_ref, leaf_ref, local_ref, stay_ref, leave_ref, buf_a, buf_b,
                         *, count, levels, next_bit):
    for p in range(count):
        buf_a[p] = mm(embed_tile(leaf_ref[p]), samples_ref[p])
    src, dst = buf_a, buf_b
    for level in range(levels):
        for r in range(count // 2):
            p0, p1 = expand(r, level, 0), expand(r, level, 1)
            stacked = jnp.concatenate([src[p0], src[p1]], axis=0)
            dst[p0] = mm(forward_weight(local_ref[level, p0], 0), stacked)
            dst[p1] = mm(forward_weight(local_ref[level, p1], 0), stacked)
        src, dst = dst, src
    write_split(lambda p: src[p], count, next_bit, sc_ref[1], stay_ref, leave_ref)


def forward_cross_kernel(sc_ref, kept_ref, arrived_ref, blocks_ref, *rest, count, bit, next_bit, last, prior=False):
    if last:
        spread_ref, out_ref, buf = (rest[0],) + rest[1 + prior:]
    else:
        stay_ref, leave_ref, buf = rest
    own = sc_ref[0]
    for r in range(count // 2):
        stacked = jnp.concatenate([kept_ref[r], arrived_ref[r]], axis=0)
        for j in range(2):
            p = expand(r, bit, j)
            buf[p] = mm(forward_weight(blocks_ref[p], own), stacked)
    if last:
        for p in range(count):
            out_ref[p] = mm(embed_tile(spread_ref[p]), buf[p])
    else:
        write_split(lambda p: buf[p], count, next_bit, sc_ref[1], stay_ref, leave_ref)


def adjoint_first_kernel(sc_ref, echoes_ref, spread_ref, blocks_ref, kept_ref, leave_ref, buf, *, count, bit):
    for p in range(count):
        buf[p] = mm_t(embed_tile(spread_ref[p]), echoes_ref[p])
    own = sc_ref[0]
    for r in range(count // 2):
        kept_ref[r], leave_ref[r] = adjoint_pair(lambda p: buf[p], blocks_ref, bit, r, own)


def adjoint_cross_kernel(sc_ref, prev_kept_ref, prev_arrived_ref, blocks_ref, kept_ref, leave_ref,
                         *, count, bit, prev_bit):
    value_of = read_split(prev_kept_ref, prev_arrived_ref, prev_bit, sc_ref[1])
    own = sc_ref[0]
    for r in range(count // 2):
        kept_ref[r], leave_ref[r] = adjoint_pair(value_of, blocks_ref, bit, r, own)


def adjoint_local_kernel(sc_ref, prev_kept_ref, prev_arrived_ref, local_ref, leaf_ref, *rest,
                         count, levels, prev_bit, prior=False):
    out_ref, buf_a, buf_b = rest[prior:]
    value_of = read_split(prev_kept_ref, prev_arrived_ref, prev_bit, sc_ref[1])
    for p in range(count):
        buf_a[p] = value_of(p)
    src, dst = buf_a, buf_b
    for level in reversed(range(levels)):
        for r in range(count // 2):
            first, second = adjoint_pair(lambda p: src[p], local_ref.at[level], level, r, 0)
            dst[expand(r, level, 0)] = first
            dst[expand(r, level, 1)] = second
        src, dst = dst, src
    for p in range(count):
        out_ref[p] = mm_t(embed_tile(leaf_ref[p]), src[p])


def whole(shape):
    return pl.BlockSpec(shape, lambda i, sc, n=len(shape): (0,) * n)


def column_block(shape, chunk):
    return pl.BlockSpec(shape, lambda i, sc, c=chunk: (0, 0, c))


def level_block(shape, level, count, grouped):
    if grouped:
        return pl.BlockSpec((None, count) + tuple(shape[2:]), lambda i, sc, v=level: (v, sc[2], 0, 0))
    return pl.BlockSpec((None, count) + tuple(shape[2:]), lambda i, sc, v=level: (v, 0, 0, 0))


def call(kernel, scalars, inputs, in_specs, out_shapes, scratch, out_specs=None, aliases=None):
    grid_spec = pltpu.PrefetchScalarGridSpec(
        num_scalar_prefetch=1,
        grid=(1,),
        in_specs=in_specs,
        out_specs=out_specs or [whole(s.shape) for s in out_shapes],
        scratch_shapes=scratch,
    )
    return pl.pallas_call(
        kernel,
        grid_spec=grid_spec,
        out_shape=out_shapes,
        input_output_aliases=aliases or {},
        compiler_params=pltpu.CompilerParams(vmem_limit_bytes=48 * 1024 * 1024),
    )(scalars, *inputs)


def into_columns(kernel, scalars, inputs, in_specs, scratch, full, part, chunk, prior):
    if prior is None:
        return call(kernel, scalars, inputs, in_specs, [full], scratch,
                    out_specs=[column_block(part.shape, chunk)])
    return call(functools.partial(kernel, prior=True), scalars, inputs[:len(in_specs)] + [prior],
                in_specs + [pl.BlockSpec(memory_space=pl.ANY)], [full], scratch,
                out_specs=[column_block(part.shape, chunk)], aliases={1 + len(in_specs): 0})


def per_device(samples, echoes, leaf_maps, local_blocks, cross_blocks, outer_blocks, spread_maps):
    levels_local = local_blocks.shape[0]
    inner_bits = cross_blocks.shape[0]
    outer_bits = outer_blocks.shape[0]
    count, rows, columns = samples.shape
    width = columns // CHUNKS
    tgt_index = lax.axis_index("tgt")
    src_index = lax.axis_index("src")
    bits = [m for m in range(inner_bits)] + [m for m in range(outer_bits)]
    axes = ["tgt"] * inner_bits + ["src"] * outer_bits
    own_bits = [tgt_index >> m & 1 for m in range(inner_bits)] + [src_index >> m & 1 for m in range(outer_bits)]
    sources = [(cross_blocks, m, True) for m in range(inner_bits)] + [(outer_blocks, m, False) for m in range(outer_bits)]
    n_cross = len(bits)

    def scalars(first, second):
        return jnp.stack([first, second, tgt_index]).astype(jnp.int32)

    def blocks_spec(index):
        array, level, grouped = sources[index]
        return level_block(array.shape, level, count, grouped)

    block = jax.ShapeDtypeStruct((count, rows, width), jnp.bfloat16)
    half = jax.ShapeDtypeStruct((count // 2, rows, width), jnp.bfloat16)
    half_spec = whole(half.shape)
    zero = tgt_index * 0

    def in_order(leave, earlier):
        if earlier is None:
            return leave
        leave, _ = lax.optimization_barrier((leave, earlier))
        return leave

    fwd = []
    for chunk in range(CHUNKS):
        fwd.append(call(
            functools.partial(forward_local_kernel, count=count, levels=levels_local, next_bit=bits[0]),
            scalars(zero, own_bits[0]),
            [samples, leaf_maps, local_blocks],
            [column_block((count, rows, width), chunk), whole(leaf_maps.shape), whole(local_blocks.shape)],
            [half, half],
            [pltpu.VMEM(block.shape, jnp.bfloat16), pltpu.VMEM(block.shape, jnp.bfloat16)],
        ))
    top = n_cross - 1
    adj = []
    for chunk in range(CHUNKS):
        adj.append(call(
            functools.partial(adjoint_first_kernel, count=count, bit=bits[top]),
            scalars(own_bits[top], zero),
            [echoes, spread_maps, sources[top][0]],
            [column_block((count, rows, width), chunk), whole(spread_maps.shape), blocks_spec(top)],
            [half, half],
            [pltpu.VMEM(block.shape, jnp.bfloat16)],
        ))

    full = jax.ShapeDtypeStruct(samples.shape, jnp.bfloat16)
    image_field = None
    for step in range(n_cross):
        index = step
        bit, axis = bits[index], axes[index]
        last = index == n_cross - 1
        next_bit = 0 if last else bits[index + 1]
        earlier = None
        for chunk in range(CHUNKS):
            stay, leave = fwd[chunk]
            arrived = from_partner(in_order(leave, earlier), axis, bit)
            earlier = arrived
            inputs = [stay, arrived, sources[index][0]]
            specs = [half_spec, half_spec, blocks_spec(index)]
            if last:
                inputs.append(spread_maps)
                specs.append(whole(spread_maps.shape))
            kernel = functools.partial(forward_cross_kernel, count=count, bit=bit, next_bit=next_bit, last=last)
            if last:
                (image_field,) = into_columns(
                    kernel, scalars(own_bits[index], zero), inputs, specs,
                    [pltpu.VMEM(block.shape, jnp.bfloat16)], full, block, chunk, image_field)
            else:
                fwd[chunk] = tuple(call(
                    kernel,
                    scalars(own_bits[index], own_bits[index + 1]),
                    inputs,
                    specs,
                    [half, half],
                    [pltpu.VMEM(block.shape, jnp.bfloat16)],
                ))

        index = top - step
        earlier = None
        for chunk in range(CHUNKS):
            kept, leave = adj[chunk]
            arrived = from_partner(in_order(leave, earlier), axes[index], bits[index])
            earlier = arrived
            if index > 0:
                adj[chunk] = tuple(call(
                    functools.partial(adjoint_cross_kernel, count=count, bit=bits[index - 1], prev_bit=bits[index]),
                    scalars(own_bits[index - 1], own_bits[index]),
                    [kept, arrived, sources[index - 1][0]],
                    [half_spec, half_spec, blocks_spec(index - 1)],
                    [half, half],
                    [],
                ))
            else:
                adj[chunk] = (kept, arrived)

    aperture_field = None
    for chunk in range(CHUNKS):
        kept, arrived = adj[chunk]
        (aperture_field,) = into_columns(
            functools.partial(adjoint_local_kernel, count=count, levels=levels_local, prev_bit=bits[0]),
            scalars(zero, own_bits[0]),
            [kept, arrived, local_blocks, leaf_maps],
            [half_spec, half_spec, whole(local_blocks.shape), whole(leaf_maps.shape)],
            [pltpu.VMEM(block.shape, jnp.bfloat16), pltpu.VMEM(block.shape, jnp.bfloat16)],
            full, block, chunk, aperture_field)
    return (image_field, aperture_field)


def solution(mesh):
    return jax.shard_map(
        per_device,
        mesh=mesh,
        in_specs=(
            P(("src", "tgt"), None, None),
            P(("src", "tgt"), None, None),
            P(("src", "tgt"), None, None),
            P(None, ("src", "tgt"), None, None),
            P(None, "src", None, None),
            P(None, ("src", "tgt"), None, None),
            P(("src", "tgt"), None, None),
        ),
        out_specs=(P(("src", "tgt"), None, None), P(("src", "tgt"), None, None)),
        check_vma=False,
    )
```

```python
import functools

import jax
import jax.numpy as jnp
from jax import lax
from jax.experimental import pallas as pl
from jax.experimental.pallas import tpu as pltpu
from jax.sharding import PartitionSpec as P

CHUNKS = 2


def from_partner(x, axis, apart):
    return lax.ppermute(x, axis, [(i, i ^ 1 << apart) for i in range(lax.axis_size(axis))])


def expand(r, bit, j):
    return ((r >> bit) << (bit + 1)) | (j << bit) | (r & ((1 << bit) - 1))


def compress(p, bit):
    return ((p >> (bit + 1)) << bit) | (p & ((1 << bit) - 1))


def mm(w, x):
    return jnp.dot(w, x, preferred_element_type=jnp.float32).astype(jnp.bfloat16)


def mm_t(w, x):
    product = lax.dot_general(w, x, (((0,), (0,)), ((), ())), preferred_element_type=jnp.float32)
    return product.astype(jnp.bfloat16)


def embed_tile(stored):
    half = stored.shape[-1] // 2
    lane = lax.broadcasted_iota(jnp.int32, stored.shape, 1)
    top = jnp.where(lane < half, stored, -stored)
    bottom = pltpu.roll(stored, half, 1)
    return jnp.concatenate([top, bottom], axis=0)


def block_pair(stored, own):
    width = stored.shape[-1] // 2
    first = embed_tile(stored[:, :width])
    second = embed_tile(stored[:, width:])
    if isinstance(own, int) and own == 0:
        return first, second
    return jnp.where(own == 0, first, second), jnp.where(own == 0, second, first)


def forward_weight(stored, own):
    first, second = block_pair(stored, own)
    return jnp.concatenate([first, second], axis=1)


def write_split(value_of, count, bit, own, stay_ref, leave_ref):
    for p in range(count):
        r = compress(p, bit)
        here = ((p >> bit) & 1) == own

        @pl.when(here)
        def _():
            stay_ref[r] = value_of(p)

        @pl.when(jnp.logical_not(here))
        def _():
            leave_ref[r] = value_of(p)


def read_split(kept_ref, arrived_ref, bit, own):
    def value_of(p):
        r = compress(p, bit)
        return jnp.where(((p >> bit) & 1) == own, kept_ref[r], arrived_ref[r])

    return value_of


def adjoint_pair(value_of, weight_ref, bit, r):
    stacked = jnp.concatenate([value_of(expand(r, bit, 0)), value_of(expand(r, bit, 1))], axis=0)
    return mm(weight_ref[r, 0], stacked), mm(weight_ref[r, 1], stacked)


def forward_local_kernel(sc_ref, samples_ref, leaf_ref, local_ref, stay_ref, leave_ref, buf_a, buf_b,
                         *, count, levels, next_bit):
    for p in range(count):
        buf_a[p] = mm(embed_tile(leaf_ref[p]), samples_ref[p])
    src, dst = buf_a, buf_b
    for level in range(levels):
        for r in range(count // 2):
            p0, p1 = expand(r, level, 0), expand(r, level, 1)
            stacked = jnp.concatenate([src[p0], src[p1]], axis=0)
            dst[p0] = mm(forward_weight(local_ref[level, p0], 0), stacked)
            dst[p1] = mm(forward_weight(local_ref[level, p1], 0), stacked)
        src, dst = dst, src
    write_split(lambda p: src[p], count, next_bit, sc_ref[1], stay_ref, leave_ref)


def forward_cross_kernel(sc_ref, kept_ref, arrived_ref, blocks_ref, *rest, count, bit, next_bit, last, prior=False):
    if last:
        spread_ref, out_ref, buf = (rest[0],) + rest[1 + prior:]
    else:
        stay_ref, leave_ref, buf = rest
    own = sc_ref[0]
    for r in range(count // 2):
        stacked = jnp.concatenate([kept_ref[r], arrived_ref[r]], axis=0)
        for j in range(2):
            p = expand(r, bit, j)
            buf[p] = mm(forward_weight(blocks_ref[p], own), stacked)
    if last:
        for p in range(count):
            out_ref[p] = mm(embed_tile(spread_ref[p]), buf[p])
    else:
        write_split(lambda p: buf[p], count, next_bit, sc_ref[1], stay_ref, leave_ref)


def adjoint_first_kernel(sc_ref, echoes_ref, spread_ref, blocks_ref, kept_ref, leave_ref, buf, *, count, bit):
    for p in range(count):
        buf[p] = mm(spread_ref[p], echoes_ref[p])
    for r in range(count // 2):
        kept_ref[r], leave_ref[r] = adjoint_pair(lambda p: buf[p], blocks_ref, bit, r)


def adjoint_cross_kernel(sc_ref, prev_kept_ref, prev_arrived_ref, blocks_ref, kept_ref, leave_ref,
                         *, count, bit, prev_bit):
    value_of = read_split(prev_kept_ref, prev_arrived_ref, prev_bit, sc_ref[1])
    for r in range(count // 2):
        kept_ref[r], leave_ref[r] = adjoint_pair(value_of, blocks_ref, bit, r)


def adjoint_local_kernel(sc_ref, prev_kept_ref, prev_arrived_ref, local_ref, leaf_ref, *rest,
                         count, levels, prev_bit, prior=False):
    out_ref, buf_a, buf_b = rest[prior:]
    value_of = read_split(prev_kept_ref, prev_arrived_ref, prev_bit, sc_ref[1])
    for p in range(count):
        buf_a[p] = value_of(p)
    src, dst = buf_a, buf_b
    for level in reversed(range(levels)):
        for r in range(count // 2):
            first, second = adjoint_pair(lambda p: src[p], local_ref.at[level], level, r)
            dst[expand(r, level, 0)] = first
            dst[expand(r, level, 1)] = second
        src, dst = dst, src
    for p in range(count):
        out_ref[p] = mm(leaf_ref[p], src[p])


def transpose_tile(tile):
    return tile.astype(jnp.float32).T.astype(jnp.bfloat16)


def prep_adjoint_kernel(sc_ref, blocks_ref, adj_ref, *, count, bits, flip):
    size = 2 * blocks_ref.shape[-2]
    own = sc_ref[0] if flip else 0
    for level, bit in enumerate(bits):
        for r in range(count // 2):
            for j in range(2):
                first, second = block_pair(blocks_ref[level, expand(r, bit, j)], own)
                adj_ref[level, r, 0, :, j * size:(j + 1) * size] = transpose_tile(first)
                adj_ref[level, r, 1, :, j * size:(j + 1) * size] = transpose_tile(second)


def prep_map_kernel(maps_ref, adj_ref, *, count):
    for p in range(count):
        adj_ref[p] = transpose_tile(embed_tile(maps_ref[p]))


def prep_map(maps):
    count, rank, width = maps.shape
    return pl.pallas_call(
        functools.partial(prep_map_kernel, count=count),
        grid=(1,),
        in_specs=[pl.BlockSpec((count, rank, width), lambda i: (0, 0, 0))],
        out_specs=pl.BlockSpec((count, width, width), lambda i: (0, 0, 0)),
        out_shape=jax.ShapeDtypeStruct((count, width, width), jnp.bfloat16),
    )(maps)


def prep_adjoint(blocks, spec, scalars, bits, count, flip):
    levels = len(bits)
    rank, width = blocks.shape[-2], blocks.shape[-1]
    shape = (levels, count // 2, 2, 2 * rank, width)
    return pl.pallas_call(
        functools.partial(prep_adjoint_kernel, count=count, bits=bits, flip=flip),
        grid_spec=pltpu.PrefetchScalarGridSpec(
            num_scalar_prefetch=1, grid=(1,), in_specs=[spec], out_specs=whole(shape)),
        out_shape=jax.ShapeDtypeStruct(shape, jnp.bfloat16),
    )(scalars, blocks)


def whole(shape):
    return pl.BlockSpec(shape, lambda i, sc, n=len(shape): (0,) * n)


def column_block(shape, chunk):
    return pl.BlockSpec(shape, lambda i, sc, c=chunk: (0, 0, c))


def level_block(shape, level, count, grouped):
    if grouped:
        return pl.BlockSpec((None, count) + tuple(shape[2:]), lambda i, sc, v=level: (v, sc[2], 0, 0))
    return pl.BlockSpec((None, count) + tuple(shape[2:]), lambda i, sc, v=level: (v, 0, 0, 0))


def call(kernel, scalars, inputs, in_specs, out_shapes, scratch, out_specs=None, aliases=None):
    grid_spec = pltpu.PrefetchScalarGridSpec(
        num_scalar_prefetch=1,
        grid=(1,),
        in_specs=in_specs,
        out_specs=out_specs or [whole(s.shape) for s in out_shapes],
        scratch_shapes=scratch,
    )
    return pl.pallas_call(
        kernel,
        grid_spec=grid_spec,
        out_shape=out_shapes,
        input_output_aliases=aliases or {},
        compiler_params=pltpu.CompilerParams(vmem_limit_bytes=48 * 1024 * 1024),
    )(scalars, *inputs)


def into_columns(kernel, scalars, inputs, in_specs, scratch, full, part, chunk, prior):
    if prior is None:
        return call(kernel, scalars, inputs, in_specs, [full], scratch,
                    out_specs=[column_block(part.shape, chunk)])
    return call(functools.partial(kernel, prior=True), scalars, inputs[:len(in_specs)] + [prior],
                in_specs + [pl.BlockSpec(memory_space=pl.ANY)], [full], scratch,
                out_specs=[column_block(part.shape, chunk)], aliases={1 + len(in_specs): 0})


def zero_of(index):
    return index * 0


def per_device(samples, echoes, leaf_maps, local_blocks, cross_blocks, outer_blocks, spread_maps):
    levels_local = local_blocks.shape[0]
    inner_bits = cross_blocks.shape[0]
    outer_bits = outer_blocks.shape[0]
    count, rows, columns = samples.shape
    width = columns // CHUNKS
    tgt_index = lax.axis_index("tgt")
    src_index = lax.axis_index("src")
    bits = [m for m in range(inner_bits)] + [m for m in range(outer_bits)]
    axes = ["tgt"] * inner_bits + ["src"] * outer_bits
    own_bits = [tgt_index >> m & 1 for m in range(inner_bits)] + [src_index >> m & 1 for m in range(outer_bits)]
    sources = [(cross_blocks, m, True) for m in range(inner_bits)] + [(outer_blocks, m, False) for m in range(outer_bits)]
    n_cross = len(bits)

    def scalars(first, second):
        return jnp.stack([first, second, tgt_index]).astype(jnp.int32)

    def blocks_spec(index):
        array, level, grouped = sources[index]
        return level_block(array.shape, level, count, grouped)

    spread_t = prep_map(spread_maps)
    leaf_t = prep_map(leaf_maps)
    adjoint_weights = []
    for index in range(n_cross):
        array, level, grouped = sources[index]
        spec = level_block(array.shape, level, count, grouped)
        spec = pl.BlockSpec((1,) + spec.block_shape[1:], lambda i, sc, f=spec.index_map: f(i, sc))
        adjoint_weights.append(prep_adjoint(array, spec, scalars(own_bits[index], zero_of(tgt_index)),
                                            (bits[index],), count, True)[0])
    local_spec = pl.BlockSpec(local_blocks.shape, lambda i, sc: (0, 0, 0, 0))
    local_t = prep_adjoint(local_blocks, local_spec, scalars(zero_of(tgt_index), zero_of(tgt_index)),
                           tuple(range(levels_local)), count, False)

    block = jax.ShapeDtypeStruct((count, rows, width), jnp.bfloat16)
    half = jax.ShapeDtypeStruct((count // 2, rows, width), jnp.bfloat16)
    half_spec = whole(half.shape)
    zero = tgt_index * 0

    def in_order(leave, earlier):
        if earlier is None:
            return leave
        leave, _ = lax.optimization_barrier((leave, earlier))
        return leave

    fwd = []
    for chunk in range(CHUNKS):
        fwd.append(call(
            functools.partial(forward_local_kernel, count=count, levels=levels_local, next_bit=bits[0]),
            scalars(zero, own_bits[0]),
            [samples, leaf_maps, local_blocks],
            [column_block((count, rows, width), chunk), whole(leaf_maps.shape), whole(local_blocks.shape)],
            [half, half],
            [pltpu.VMEM(block.shape, jnp.bfloat16), pltpu.VMEM(block.shape, jnp.bfloat16)],
        ))
    top = n_cross - 1
    adj = []
    for chunk in range(CHUNKS):
        adj.append(call(
            functools.partial(adjoint_first_kernel, count=count, bit=bits[top]),
            scalars(own_bits[top], zero),
            [echoes, spread_t, adjoint_weights[top]],
            [column_block((count, rows, width), chunk), whole(spread_t.shape), whole(adjoint_weights[top].shape)],
            [half, half],
            [pltpu.VMEM(block.shape, jnp.bfloat16)],
        ))

    full = jax.ShapeDtypeStruct(samples.shape, jnp.bfloat16)
    image_field = None
    for step in range(n_cross):
        index = step
        bit, axis = bits[index], axes[index]
        last = index == n_cross - 1
        next_bit = 0 if last else bits[index + 1]
        earlier = None
        for chunk in range(CHUNKS):
            stay, leave = fwd[chunk]
            arrived = from_partner(in_order(leave, earlier), axis, bit)
            earlier = arrived
            inputs = [stay, arrived, sources[index][0]]
            specs = [half_spec, half_spec, blocks_spec(index)]
            if last:
                inputs.append(spread_maps)
                specs.append(whole(spread_maps.shape))
            kernel = functools.partial(forward_cross_kernel, count=count, bit=bit, next_bit=next_bit, last=last)
            if last:
                (image_field,) = into_columns(
                    kernel, scalars(own_bits[index], zero), inputs, specs,
                    [pltpu.VMEM(block.shape, jnp.bfloat16)], full, block, chunk, image_field)
            else:
                fwd[chunk] = tuple(call(
                    kernel,
                    scalars(own_bits[index], own_bits[index + 1]),
                    inputs,
                    specs,
                    [half, half],
                    [pltpu.VMEM(block.shape, jnp.bfloat16)],
                ))

        index = top - step
        earlier = None
        for chunk in range(CHUNKS):
            kept, leave = adj[chunk]
            arrived = from_partner(in_order(leave, earlier), axes[index], bits[index])
            earlier = arrived
            if index > 0:
                adj[chunk] = tuple(call(
                    functools.partial(adjoint_cross_kernel, count=count, bit=bits[index - 1], prev_bit=bits[index]),
                    scalars(own_bits[index - 1], own_bits[index]),
                    [kept, arrived, adjoint_weights[index - 1]],
                    [half_spec, half_spec, whole(adjoint_weights[index - 1].shape)],
                    [half, half],
                    [],
                ))
            else:
                adj[chunk] = (kept, arrived)

    aperture_field = None
    for chunk in range(CHUNKS):
        kept, arrived = adj[chunk]
        (aperture_field,) = into_columns(
            functools.partial(adjoint_local_kernel, count=count, levels=levels_local, prev_bit=bits[0]),
            scalars(zero, own_bits[0]),
            [kept, arrived, local_t, leaf_t],
            [half_spec, half_spec, whole(local_t.shape), whole(leaf_t.shape)],
            [pltpu.VMEM(block.shape, jnp.bfloat16), pltpu.VMEM(block.shape, jnp.bfloat16)],
            full, block, chunk, aperture_field)
    return (image_field, aperture_field)


def solution(mesh):
    return jax.shard_map(
        per_device,
        mesh=mesh,
        in_specs=(
            P(("src", "tgt"), None, None),
            P(("src", "tgt"), None, None),
            P(("src", "tgt"), None, None),
            P(None, ("src", "tgt"), None, None),
            P(None, "src", None, None),
            P(None, ("src", "tgt"), None, None),
            P(("src", "tgt"), None, None),
        ),
        out_specs=(P(("src", "tgt"), None, None), P(("src", "tgt"), None, None)),
        check_vma=False,
    )
```

```python
import functools

import jax
import jax.numpy as jnp
from jax import lax
from jax.experimental import pallas as pl
from jax.experimental.pallas import tpu as pltpu
from jax.sharding import PartitionSpec as P

CHUNKS = 2


def from_partner(x, axis, apart):
    return lax.ppermute(x, axis, [(i, i ^ 1 << apart) for i in range(lax.axis_size(axis))])


def expand(r, bit, j):
    return ((r >> bit) << (bit + 1)) | (j << bit) | (r & ((1 << bit) - 1))


def compress(p, bit):
    return ((p >> (bit + 1)) << bit) | (p & ((1 << bit) - 1))


def mm(w, x):
    return jnp.dot(w, x, preferred_element_type=jnp.float32).astype(jnp.bfloat16)


def mm_t(w, x):
    product = lax.dot_general(w, x, (((0,), (0,)), ((), ())), preferred_element_type=jnp.float32)
    return product.astype(jnp.bfloat16)


def embed_tile(stored):
    half = stored.shape[-1] // 2
    lane = lax.broadcasted_iota(jnp.int32, stored.shape, 1)
    top = jnp.where(lane < half, stored, -stored)
    bottom = pltpu.roll(stored, half, 1)
    return jnp.concatenate([top, bottom], axis=0)


def block_pair(stored, own):
    width = stored.shape[-1] // 2
    first = embed_tile(stored[:, :width])
    second = embed_tile(stored[:, width:])
    if isinstance(own, int) and own == 0:
        return first, second
    return jnp.where(own == 0, first, second), jnp.where(own == 0, second, first)


def forward_weight(stored, own):
    first, second = block_pair(stored, own)
    return jnp.concatenate([first, second], axis=1)


def write_split(value_of, count, bit, own, stay_ref, leave_ref):
    for p in range(count):
        r = compress(p, bit)
        here = ((p >> bit) & 1) == own

        @pl.when(here)
        def _():
            stay_ref[r] = value_of(p)

        @pl.when(jnp.logical_not(here))
        def _():
            leave_ref[r] = value_of(p)


def read_split(kept_ref, arrived_ref, bit, own):
    def value_of(p):
        r = compress(p, bit)
        return jnp.where(((p >> bit) & 1) == own, kept_ref[r], arrived_ref[r])

    return value_of


def adjoint_pair(value_of, blocks_ref, bit, r, own):
    lower, upper = expand(r, bit, 0), expand(r, bit, 1)
    stacked = jnp.concatenate([value_of(lower), value_of(upper)], axis=0)
    first_lower, second_lower = block_pair(blocks_ref[lower], own)
    first_upper, second_upper = block_pair(blocks_ref[upper], own)
    kept = mm_t(jnp.concatenate([first_lower, first_upper], axis=0), stacked)
    leave = mm_t(jnp.concatenate([second_lower, second_upper], axis=0), stacked)
    return kept, leave


def forward_local_kernel(sc_ref, samples_ref, leaf_ref, local_ref, stay_ref, leave_ref, buf_a, buf_b,
                         *, count, levels, next_bit):
    for p in range(count):
        buf_a[p] = mm(embed_tile(leaf_ref[p]), samples_ref[p])
    src, dst = buf_a, buf_b
    for level in range(levels):
        for r in range(count // 2):
            p0, p1 = expand(r, level, 0), expand(r, level, 1)
            stacked = jnp.concatenate([src[p0], src[p1]], axis=0)
            dst[p0] = mm(forward_weight(local_ref[level, p0], 0), stacked)
            dst[p1] = mm(forward_weight(local_ref[level, p1], 0), stacked)
        src, dst = dst, src
    write_split(lambda p: src[p], count, next_bit, sc_ref[1], stay_ref, leave_ref)


def forward_cross_kernel(sc_ref, kept_ref, arrived_ref, blocks_ref, *rest, count, bit, next_bit, last, prior=False):
    if last:
        spread_ref, out_ref, buf = (rest[0],) + rest[1 + prior:]
    else:
        stay_ref, leave_ref, buf = rest
    own = sc_ref[0]
    for r in range(count // 2):
        stacked = jnp.concatenate([kept_ref[r], arrived_ref[r]], axis=0)
        for j in range(2):
            p = expand(r, bit, j)
            buf[p] = mm(forward_weight(blocks_ref[p], own), stacked)
    if last:
        for p in range(count):
            out_ref[p] = mm(embed_tile(spread_ref[p]), buf[p])
    else:
        write_split(lambda p: buf[p], count, next_bit, sc_ref[1], stay_ref, leave_ref)


def adjoint_first_kernel(sc_ref, echoes_ref, spread_ref, blocks_ref, kept_ref, leave_ref, buf, *, count, bit):
    for p in range(count):
        buf[p] = mm_t(embed_tile(spread_ref[p]), echoes_ref[p])
    own = sc_ref[0]
    for r in range(count // 2):
        kept_ref[r], leave_ref[r] = adjoint_pair(lambda p: buf[p], blocks_ref, bit, r, own)


def adjoint_cross_kernel(sc_ref, prev_kept_ref, prev_arrived_ref, blocks_ref, kept_ref, leave_ref,
                         *, count, bit, prev_bit):
    value_of = read_split(prev_kept_ref, prev_arrived_ref, prev_bit, sc_ref[1])
    own = sc_ref[0]
    for r in range(count // 2):
        kept_ref[r], leave_ref[r] = adjoint_pair(value_of, blocks_ref, bit, r, own)


def adjoint_local_kernel(sc_ref, prev_kept_ref, prev_arrived_ref, local_ref, leaf_ref, *rest,
                         count, levels, prev_bit, prior=False):
    out_ref, buf_a, buf_b = rest[prior:]
    value_of = read_split(prev_kept_ref, prev_arrived_ref, prev_bit, sc_ref[1])
    for p in range(count):
        buf_a[p] = value_of(p)
    src, dst = buf_a, buf_b
    for level in reversed(range(levels)):
        for r in range(count // 2):
            first, second = adjoint_pair(lambda p: src[p], local_ref.at[level], level, r, 0)
            dst[expand(r, level, 0)] = first
            dst[expand(r, level, 1)] = second
        src, dst = dst, src
    for p in range(count):
        out_ref[p] = mm_t(embed_tile(leaf_ref[p]), src[p])


def whole(shape):
    return ("whole", tuple(shape), None)


def column_block(shape, chunk):
    return ("cols", tuple(shape), chunk)


def level_block(shape, level, count, grouped):
    return ("level", (count,) + tuple(shape[2:]), (level, count, grouped))


def out_spec(shape, chunk=None):
    if chunk is None:
        return pl.BlockSpec(shape, lambda i, sc, n=len(shape): (0,) * n)
    return pl.BlockSpec(shape, lambda i, sc, c=chunk: (0, 0, c))


def call(kernel, scalars, inputs, in_specs, out_shapes, scratch, out_specs=None, aliases=None):
    n_in, n_out, n_scratch = len(inputs), len(out_shapes), len(scratch)
    copies = [i for i, spec in enumerate(in_specs) if spec[0] != "any"]

    def wrapped(sc_ref, *refs):
        ins, outs = refs[:n_in], refs[n_in:n_in + n_out]
        user = refs[n_in + n_out:n_in + n_out + n_scratch]
        bufs, sem = refs[n_in + n_out + n_scratch:-1], refs[-1]
        views = list(ins)
        started = []
        for k, i in enumerate(copies):
            kind, shape, arg = in_specs[i]
            source = ins[i]
            if kind == "cols":
                source = source.at[:, :, pl.ds(arg * shape[2], shape[2])]
            elif kind == "level":
                level, count, grouped = arg
                source = source.at[level, pl.ds(sc_ref[2] * count if grouped else 0, count)]
            copy = pltpu.make_async_copy(source, bufs[k], sem.at[k])
            copy.start()
            started.append(copy)
            views[i] = bufs[k]
        for copy in started:
            copy.wait()
        kernel(sc_ref, *views, *outs, *user)

    grid_spec = pltpu.PrefetchScalarGridSpec(
        num_scalar_prefetch=1,
        grid=(1,),
        in_specs=[pl.BlockSpec(memory_space=pltpu.HBM)] * n_in,
        out_specs=out_specs or [out_spec(s.shape) for s in out_shapes],
        scratch_shapes=list(scratch) + [pltpu.VMEM(in_specs[i][1], jnp.bfloat16) for i in copies]
        + [pltpu.SemaphoreType.DMA((len(copies),))],
    )
    return pl.pallas_call(
        wrapped,
        grid_spec=grid_spec,
        out_shape=out_shapes,
        input_output_aliases=aliases or {},
        compiler_params=pltpu.CompilerParams(vmem_limit_bytes=48 * 1024 * 1024),
    )(scalars, *inputs)


def into_columns(kernel, scalars, inputs, in_specs, scratch, full, part, chunk, prior):
    if prior is None:
        return call(kernel, scalars, inputs, in_specs, [full], scratch,
                    out_specs=[out_spec(part.shape, chunk)])
    return call(functools.partial(kernel, prior=True), scalars, inputs[:len(in_specs)] + [prior],
                in_specs + [("any", None, None)], [full], scratch,
                out_specs=[out_spec(part.shape, chunk)], aliases={1 + len(in_specs): 0})


def per_device(samples, echoes, leaf_maps, local_blocks, cross_blocks, outer_blocks, spread_maps):
    levels_local = local_blocks.shape[0]
    inner_bits = cross_blocks.shape[0]
    outer_bits = outer_blocks.shape[0]
    count, rows, columns = samples.shape
    width = columns // CHUNKS
    tgt_index = lax.axis_index("tgt")
    src_index = lax.axis_index("src")
    bits = [m for m in range(inner_bits)] + [m for m in range(outer_bits)]
    axes = ["tgt"] * inner_bits + ["src"] * outer_bits
    own_bits = [tgt_index >> m & 1 for m in range(inner_bits)] + [src_index >> m & 1 for m in range(outer_bits)]
    sources = [(cross_blocks, m, True) for m in range(inner_bits)] + [(outer_blocks, m, False) for m in range(outer_bits)]
    n_cross = len(bits)

    def scalars(first, second):
        return jnp.stack([first, second, tgt_index]).astype(jnp.int32)

    def blocks_spec(index):
        array, level, grouped = sources[index]
        return level_block(array.shape, level, count, grouped)

    block = jax.ShapeDtypeStruct((count, rows, width), jnp.bfloat16)
    half = jax.ShapeDtypeStruct((count // 2, rows, width), jnp.bfloat16)
    half_spec = whole(half.shape)
    zero = tgt_index * 0

    def in_order(leave, earlier):
        if earlier is None:
            return leave
        leave, _ = lax.optimization_barrier((leave, earlier))
        return leave

    fwd = []
    for chunk in range(CHUNKS):
        fwd.append(call(
            functools.partial(forward_local_kernel, count=count, levels=levels_local, next_bit=bits[0]),
            scalars(zero, own_bits[0]),
            [samples, leaf_maps, local_blocks],
            [column_block((count, rows, width), chunk), whole(leaf_maps.shape), whole(local_blocks.shape)],
            [half, half],
            [pltpu.VMEM(block.shape, jnp.bfloat16), pltpu.VMEM(block.shape, jnp.bfloat16)],
        ))
    top = n_cross - 1
    adj = []
    for chunk in range(CHUNKS):
        adj.append(call(
            functools.partial(adjoint_first_kernel, count=count, bit=bits[top]),
            scalars(own_bits[top], zero),
            [echoes, spread_maps, sources[top][0]],
            [column_block((count, rows, width), chunk), whole(spread_maps.shape), blocks_spec(top)],
            [half, half],
            [pltpu.VMEM(block.shape, jnp.bfloat16)],
        ))

    full = jax.ShapeDtypeStruct(samples.shape, jnp.bfloat16)
    image_field = None
    for step in range(n_cross):
        index = step
        bit, axis = bits[index], axes[index]
        last = index == n_cross - 1
        next_bit = 0 if last else bits[index + 1]
        earlier = None
        for chunk in range(CHUNKS):
            stay, leave = fwd[chunk]
            arrived = from_partner(in_order(leave, earlier), axis, bit)
            earlier = arrived
            inputs = [stay, arrived, sources[index][0]]
            specs = [half_spec, half_spec, blocks_spec(index)]
            if last:
                inputs.append(spread_maps)
                specs.append(whole(spread_maps.shape))
            kernel = functools.partial(forward_cross_kernel, count=count, bit=bit, next_bit=next_bit, last=last)
            if last:
                (image_field,) = into_columns(
                    kernel, scalars(own_bits[index], zero), inputs, specs,
                    [pltpu.VMEM(block.shape, jnp.bfloat16)], full, block, chunk, image_field)
            else:
                fwd[chunk] = tuple(call(
                    kernel,
                    scalars(own_bits[index], own_bits[index + 1]),
                    inputs,
                    specs,
                    [half, half],
                    [pltpu.VMEM(block.shape, jnp.bfloat16)],
                ))

        index = top - step
        earlier = None
        for chunk in range(CHUNKS):
            kept, leave = adj[chunk]
            arrived = from_partner(in_order(leave, earlier), axes[index], bits[index])
            earlier = arrived
            if index > 0:
                adj[chunk] = tuple(call(
                    functools.partial(adjoint_cross_kernel, count=count, bit=bits[index - 1], prev_bit=bits[index]),
                    scalars(own_bits[index - 1], own_bits[index]),
                    [kept, arrived, sources[index - 1][0]],
                    [half_spec, half_spec, blocks_spec(index - 1)],
                    [half, half],
                    [],
                ))
            else:
                adj[chunk] = (kept, arrived)

    aperture_field = None
    for chunk in range(CHUNKS):
        kept, arrived = adj[chunk]
        (aperture_field,) = into_columns(
            functools.partial(adjoint_local_kernel, count=count, levels=levels_local, prev_bit=bits[0]),
            scalars(zero, own_bits[0]),
            [kept, arrived, local_blocks, leaf_maps],
            [half_spec, half_spec, whole(local_blocks.shape), whole(leaf_maps.shape)],
            [pltpu.VMEM(block.shape, jnp.bfloat16), pltpu.VMEM(block.shape, jnp.bfloat16)],
            full, block, chunk, aperture_field)
    return (image_field, aperture_field)


def solution(mesh):
    return jax.shard_map(
        per_device,
        mesh=mesh,
        in_specs=(
            P(("src", "tgt"), None, None),
            P(("src", "tgt"), None, None),
            P(("src", "tgt"), None, None),
            P(None, ("src", "tgt"), None, None),
            P(None, "src", None, None),
            P(None, ("src", "tgt"), None, None),
            P(("src", "tgt"), None, None),
        ),
        out_specs=(P(("src", "tgt"), None, None), P(("src", "tgt"), None, None)),
        check_vma=False,
    )
```

```python
import functools

import jax
import jax.numpy as jnp
from jax import lax
from jax.experimental import pallas as pl
from jax.experimental.pallas import tpu as pltpu
from jax.sharding import PartitionSpec as P

CHUNKS = 2


def from_partner(x, axis, apart):
    return lax.ppermute(x, axis, [(i, i ^ 1 << apart) for i in range(lax.axis_size(axis))])


def expand(r, bit, j):
    return ((r >> bit) << (bit + 1)) | (j << bit) | (r & ((1 << bit) - 1))


def compress(p, bit):
    return ((p >> (bit + 1)) << bit) | (p & ((1 << bit) - 1))


def mm(w, x):
    return jnp.dot(w, x, preferred_element_type=jnp.float32).astype(jnp.bfloat16)


def mm_t(w, x):
    product = lax.dot_general(w, x, (((0,), (0,)), ((), ())), preferred_element_type=jnp.float32)
    return product.astype(jnp.bfloat16)


def embed_tile(stored):
    half = stored.shape[-1] // 2
    lane = lax.broadcasted_iota(jnp.int32, stored.shape, 1)
    top = jnp.where(lane < half, stored, -stored)
    bottom = pltpu.roll(stored, half, 1)
    return jnp.concatenate([top, bottom], axis=0)


def block_pair(stored, own):
    width = stored.shape[-1] // 2
    first = embed_tile(stored[:, :width])
    second = embed_tile(stored[:, width:])
    if isinstance(own, int) and own == 0:
        return first, second
    return jnp.where(own == 0, first, second), jnp.where(own == 0, second, first)


def forward_weight(stored, own):
    first, second = block_pair(stored, own)
    return jnp.concatenate([first, second], axis=1)


def write_split(value_of, count, bit, own, stay_ref, leave_ref):
    for p in range(count):
        r = compress(p, bit)
        here = ((p >> bit) & 1) == own

        @pl.when(here)
        def _():
            stay_ref[r] = value_of(p)

        @pl.when(jnp.logical_not(here))
        def _():
            leave_ref[r] = value_of(p)


def read_split(kept_ref, arrived_ref, bit, own):
    def value_of(p):
        r = compress(p, bit)
        return jnp.where(((p >> bit) & 1) == own, kept_ref[r], arrived_ref[r])

    return value_of


def adjoint_pair(value_of, blocks_ref, bit, r, own):
    lower, upper = expand(r, bit, 0), expand(r, bit, 1)
    stacked = jnp.concatenate([value_of(lower), value_of(upper)], axis=0)
    first_lower, second_lower = block_pair(blocks_ref[lower], own)
    first_upper, second_upper = block_pair(blocks_ref[upper], own)
    kept = mm_t(jnp.concatenate([first_lower, first_upper], axis=0), stacked)
    leave = mm_t(jnp.concatenate([second_lower, second_upper], axis=0), stacked)
    return kept, leave


def forward_local_kernel(sc_ref, samples_ref, leaf_ref, local_ref, stay_ref, leave_ref, buf_a, buf_b,
                         *, count, levels, next_bit):
    for p in range(count):
        buf_a[p] = mm(embed_tile(leaf_ref[p]), samples_ref[p])
    src, dst = buf_a, buf_b
    for level in range(levels):
        for r in range(count // 2):
            p0, p1 = expand(r, level, 0), expand(r, level, 1)
            stacked = jnp.concatenate([src[p0], src[p1]], axis=0)
            dst[p0] = mm(forward_weight(local_ref[level, p0], 0), stacked)
            dst[p1] = mm(forward_weight(local_ref[level, p1], 0), stacked)
        src, dst = dst, src
    write_split(lambda p: src[p], count, next_bit, sc_ref[1], stay_ref, leave_ref)


def forward_cross_kernel(sc_ref, kept_ref, arrived_ref, blocks_ref, *rest, count, bit, next_bit, last, prior=False):
    if last:
        spread_ref, out_ref, buf = (rest[0],) + rest[1 + prior:]
    else:
        stay_ref, leave_ref, buf = rest
    own = sc_ref[0]
    for r in range(count // 2):
        stacked = jnp.concatenate([kept_ref[r], arrived_ref[r]], axis=0)
        for j in range(2):
            p = expand(r, bit, j)
            buf[p] = mm(forward_weight(blocks_ref[p], own), stacked)
    if last:
        for p in range(count):
            out_ref[p] = mm(embed_tile(spread_ref[p]), buf[p])
    else:
        write_split(lambda p: buf[p], count, next_bit, sc_ref[1], stay_ref, leave_ref)


def adjoint_first_kernel(sc_ref, echoes_ref, spread_ref, blocks_ref, kept_ref, leave_ref, buf, *, count, bit):
    for p in range(count):
        buf[p] = mm_t(embed_tile(spread_ref[p]), echoes_ref[p])
    own = sc_ref[0]
    for r in range(count // 2):
        kept_ref[r], leave_ref[r] = adjoint_pair(lambda p: buf[p], blocks_ref, bit, r, own)


def adjoint_cross_kernel(sc_ref, prev_kept_ref, prev_arrived_ref, blocks_ref, kept_ref, leave_ref,
                         *, count, bit, prev_bit):
    value_of = read_split(prev_kept_ref, prev_arrived_ref, prev_bit, sc_ref[1])
    own = sc_ref[0]
    for r in range(count // 2):
        kept_ref[r], leave_ref[r] = adjoint_pair(value_of, blocks_ref, bit, r, own)


def adjoint_local_kernel(sc_ref, prev_kept_ref, prev_arrived_ref, local_ref, leaf_ref, *rest,
                         count, levels, prev_bit, prior=False):
    out_ref, buf_a, buf_b = rest[prior:]
    value_of = read_split(prev_kept_ref, prev_arrived_ref, prev_bit, sc_ref[1])
    for p in range(count):
        buf_a[p] = value_of(p)
    src, dst = buf_a, buf_b
    for level in reversed(range(levels)):
        for r in range(count // 2):
            first, second = adjoint_pair(lambda p: src[p], local_ref.at[level], level, r, 0)
            dst[expand(r, level, 0)] = first
            dst[expand(r, level, 1)] = second
        src, dst = dst, src
    for p in range(count):
        out_ref[p] = mm_t(embed_tile(leaf_ref[p]), src[p])


def whole(shape):
    return pl.BlockSpec(shape, lambda i, sc, n=len(shape): (0,) * n)


def column_block(shape, chunk):
    return pl.BlockSpec(shape, lambda i, sc, c=chunk: (0, 0, c))


def level_block(shape, level, count, grouped):
    if grouped:
        return pl.BlockSpec((None, count) + tuple(shape[2:]), lambda i, sc, v=level: (v, sc[2], 0, 0))
    return pl.BlockSpec((None, count) + tuple(shape[2:]), lambda i, sc, v=level: (v, 0, 0, 0))


def call(kernel, scalars, inputs, in_specs, out_shapes, scratch, out_specs=None, aliases=None):
    grid_spec = pltpu.PrefetchScalarGridSpec(
        num_scalar_prefetch=1,
        grid=(1,),
        in_specs=in_specs,
        out_specs=out_specs or [whole(s.shape) for s in out_shapes],
        scratch_shapes=scratch,
    )
    return pl.pallas_call(
        kernel,
        grid_spec=grid_spec,
        out_shape=out_shapes,
        input_output_aliases=aliases or {},
        compiler_params=pltpu.CompilerParams(vmem_limit_bytes=48 * 1024 * 1024),
    )(scalars, *inputs)


def into_columns(kernel, scalars, inputs, in_specs, scratch, full, part, chunk, prior):
    if prior is None:
        return call(kernel, scalars, inputs, in_specs, [full], scratch,
                    out_specs=[column_block(part.shape, chunk)])
    return call(functools.partial(kernel, prior=True), scalars, inputs[:len(in_specs)] + [prior],
                in_specs + [pl.BlockSpec(memory_space=pl.ANY)], [full], scratch,
                out_specs=[column_block(part.shape, chunk)], aliases={1 + len(in_specs): 0})


def task_order(chunks, stages):
    if chunks == 2 and stages == 6:
        names = "f00 a00 f10 a10 f01 f11 a01 f02 f03 f12 a02 f13 a11 f04 a03 a12 f14 a04 a13 f05 a05 a14 f15 a15"
        return [(n[0], int(n[1]), int(n[2])) for n in names.split()]
    return [(chain, chunk, step) for step in range(stages) for chain in "fa" for chunk in range(chunks)]


def per_device(samples, echoes, leaf_maps, local_blocks, cross_blocks, outer_blocks, spread_maps):
    levels_local = local_blocks.shape[0]
    inner_bits = cross_blocks.shape[0]
    outer_bits = outer_blocks.shape[0]
    count, rows, columns = samples.shape
    width = columns // CHUNKS
    tgt_index = lax.axis_index("tgt")
    src_index = lax.axis_index("src")
    bits = [m for m in range(inner_bits)] + [m for m in range(outer_bits)]
    axes = ["tgt"] * inner_bits + ["src"] * outer_bits
    own_bits = [tgt_index >> m & 1 for m in range(inner_bits)] + [src_index >> m & 1 for m in range(outer_bits)]
    sources = [(cross_blocks, m, True) for m in range(inner_bits)] + [(outer_blocks, m, False) for m in range(outer_bits)]
    n_cross = len(bits)

    def scalars(first, second):
        return jnp.stack([first, second, tgt_index]).astype(jnp.int32)

    def blocks_spec(index):
        array, level, grouped = sources[index]
        return level_block(array.shape, level, count, grouped)

    block = jax.ShapeDtypeStruct((count, rows, width), jnp.bfloat16)
    half = jax.ShapeDtypeStruct((count // 2, rows, width), jnp.bfloat16)
    half_spec = whole(half.shape)
    zero = tgt_index * 0

    def in_order(leave, earlier):
        if earlier is None:
            return leave
        leave, _ = lax.optimization_barrier((leave, earlier))
        return leave

    top = n_cross - 1
    stages = n_cross + 1
    state, arrivals, latest = {}, {}, {}
    outputs = {"f": None, "a": None}
    token = [None]

    def tied(x):
        if token[0] is None:
            return x
        x, _ = lax.optimization_barrier((x, token[0]))
        return x

    def send(chain, chunk, step, leave, axis, bit):
        arrived = from_partner(in_order(leave, latest.get((chain, step))), axis, bit)
        latest[(chain, step)] = arrived
        arrivals[(chain, chunk, step + 1)] = arrived

    def run(chain, chunk, step):
        if chain == "f" and step == 0:
            stay, leave = call(
                functools.partial(forward_local_kernel, count=count, levels=levels_local, next_bit=bits[0]),
                scalars(zero, own_bits[0]),
                [tied(samples), leaf_maps, local_blocks],
                [column_block((count, rows, width), chunk), whole(leaf_maps.shape), whole(local_blocks.shape)],
                [half, half],
                [pltpu.VMEM(block.shape, jnp.bfloat16), pltpu.VMEM(block.shape, jnp.bfloat16)],
            )
            state[("f", chunk)] = stay
            send("f", chunk, 0, leave, axes[0], bits[0])
            return stay
        if chain == "f":
            index = step - 1
            last = index == n_cross - 1
            kernel = functools.partial(forward_cross_kernel, count=count, bit=bits[index],
                                       next_bit=0 if last else bits[index + 1], last=last)
            inputs = [tied(state[("f", chunk)]), arrivals[("f", chunk, step)], sources[index][0]]
            specs = [half_spec, half_spec, blocks_spec(index)]
            if last:
                (outputs["f"],) = into_columns(
                    kernel, scalars(own_bits[index], zero), inputs + [spread_maps], specs + [whole(spread_maps.shape)],
                    [pltpu.VMEM(block.shape, jnp.bfloat16)], full, block, chunk, outputs["f"])
                return outputs["f"]
            stay, leave = call(kernel, scalars(own_bits[index], own_bits[index + 1]), inputs, specs, [half, half],
                               [pltpu.VMEM(block.shape, jnp.bfloat16)])
            state[("f", chunk)] = stay
            send("f", chunk, step, leave, axes[index + 1], bits[index + 1])
            return stay
        if step == 0:
            kept, leave = call(
                functools.partial(adjoint_first_kernel, count=count, bit=bits[top]),
                scalars(own_bits[top], zero),
                [tied(echoes), spread_maps, sources[top][0]],
                [column_block((count, rows, width), chunk), whole(spread_maps.shape), blocks_spec(top)],
                [half, half],
                [pltpu.VMEM(block.shape, jnp.bfloat16)],
            )
            state[("a", chunk)] = kept
            send("a", chunk, 0, leave, axes[top], bits[top])
            return kept
        index = top - step + 1
        if index > 0:
            kept, leave = call(
                functools.partial(adjoint_cross_kernel, count=count, bit=bits[index - 1], prev_bit=bits[index]),
                scalars(own_bits[index - 1], own_bits[index]),
                [tied(state[("a", chunk)]), arrivals[("a", chunk, step)], sources[index - 1][0]],
                [half_spec, half_spec, blocks_spec(index - 1)],
                [half, half],
                [],
            )
            state[("a", chunk)] = kept
            send("a", chunk, step, leave, axes[index - 1], bits[index - 1])
            return kept
        (outputs["a"],) = into_columns(
            functools.partial(adjoint_local_kernel, count=count, levels=levels_local, prev_bit=bits[0]),
            scalars(zero, own_bits[0]),
            [tied(state[("a", chunk)]), arrivals[("a", chunk, step)], local_blocks, leaf_maps],
            [half_spec, half_spec, whole(local_blocks.shape), whole(leaf_maps.shape)],
            [pltpu.VMEM(block.shape, jnp.bfloat16), pltpu.VMEM(block.shape, jnp.bfloat16)],
            full, block, chunk, outputs["a"])
        return outputs["a"]

    full = jax.ShapeDtypeStruct(samples.shape, jnp.bfloat16)
    for chain, chunk, step in task_order(CHUNKS, stages):
        token[0] = run(chain, chunk, step)
    image_field, aperture_field = outputs["f"], outputs["a"]
    return (image_field, aperture_field)


def solution(mesh):
    return jax.shard_map(
        per_device,
        mesh=mesh,
        in_specs=(
            P(("src", "tgt"), None, None),
            P(("src", "tgt"), None, None),
            P(("src", "tgt"), None, None),
            P(None, ("src", "tgt"), None, None),
            P(None, "src", None, None),
            P(None, ("src", "tgt"), None, None),
            P(("src", "tgt"), None, None),
        ),
        out_specs=(P(("src", "tgt"), None, None), P(("src", "tgt"), None, None)),
        check_vma=False,
    )
```

```python
import functools

import jax
import jax.numpy as jnp
from jax import lax
from jax.experimental import pallas as pl
from jax.experimental.pallas import tpu as pltpu
from jax.sharding import PartitionSpec as P

CHUNKS = 2


def from_partner(x, axis, apart):
    return lax.ppermute(x, axis, [(i, i ^ 1 << apart) for i in range(lax.axis_size(axis))])


def expand(r, bit, j):
    return ((r >> bit) << (bit + 1)) | (j << bit) | (r & ((1 << bit) - 1))


def compress(p, bit):
    return ((p >> (bit + 1)) << bit) | (p & ((1 << bit) - 1))


def mm(w, x):
    return jnp.dot(w, x, preferred_element_type=jnp.float32).astype(jnp.bfloat16)


def mm_t(w, x):
    product = lax.dot_general(w, x, (((0,), (0,)), ((), ())), preferred_element_type=jnp.float32)
    return product.astype(jnp.bfloat16)


def embed_tile(stored):
    half = stored.shape[-1] // 2
    lane = lax.broadcasted_iota(jnp.int32, stored.shape, 1)
    top = jnp.where(lane < half, stored, -stored)
    bottom = pltpu.roll(stored, half, 1)
    return jnp.concatenate([top, bottom], axis=0)


def block_pair(stored, own):
    width = stored.shape[-1] // 2
    first = embed_tile(stored[:, :width])
    second = embed_tile(stored[:, width:])
    if isinstance(own, int) and own == 0:
        return first, second
    return jnp.where(own == 0, first, second), jnp.where(own == 0, second, first)


def forward_weight(stored, own):
    first, second = block_pair(stored, own)
    return jnp.concatenate([first, second], axis=1)


def write_split(value_of, count, bit, own, stay_ref, leave_ref):
    for p in range(count):
        r = compress(p, bit)
        here = ((p >> bit) & 1) == own

        @pl.when(here)
        def _():
            stay_ref[r] = value_of(p)

        @pl.when(jnp.logical_not(here))
        def _():
            leave_ref[r] = value_of(p)


def read_split(kept_ref, arrived_ref, bit, own):
    def value_of(p):
        r = compress(p, bit)
        return jnp.where(((p >> bit) & 1) == own, kept_ref[r], arrived_ref[r])

    return value_of


def adjoint_pair(value_of, blocks_ref, bit, r, own):
    lower, upper = expand(r, bit, 0), expand(r, bit, 1)
    stacked = jnp.concatenate([value_of(lower), value_of(upper)], axis=0)
    first_lower, second_lower = block_pair(blocks_ref[lower], own)
    first_upper, second_upper = block_pair(blocks_ref[upper], own)
    kept = mm_t(jnp.concatenate([first_lower, first_upper], axis=0), stacked)
    leave = mm_t(jnp.concatenate([second_lower, second_upper], axis=0), stacked)
    return kept, leave


def forward_local_kernel(sc_ref, samples_ref, leaf_ref, local_ref, stay_ref, leave_ref, buf_a, buf_b,
                         *, count, levels, next_bit):
    for p in range(count):
        buf_a[p] = mm(embed_tile(leaf_ref[p]), samples_ref[p])
    src, dst = buf_a, buf_b
    for level in range(levels):
        for r in range(count // 2):
            p0, p1 = expand(r, level, 0), expand(r, level, 1)
            stacked = jnp.concatenate([src[p0], src[p1]], axis=0)
            dst[p0] = mm(forward_weight(local_ref[level, p0], 0), stacked)
            dst[p1] = mm(forward_weight(local_ref[level, p1], 0), stacked)
        src, dst = dst, src
    write_split(lambda p: src[p], count, next_bit, sc_ref[1], stay_ref, leave_ref)


def forward_cross_kernel(sc_ref, kept_ref, arrived_ref, blocks_ref, *rest, count, bit, next_bit, last, prior=False):
    if last:
        spread_ref, out_ref, buf = (rest[0],) + rest[1 + prior:]
    else:
        stay_ref, leave_ref, buf = rest
    own = sc_ref[0]
    for r in range(count // 2):
        stacked = jnp.concatenate([kept_ref[r], arrived_ref[r]], axis=0)
        for j in range(2):
            p = expand(r, bit, j)
            buf[p] = mm(forward_weight(blocks_ref[p], own), stacked)
    if last:
        for p in range(count):
            out_ref[p] = mm(embed_tile(spread_ref[p]), buf[p])
    else:
        write_split(lambda p: buf[p], count, next_bit, sc_ref[1], stay_ref, leave_ref)


def adjoint_first_kernel(sc_ref, echoes_ref, spread_ref, blocks_ref, kept_ref, leave_ref, buf, *, count, bit):
    for p in range(count):
        buf[p] = mm_t(embed_tile(spread_ref[p]), echoes_ref[p])
    own = sc_ref[0]
    for r in range(count // 2):
        kept_ref[r], leave_ref[r] = adjoint_pair(lambda p: buf[p], blocks_ref, bit, r, own)


def adjoint_cross_kernel(sc_ref, prev_kept_ref, prev_arrived_ref, blocks_ref, kept_ref, leave_ref,
                         *, count, bit, prev_bit):
    value_of = read_split(prev_kept_ref, prev_arrived_ref, prev_bit, sc_ref[1])
    own = sc_ref[0]
    for r in range(count // 2):
        kept_ref[r], leave_ref[r] = adjoint_pair(value_of, blocks_ref, bit, r, own)


def adjoint_local_kernel(sc_ref, prev_kept_ref, prev_arrived_ref, local_ref, leaf_ref, *rest,
                         count, levels, prev_bit, prior=False):
    out_ref, buf_a, buf_b = rest[prior:]
    value_of = read_split(prev_kept_ref, prev_arrived_ref, prev_bit, sc_ref[1])
    for p in range(count):
        buf_a[p] = value_of(p)
    src, dst = buf_a, buf_b
    for level in reversed(range(levels)):
        for r in range(count // 2):
            first, second = adjoint_pair(lambda p: src[p], local_ref.at[level], level, r, 0)
            dst[expand(r, level, 0)] = first
            dst[expand(r, level, 1)] = second
        src, dst = dst, src
    for p in range(count):
        out_ref[p] = mm_t(embed_tile(leaf_ref[p]), src[p])


def whole(shape):
    return pl.BlockSpec(shape, lambda i, sc, n=len(shape): (0,) * n)


def column_block(shape, chunk):
    return pl.BlockSpec(shape, lambda i, sc, c=chunk: (0, 0, c))


def level_block(shape, level, count, grouped):
    if grouped:
        return pl.BlockSpec((None, count) + tuple(shape[2:]), lambda i, sc, v=level: (v, sc[2], 0, 0))
    return pl.BlockSpec((None, count) + tuple(shape[2:]), lambda i, sc, v=level: (v, 0, 0, 0))


def call(kernel, scalars, inputs, in_specs, out_shapes, scratch, out_specs=None, aliases=None):
    grid_spec = pltpu.PrefetchScalarGridSpec(
        num_scalar_prefetch=1,
        grid=(1,),
        in_specs=in_specs,
        out_specs=out_specs or [whole(s.shape) for s in out_shapes],
        scratch_shapes=scratch,
    )
    return pl.pallas_call(
        kernel,
        grid_spec=grid_spec,
        out_shape=out_shapes,
        input_output_aliases=aliases or {},
        compiler_params=pltpu.CompilerParams(vmem_limit_bytes=48 * 1024 * 1024),
    )(scalars, *inputs)


def into_columns(kernel, scalars, inputs, in_specs, scratch, full, part, chunk, prior):
    if prior is None:
        return call(kernel, scalars, inputs, in_specs, [full], scratch,
                    out_specs=[column_block(part.shape, chunk)])
    return call(functools.partial(kernel, prior=True), scalars, inputs[:len(in_specs)] + [prior],
                in_specs + [pl.BlockSpec(memory_space=pl.ANY)], [full], scratch,
                out_specs=[column_block(part.shape, chunk)], aliases={1 + len(in_specs): 0})


def per_device(samples, echoes, leaf_maps, local_blocks, cross_blocks, outer_blocks, spread_maps):
    levels_local = local_blocks.shape[0]
    inner_bits = cross_blocks.shape[0]
    outer_bits = outer_blocks.shape[0]
    count, rows, columns = samples.shape
    width = columns // CHUNKS
    tgt_index = lax.axis_index("tgt")
    src_index = lax.axis_index("src")
    bits = [m for m in range(inner_bits)] + [m for m in range(outer_bits)]
    axes = ["tgt"] * inner_bits + ["src"] * outer_bits
    own_bits = [tgt_index >> m & 1 for m in range(inner_bits)] + [src_index >> m & 1 for m in range(outer_bits)]
    sources = [(cross_blocks, m, True) for m in range(inner_bits)] + [(outer_blocks, m, False) for m in range(outer_bits)]
    n_cross = len(bits)

    def scalars(first, second):
        return jnp.stack([first, second, tgt_index]).astype(jnp.int32)

    def blocks_spec(index):
        array, level, grouped = sources[index]
        return level_block(array.shape, level, count, grouped)

    block = jax.ShapeDtypeStruct((count, rows, width), jnp.bfloat16)
    half = jax.ShapeDtypeStruct((count // 2, rows, width), jnp.bfloat16)
    half_spec = whole(half.shape)
    zero = tgt_index * 0

    def in_order(leave, earlier):
        if earlier is None:
            return leave
        leave, _ = lax.optimization_barrier((leave, earlier))
        return leave

    top = n_cross - 1
    adj = []
    for chunk in range(CHUNKS):
        adj.append(call(
            functools.partial(adjoint_first_kernel, count=count, bit=bits[top]),
            scalars(own_bits[top], zero),
            [echoes, spread_maps, sources[top][0]],
            [column_block((count, rows, width), chunk), whole(spread_maps.shape), blocks_spec(top)],
            [half, half],
            [pltpu.VMEM(block.shape, jnp.bfloat16)],
        ))

    fwd = []
    for chunk in range(CHUNKS):
        fwd.append(call(
            functools.partial(forward_local_kernel, count=count, levels=levels_local, next_bit=bits[0]),
            scalars(zero, own_bits[0]),
            [lax.optimization_barrier((samples, adj[chunk][0]))[0], leaf_maps, local_blocks],
            [column_block((count, rows, width), chunk), whole(leaf_maps.shape), whole(local_blocks.shape)],
            [half, half],
            [pltpu.VMEM(block.shape, jnp.bfloat16), pltpu.VMEM(block.shape, jnp.bfloat16)],
        ))
    full = jax.ShapeDtypeStruct(samples.shape, jnp.bfloat16)
    image_field = None
    for step in range(n_cross):
        index = step
        bit, axis = bits[index], axes[index]
        last = index == n_cross - 1
        next_bit = 0 if last else bits[index + 1]
        earlier = None
        for chunk in range(CHUNKS):
            stay, leave = fwd[chunk]
            arrived = from_partner(in_order(leave, earlier), axis, bit)
            earlier = arrived
            inputs = [stay, arrived, sources[index][0]]
            specs = [half_spec, half_spec, blocks_spec(index)]
            if last:
                inputs.append(spread_maps)
                specs.append(whole(spread_maps.shape))
            kernel = functools.partial(forward_cross_kernel, count=count, bit=bit, next_bit=next_bit, last=last)
            if last:
                (image_field,) = into_columns(
                    kernel, scalars(own_bits[index], zero), inputs, specs,
                    [pltpu.VMEM(block.shape, jnp.bfloat16)], full, block, chunk, image_field)
            else:
                fwd[chunk] = tuple(call(
                    kernel,
                    scalars(own_bits[index], own_bits[index + 1]),
                    inputs,
                    specs,
                    [half, half],
                    [pltpu.VMEM(block.shape, jnp.bfloat16)],
                ))

        index = top - step
        earlier = None
        for chunk in range(CHUNKS):
            kept, leave = adj[chunk]
            arrived = from_partner(in_order(leave, earlier), axes[index], bits[index])
            earlier = arrived
            if index > 0:
                adj[chunk] = tuple(call(
                    functools.partial(adjoint_cross_kernel, count=count, bit=bits[index - 1], prev_bit=bits[index]),
                    scalars(own_bits[index - 1], own_bits[index]),
                    [kept, arrived, sources[index - 1][0]],
                    [half_spec, half_spec, blocks_spec(index - 1)],
                    [half, half],
                    [],
                ))
            else:
                adj[chunk] = (kept, arrived)

    aperture_field = None
    for chunk in range(CHUNKS):
        kept, arrived = adj[chunk]
        (aperture_field,) = into_columns(
            functools.partial(adjoint_local_kernel, count=count, levels=levels_local, prev_bit=bits[0]),
            scalars(zero, own_bits[0]),
            [kept, arrived, local_blocks, leaf_maps],
            [half_spec, half_spec, whole(local_blocks.shape), whole(leaf_maps.shape)],
            [pltpu.VMEM(block.shape, jnp.bfloat16), pltpu.VMEM(block.shape, jnp.bfloat16)],
            full, block, chunk, aperture_field)
    return (image_field, aperture_field)


def solution(mesh):
    return jax.shard_map(
        per_device,
        mesh=mesh,
        in_specs=(
            P(("src", "tgt"), None, None),
            P(("src", "tgt"), None, None),
            P(("src", "tgt"), None, None),
            P(None, ("src", "tgt"), None, None),
            P(None, "src", None, None),
            P(None, ("src", "tgt"), None, None),
            P(("src", "tgt"), None, None),
        ),
        out_specs=(P(("src", "tgt"), None, None), P(("src", "tgt"), None, None)),
        check_vma=False,
    )
```

```python
import functools

import jax
import jax.numpy as jnp
from jax import lax
from jax.experimental import pallas as pl
from jax.experimental.pallas import tpu as pltpu
from jax.sharding import PartitionSpec as P

CHUNKS = 2


def from_partner(x, axis, apart):
    return lax.ppermute(x, axis, [(i, i ^ 1 << apart) for i in range(lax.axis_size(axis))])


def expand(r, bit, j):
    return ((r >> bit) << (bit + 1)) | (j << bit) | (r & ((1 << bit) - 1))


def compress(p, bit):
    return ((p >> (bit + 1)) << bit) | (p & ((1 << bit) - 1))


def mm(w, x):
    return jnp.dot(w, x, preferred_element_type=jnp.float32).astype(jnp.bfloat16)


def mm_t(w, x):
    product = lax.dot_general(w, x, (((0,), (0,)), ((), ())), preferred_element_type=jnp.float32)
    return product.astype(jnp.bfloat16)


def embed_tile(stored):
    half = stored.shape[-1] // 2
    lane = lax.broadcasted_iota(jnp.int32, stored.shape, 1)
    top = jnp.where(lane < half, stored, -stored)
    bottom = pltpu.roll(stored, half, 1)
    return jnp.concatenate([top, bottom], axis=0)


def block_pair(stored, own):
    width = stored.shape[-1] // 2
    first = embed_tile(stored[:, :width])
    second = embed_tile(stored[:, width:])
    if isinstance(own, int) and own == 0:
        return first, second
    return jnp.where(own == 0, first, second), jnp.where(own == 0, second, first)


def forward_weight(stored, own):
    first, second = block_pair(stored, own)
    return jnp.concatenate([first, second], axis=1)


def write_split(value_of, count, bit, own, stay_ref, leave_ref):
    for p in range(count):
        r = compress(p, bit)
        here = ((p >> bit) & 1) == own

        @pl.when(here)
        def _():
            stay_ref[r] = value_of(p)

        @pl.when(jnp.logical_not(here))
        def _():
            leave_ref[r] = value_of(p)


def read_split(kept_ref, arrived_ref, bit, own):
    def value_of(p):
        r = compress(p, bit)
        return jnp.where(((p >> bit) & 1) == own, kept_ref[r], arrived_ref[r])

    return value_of


def adjoint_pair(value_of, blocks_ref, bit, r, own):
    lower, upper = expand(r, bit, 0), expand(r, bit, 1)
    stacked = jnp.concatenate([value_of(lower), value_of(upper)], axis=0)
    first_lower, second_lower = block_pair(blocks_ref[lower], own)
    first_upper, second_upper = block_pair(blocks_ref[upper], own)
    kept = mm_t(jnp.concatenate([first_lower, first_upper], axis=0), stacked)
    leave = mm_t(jnp.concatenate([second_lower, second_upper], axis=0), stacked)
    return kept, leave


def forward_local_kernel(sc_ref, samples_ref, leaf_ref, local_ref, stay_ref, leave_ref, buf_a, buf_b,
                         *, count, levels, next_bit):
    for p in range(count):
        buf_a[p] = mm(embed_tile(leaf_ref[p]), samples_ref[p])
    src, dst = buf_a, buf_b
    for level in range(levels):
        for r in range(count // 2):
            p0, p1 = expand(r, level, 0), expand(r, level, 1)
            stacked = jnp.concatenate([src[p0], src[p1]], axis=0)
            dst[p0] = mm(forward_weight(local_ref[level, p0], 0), stacked)
            dst[p1] = mm(forward_weight(local_ref[level, p1], 0), stacked)
        src, dst = dst, src
    write_split(lambda p: src[p], count, next_bit, sc_ref[1], stay_ref, leave_ref)


def forward_cross_kernel(sc_ref, kept_ref, arrived_ref, blocks_ref, *rest, count, bit, next_bit, last, prior=False):
    if last:
        spread_ref, out_ref, buf = (rest[0],) + rest[1 + prior:]
    else:
        stay_ref, leave_ref, buf = rest
    own = sc_ref[0]
    for r in range(count // 2):
        stacked = jnp.concatenate([kept_ref[r], arrived_ref[r]], axis=0)
        for j in range(2):
            p = expand(r, bit, j)
            buf[p] = mm(forward_weight(blocks_ref[p], own), stacked)
    if last:
        for p in range(count):
            out_ref[p] = mm(embed_tile(spread_ref[p]), buf[p])
    else:
        write_split(lambda p: buf[p], count, next_bit, sc_ref[1], stay_ref, leave_ref)


def adjoint_first_kernel(sc_ref, echoes_ref, spread_ref, blocks_ref, kept_ref, leave_ref, buf, *, count, bit):
    for p in range(count):
        buf[p] = mm_t(embed_tile(spread_ref[p]), echoes_ref[p])
    own = sc_ref[0]
    for r in range(count // 2):
        kept_ref[r], leave_ref[r] = adjoint_pair(lambda p: buf[p], blocks_ref, bit, r, own)


def adjoint_cross_kernel(sc_ref, prev_kept_ref, prev_arrived_ref, blocks_ref, kept_ref, leave_ref,
                         *, count, bit, prev_bit):
    value_of = read_split(prev_kept_ref, prev_arrived_ref, prev_bit, sc_ref[1])
    own = sc_ref[0]
    for r in range(count // 2):
        kept_ref[r], leave_ref[r] = adjoint_pair(value_of, blocks_ref, bit, r, own)


def adjoint_local_kernel(sc_ref, prev_kept_ref, prev_arrived_ref, local_ref, leaf_ref, *rest,
                         count, levels, prev_bit, prior=False):
    out_ref, buf_a, buf_b = rest[prior:]
    value_of = read_split(prev_kept_ref, prev_arrived_ref, prev_bit, sc_ref[1])
    for p in range(count):
        buf_a[p] = value_of(p)
    src, dst = buf_a, buf_b
    for level in reversed(range(levels)):
        for r in range(count // 2):
            first, second = adjoint_pair(lambda p: src[p], local_ref.at[level], level, r, 0)
            dst[expand(r, level, 0)] = first
            dst[expand(r, level, 1)] = second
        src, dst = dst, src
    for p in range(count):
        out_ref[p] = mm_t(embed_tile(leaf_ref[p]), src[p])


def whole(shape):
    return pl.BlockSpec(shape, lambda i, sc, n=len(shape): (0,) * n)


def column_block(shape, chunk):
    return pl.BlockSpec(shape, lambda i, sc, c=chunk: (0, 0, c))


def level_block(shape, level, count, grouped):
    if grouped:
        return pl.BlockSpec((None, count) + tuple(shape[2:]), lambda i, sc, v=level: (v, sc[2], 0, 0))
    return pl.BlockSpec((None, count) + tuple(shape[2:]), lambda i, sc, v=level: (v, 0, 0, 0))


def call(kernel, scalars, inputs, in_specs, out_shapes, scratch, out_specs=None, aliases=None):
    grid_spec = pltpu.PrefetchScalarGridSpec(
        num_scalar_prefetch=1,
        grid=(1,),
        in_specs=in_specs,
        out_specs=out_specs or [whole(s.shape) for s in out_shapes],
        scratch_shapes=scratch,
    )
    return pl.pallas_call(
        kernel,
        grid_spec=grid_spec,
        out_shape=out_shapes,
        input_output_aliases=aliases or {},
        compiler_params=pltpu.CompilerParams(vmem_limit_bytes=48 * 1024 * 1024),
    )(scalars, *inputs)


def into_columns(kernel, scalars, inputs, in_specs, scratch, full, part, chunk, prior):
    if prior is None:
        return call(kernel, scalars, inputs, in_specs, [full], scratch,
                    out_specs=[column_block(part.shape, chunk)])
    return call(functools.partial(kernel, prior=True), scalars, inputs[:len(in_specs)] + [prior],
                in_specs + [pl.BlockSpec(memory_space=pl.ANY)], [full], scratch,
                out_specs=[column_block(part.shape, chunk)], aliases={1 + len(in_specs): 0})


def per_device(samples, echoes, leaf_maps, local_blocks, cross_blocks, outer_blocks, spread_maps):
    levels_local = local_blocks.shape[0]
    inner_bits = cross_blocks.shape[0]
    outer_bits = outer_blocks.shape[0]
    count, rows, columns = samples.shape
    width = columns // CHUNKS
    tgt_index = lax.axis_index("tgt")
    src_index = lax.axis_index("src")
    bits = [m for m in range(inner_bits)] + [m for m in range(outer_bits)]
    axes = ["tgt"] * inner_bits + ["src"] * outer_bits
    own_bits = [tgt_index >> m & 1 for m in range(inner_bits)] + [src_index >> m & 1 for m in range(outer_bits)]
    sources = [(cross_blocks, m, True) for m in range(inner_bits)] + [(outer_blocks, m, False) for m in range(outer_bits)]
    n_cross = len(bits)

    def scalars(first, second):
        return jnp.stack([first, second, tgt_index]).astype(jnp.int32)

    def blocks_spec(index):
        array, level, grouped = sources[index]
        return level_block(array.shape, level, count, grouped)

    block = jax.ShapeDtypeStruct((count, rows, width), jnp.bfloat16)
    half = jax.ShapeDtypeStruct((count // 2, rows, width), jnp.bfloat16)
    half_spec = whole(half.shape)
    zero = tgt_index * 0

    def in_order(leave, earlier):
        if earlier is None:
            return leave
        leave, _ = lax.optimization_barrier((leave, earlier))
        return leave

    fwd = []
    for chunk in range(CHUNKS):
        fwd.append(call(
            functools.partial(forward_local_kernel, count=count, levels=levels_local, next_bit=bits[0]),
            scalars(zero, own_bits[0]),
            [samples, leaf_maps, local_blocks],
            [column_block((count, rows, width), chunk), whole(leaf_maps.shape), whole(local_blocks.shape)],
            [half, half],
            [pltpu.VMEM(block.shape, jnp.bfloat16), pltpu.VMEM(block.shape, jnp.bfloat16)],
        ))
    top = n_cross - 1
    adj = []
    for chunk in range(CHUNKS):
        adj.append(call(
            functools.partial(adjoint_first_kernel, count=count, bit=bits[top]),
            scalars(own_bits[top], zero),
            [echoes, spread_maps, sources[top][0]],
            [column_block((count, rows, width), chunk), whole(spread_maps.shape), blocks_spec(top)],
            [half, half],
            [pltpu.VMEM(block.shape, jnp.bfloat16)],
        ))

    full = jax.ShapeDtypeStruct(samples.shape, jnp.bfloat16)
    image_field = None
    for step in range(n_cross):
        index = step
        bit, axis = bits[index], axes[index]
        last = index == n_cross - 1
        next_bit = 0 if last else bits[index + 1]
        earlier = None
        for chunk in range(CHUNKS):
            stay, leave = fwd[chunk]
            arrived = from_partner(in_order(leave, earlier if axis == "src" and bit > 0 else None), axis, bit)
            earlier = arrived
            inputs = [stay, arrived, sources[index][0]]
            specs = [half_spec, half_spec, blocks_spec(index)]
            if last:
                inputs.append(spread_maps)
                specs.append(whole(spread_maps.shape))
            kernel = functools.partial(forward_cross_kernel, count=count, bit=bit, next_bit=next_bit, last=last)
            if last:
                (image_field,) = into_columns(
                    kernel, scalars(own_bits[index], zero), inputs, specs,
                    [pltpu.VMEM(block.shape, jnp.bfloat16)], full, block, chunk, image_field)
            else:
                fwd[chunk] = tuple(call(
                    kernel,
                    scalars(own_bits[index], own_bits[index + 1]),
                    inputs,
                    specs,
                    [half, half],
                    [pltpu.VMEM(block.shape, jnp.bfloat16)],
                ))

        index = top - step
        earlier = None
        for chunk in range(CHUNKS):
            kept, leave = adj[chunk]
            arrived = from_partner(in_order(leave, earlier if axes[index] == "src" and bits[index] > 0 else None),
                                   axes[index], bits[index])
            earlier = arrived
            if index > 0:
                adj[chunk] = tuple(call(
                    functools.partial(adjoint_cross_kernel, count=count, bit=bits[index - 1], prev_bit=bits[index]),
                    scalars(own_bits[index - 1], own_bits[index]),
                    [kept, arrived, sources[index - 1][0]],
                    [half_spec, half_spec, blocks_spec(index - 1)],
                    [half, half],
                    [],
                ))
            else:
                adj[chunk] = (kept, arrived)

    aperture_field = None
    for chunk in range(CHUNKS):
        kept, arrived = adj[chunk]
        (aperture_field,) = into_columns(
            functools.partial(adjoint_local_kernel, count=count, levels=levels_local, prev_bit=bits[0]),
            scalars(zero, own_bits[0]),
            [kept, arrived, local_blocks, leaf_maps],
            [half_spec, half_spec, whole(local_blocks.shape), whole(leaf_maps.shape)],
            [pltpu.VMEM(block.shape, jnp.bfloat16), pltpu.VMEM(block.shape, jnp.bfloat16)],
            full, block, chunk, aperture_field)
    return (image_field, aperture_field)


def solution(mesh):
    return jax.shard_map(
        per_device,
        mesh=mesh,
        in_specs=(
            P(("src", "tgt"), None, None),
            P(("src", "tgt"), None, None),
            P(("src", "tgt"), None, None),
            P(None, ("src", "tgt"), None, None),
            P(None, "src", None, None),
            P(None, ("src", "tgt"), None, None),
            P(("src", "tgt"), None, None),
        ),
        out_specs=(P(("src", "tgt"), None, None), P(("src", "tgt"), None, None)),
        check_vma=False,
    )
```

```python
import functools

import jax
import jax.numpy as jnp
from jax import lax
from jax.experimental import pallas as pl
from jax.experimental.pallas import tpu as pltpu
from jax.sharding import PartitionSpec as P

CHUNKS = 2


def from_partner(x, axis, apart):
    return lax.ppermute(x, axis, [(i, i ^ 1 << apart) for i in range(lax.axis_size(axis))])


def expand(r, bit, j):
    return ((r >> bit) << (bit + 1)) | (j << bit) | (r & ((1 << bit) - 1))


def compress(p, bit):
    return ((p >> (bit + 1)) << bit) | (p & ((1 << bit) - 1))


def mm(w, x):
    return jnp.dot(w, x, preferred_element_type=jnp.float32).astype(jnp.bfloat16)


def mm_t(w, x):
    product = lax.dot_general(w, x, (((0,), (0,)), ((), ())), preferred_element_type=jnp.float32)
    return product.astype(jnp.bfloat16)


def embed_tile(stored):
    half = stored.shape[-1] // 2
    lane = lax.broadcasted_iota(jnp.int32, stored.shape, 1)
    top = jnp.where(lane < half, stored, -stored)
    bottom = pltpu.roll(stored, half, 1)
    return jnp.concatenate([top, bottom], axis=0)


def block_pair(stored, own):
    width = stored.shape[-1] // 2
    first = embed_tile(stored[:, :width])
    second = embed_tile(stored[:, width:])
    if isinstance(own, int) and own == 0:
        return first, second
    return jnp.where(own == 0, first, second), jnp.where(own == 0, second, first)


def forward_weight(stored, own):
    first, second = block_pair(stored, own)
    return jnp.concatenate([first, second], axis=1)


def write_split(value_of, count, bit, own, stay_ref, leave_ref):
    for p in range(count):
        r = compress(p, bit)
        here = ((p >> bit) & 1) == own

        @pl.when(here)
        def _():
            stay_ref[r] = value_of(p)

        @pl.when(jnp.logical_not(here))
        def _():
            leave_ref[r] = value_of(p)


def read_split(kept_ref, arrived_ref, bit, own):
    def value_of(p):
        r = compress(p, bit)
        return jnp.where(((p >> bit) & 1) == own, kept_ref[r], arrived_ref[r])

    return value_of


def adjoint_pair(value_of, blocks_ref, bit, r, own):
    lower, upper = expand(r, bit, 0), expand(r, bit, 1)
    stacked = jnp.concatenate([value_of(lower), value_of(upper)], axis=0)
    first_lower, second_lower = block_pair(blocks_ref[lower], own)
    first_upper, second_upper = block_pair(blocks_ref[upper], own)
    kept = mm_t(jnp.concatenate([first_lower, first_upper], axis=0), stacked)
    leave = mm_t(jnp.concatenate([second_lower, second_upper], axis=0), stacked)
    return kept, leave


def forward_local_kernel(sc_ref, samples_ref, leaf_ref, local_ref, stay_ref, leave_ref, buf_a, buf_b,
                         *, count, levels, next_bit):
    for p in range(count):
        buf_a[p] = mm(embed_tile(leaf_ref[p]), samples_ref[p])
    src, dst = buf_a, buf_b
    for level in range(levels):
        for r in range(count // 2):
            p0, p1 = expand(r, level, 0), expand(r, level, 1)
            stacked = jnp.concatenate([src[p0], src[p1]], axis=0)
            dst[p0] = mm(forward_weight(local_ref[level, p0], 0), stacked)
            dst[p1] = mm(forward_weight(local_ref[level, p1], 0), stacked)
        src, dst = dst, src
    write_split(lambda p: src[p], count, next_bit, sc_ref[1], stay_ref, leave_ref)


def forward_cross_kernel(sc_ref, kept_ref, arrived_ref, blocks_ref, *rest, count, bit, next_bit, last, prior=False):
    if last:
        spread_ref, out_ref, buf = (rest[0],) + rest[1 + prior:]
    else:
        stay_ref, leave_ref, buf = rest
    own = sc_ref[0]
    for r in range(count // 2):
        stacked = jnp.concatenate([kept_ref[r], arrived_ref[r]], axis=0)
        for j in range(2):
            p = expand(r, bit, j)
            buf[p] = mm(forward_weight(blocks_ref[p], own), stacked)
    if last:
        for p in range(count):
            out_ref[p] = mm(embed_tile(spread_ref[p]), buf[p])
    else:
        write_split(lambda p: buf[p], count, next_bit, sc_ref[1], stay_ref, leave_ref)


def adjoint_first_kernel(sc_ref, echoes_ref, spread_ref, blocks_ref, kept_ref, leave_ref, buf, *, count, bit):
    for p in range(count):
        buf[p] = mm_t(embed_tile(spread_ref[p]), echoes_ref[p])
    own = sc_ref[0]
    for r in range(count // 2):
        kept_ref[r], leave_ref[r] = adjoint_pair(lambda p: buf[p], blocks_ref, bit, r, own)


def adjoint_cross_kernel(sc_ref, prev_kept_ref, prev_arrived_ref, blocks_ref, kept_ref, leave_ref,
                         *, count, bit, prev_bit):
    value_of = read_split(prev_kept_ref, prev_arrived_ref, prev_bit, sc_ref[1])
    own = sc_ref[0]
    for r in range(count // 2):
        kept_ref[r], leave_ref[r] = adjoint_pair(value_of, blocks_ref, bit, r, own)


def adjoint_local_kernel(sc_ref, prev_kept_ref, prev_arrived_ref, local_ref, leaf_ref, *rest,
                         count, levels, prev_bit, prior=False):
    out_ref, buf_a, buf_b = rest[prior:]
    value_of = read_split(prev_kept_ref, prev_arrived_ref, prev_bit, sc_ref[1])
    for p in range(count):
        buf_a[p] = value_of(p)
    src, dst = buf_a, buf_b
    for level in reversed(range(levels)):
        for r in range(count // 2):
            first, second = adjoint_pair(lambda p: src[p], local_ref.at[level], level, r, 0)
            dst[expand(r, level, 0)] = first
            dst[expand(r, level, 1)] = second
        src, dst = dst, src
    for p in range(count):
        out_ref[p] = mm_t(embed_tile(leaf_ref[p]), src[p])


def whole(shape):
    return pl.BlockSpec(shape, lambda i, sc, n=len(shape): (0,) * n)


def column_block(shape, chunk):
    return pl.BlockSpec(shape, lambda i, sc, c=chunk: (0, 0, c))


def level_block(shape, level, count, grouped):
    if grouped:
        return pl.BlockSpec((None, count) + tuple(shape[2:]), lambda i, sc, v=level: (v, sc[2], 0, 0))
    return pl.BlockSpec((None, count) + tuple(shape[2:]), lambda i, sc, v=level: (v, 0, 0, 0))


def call(kernel, scalars, inputs, in_specs, out_shapes, scratch, out_specs=None, aliases=None):
    grid_spec = pltpu.PrefetchScalarGridSpec(
        num_scalar_prefetch=1,
        grid=(1,),
        in_specs=in_specs,
        out_specs=out_specs or [whole(s.shape) for s in out_shapes],
        scratch_shapes=scratch,
    )
    return pl.pallas_call(
        kernel,
        grid_spec=grid_spec,
        out_shape=out_shapes,
        input_output_aliases=aliases or {},
        compiler_params=pltpu.CompilerParams(vmem_limit_bytes=48 * 1024 * 1024),
    )(scalars, *inputs)


def into_columns(kernel, scalars, inputs, in_specs, scratch, full, part, chunk, prior):
    if prior is None:
        return call(kernel, scalars, inputs, in_specs, [full], scratch,
                    out_specs=[column_block(part.shape, chunk)])
    return call(functools.partial(kernel, prior=True), scalars, inputs[:len(in_specs)] + [prior],
                in_specs + [pl.BlockSpec(memory_space=pl.ANY)], [full], scratch,
                out_specs=[column_block(part.shape, chunk)], aliases={1 + len(in_specs): 0})


def per_device(samples, echoes, leaf_maps, local_blocks, cross_blocks, outer_blocks, spread_maps):
    levels_local = local_blocks.shape[0]
    inner_bits = cross_blocks.shape[0]
    outer_bits = outer_blocks.shape[0]
    count, rows, columns = samples.shape
    width = columns // CHUNKS
    tgt_index = lax.axis_index("tgt")
    src_index = lax.axis_index("src")
    bits = [m for m in range(inner_bits)] + [m for m in range(outer_bits)]
    axes = ["tgt"] * inner_bits + ["src"] * outer_bits
    own_bits = [tgt_index >> m & 1 for m in range(inner_bits)] + [src_index >> m & 1 for m in range(outer_bits)]
    sources = [(cross_blocks, m, True) for m in range(inner_bits)] + [(outer_blocks, m, False) for m in range(outer_bits)]
    n_cross = len(bits)

    def scalars(first, second):
        return jnp.stack([first, second, tgt_index]).astype(jnp.int32)

    def blocks_spec(index):
        array, level, grouped = sources[index]
        return level_block(array.shape, level, count, grouped)

    block = jax.ShapeDtypeStruct((count, rows, width), jnp.bfloat16)
    half = jax.ShapeDtypeStruct((count // 2, rows, width), jnp.bfloat16)
    half_spec = whole(half.shape)
    zero = tgt_index * 0

    def in_order(leave, earlier):
        if earlier is None:
            return leave
        leave, _ = lax.optimization_barrier((leave, earlier))
        return leave

    fwd = []
    for chunk in range(CHUNKS):
        fwd.append(call(
            functools.partial(forward_local_kernel, count=count, levels=levels_local, next_bit=bits[0]),
            scalars(zero, own_bits[0]),
            [samples, leaf_maps, local_blocks],
            [column_block((count, rows, width), chunk), whole(leaf_maps.shape), whole(local_blocks.shape)],
            [half, half],
            [pltpu.VMEM(block.shape, jnp.bfloat16), pltpu.VMEM(block.shape, jnp.bfloat16)],
        ))
    top = n_cross - 1
    adj = []
    for chunk in range(CHUNKS):
        adj.append(call(
            functools.partial(adjoint_first_kernel, count=count, bit=bits[top]),
            scalars(own_bits[top], zero),
            [echoes, spread_maps, sources[top][0]],
            [column_block((count, rows, width), chunk), whole(spread_maps.shape), blocks_spec(top)],
            [half, half],
            [pltpu.VMEM(block.shape, jnp.bfloat16)],
        ))

    full = jax.ShapeDtypeStruct(samples.shape, jnp.bfloat16)
    image_field = None
    for step in range(n_cross):
        index = step
        bit, axis = bits[index], axes[index]
        last = index == n_cross - 1
        next_bit = 0 if last else bits[index + 1]
        earlier = None
        for chunk in range(CHUNKS):
            stay, leave = fwd[chunk]
            arrived = from_partner(in_order(leave, earlier if axis == "src" and bit > 1 else None), axis, bit)
            earlier = arrived
            inputs = [stay, arrived, sources[index][0]]
            specs = [half_spec, half_spec, blocks_spec(index)]
            if last:
                inputs.append(spread_maps)
                specs.append(whole(spread_maps.shape))
            kernel = functools.partial(forward_cross_kernel, count=count, bit=bit, next_bit=next_bit, last=last)
            if last:
                (image_field,) = into_columns(
                    kernel, scalars(own_bits[index], zero), inputs, specs,
                    [pltpu.VMEM(block.shape, jnp.bfloat16)], full, block, chunk, image_field)
            else:
                fwd[chunk] = tuple(call(
                    kernel,
                    scalars(own_bits[index], own_bits[index + 1]),
                    inputs,
                    specs,
                    [half, half],
                    [pltpu.VMEM(block.shape, jnp.bfloat16)],
                ))

        index = top - step
        earlier = None
        for chunk in range(CHUNKS):
            kept, leave = adj[chunk]
            arrived = from_partner(in_order(leave, earlier if axes[index] == "src" and bits[index] > 1 else None),
                                   axes[index], bits[index])
            earlier = arrived
            if index > 0:
                adj[chunk] = tuple(call(
                    functools.partial(adjoint_cross_kernel, count=count, bit=bits[index - 1], prev_bit=bits[index]),
                    scalars(own_bits[index - 1], own_bits[index]),
                    [kept, arrived, sources[index - 1][0]],
                    [half_spec, half_spec, blocks_spec(index - 1)],
                    [half, half],
                    [],
                ))
            else:
                adj[chunk] = (kept, arrived)

    aperture_field = None
    for chunk in range(CHUNKS):
        kept, arrived = adj[chunk]
        (aperture_field,) = into_columns(
            functools.partial(adjoint_local_kernel, count=count, levels=levels_local, prev_bit=bits[0]),
            scalars(zero, own_bits[0]),
            [kept, arrived, local_blocks, leaf_maps],
            [half_spec, half_spec, whole(local_blocks.shape), whole(leaf_maps.shape)],
            [pltpu.VMEM(block.shape, jnp.bfloat16), pltpu.VMEM(block.shape, jnp.bfloat16)],
            full, block, chunk, aperture_field)
    return (image_field, aperture_field)


def solution(mesh):
    return jax.shard_map(
        per_device,
        mesh=mesh,
        in_specs=(
            P(("src", "tgt"), None, None),
            P(("src", "tgt"), None, None),
            P(("src", "tgt"), None, None),
            P(None, ("src", "tgt"), None, None),
            P(None, "src", None, None),
            P(None, ("src", "tgt"), None, None),
            P(("src", "tgt"), None, None),
        ),
        out_specs=(P(("src", "tgt"), None, None), P(("src", "tgt"), None, None)),
        check_vma=False,
    )
```

```python
import functools

import jax
import jax.numpy as jnp
from jax import lax
from jax.experimental import pallas as pl
from jax.experimental.pallas import tpu as pltpu
from jax.sharding import PartitionSpec as P

CHUNKS = 2


def from_partner(x, axis, apart):
    return lax.ppermute(x, axis, [(i, i ^ 1 << apart) for i in range(lax.axis_size(axis))])


def expand(r, bit, j):
    return ((r >> bit) << (bit + 1)) | (j << bit) | (r & ((1 << bit) - 1))


def compress(p, bit):
    return ((p >> (bit + 1)) << bit) | (p & ((1 << bit) - 1))


def mm(w, x):
    return jnp.dot(w, x, preferred_element_type=jnp.float32).astype(jnp.bfloat16)


def mm_t(w, x):
    product = lax.dot_general(w, x, (((0,), (0,)), ((), ())), preferred_element_type=jnp.float32)
    return product.astype(jnp.bfloat16)


def embed_tile(stored):
    half = stored.shape[-1] // 2
    lane = lax.broadcasted_iota(jnp.int32, stored.shape, 1)
    top = jnp.where(lane < half, stored, -stored)
    bottom = pltpu.roll(stored, half, 1)
    return jnp.concatenate([top, bottom], axis=0)


def block_pair(stored, own):
    width = stored.shape[-1] // 2
    first = embed_tile(stored[:, :width])
    second = embed_tile(stored[:, width:])
    if isinstance(own, int) and own == 0:
        return first, second
    return jnp.where(own == 0, first, second), jnp.where(own == 0, second, first)


def forward_weight(stored, own):
    first, second = block_pair(stored, own)
    return jnp.concatenate([first, second], axis=1)


def write_split(value_of, count, bit, own, stay_ref, leave_ref):
    for p in range(count):
        r = compress(p, bit)
        here = ((p >> bit) & 1) == own

        @pl.when(here)
        def _():
            stay_ref[r] = value_of(p)

        @pl.when(jnp.logical_not(here))
        def _():
            leave_ref[r] = value_of(p)


def read_split(kept_ref, arrived_ref, bit, own):
    def value_of(p):
        r = compress(p, bit)
        return jnp.where(((p >> bit) & 1) == own, kept_ref[r], arrived_ref[r])

    return value_of


def adjoint_pair(value_of, blocks_ref, bit, r, own):
    lower, upper = expand(r, bit, 0), expand(r, bit, 1)
    stacked = jnp.concatenate([value_of(lower), value_of(upper)], axis=0)
    first_lower, second_lower = block_pair(blocks_ref[lower], own)
    first_upper, second_upper = block_pair(blocks_ref[upper], own)
    kept = mm_t(jnp.concatenate([first_lower, first_upper], axis=0), stacked)
    leave = mm_t(jnp.concatenate([second_lower, second_upper], axis=0), stacked)
    return kept, leave


def forward_local_kernel(sc_ref, samples_ref, leaf_ref, local_ref, stay_ref, leave_ref, buf_a, buf_b,
                         *, count, levels, next_bit):
    for p in range(count):
        buf_a[p] = mm(embed_tile(leaf_ref[p]), samples_ref[p])
    src, dst = buf_a, buf_b
    for level in range(levels):
        for r in range(count // 2):
            p0, p1 = expand(r, level, 0), expand(r, level, 1)
            stacked = jnp.concatenate([src[p0], src[p1]], axis=0)
            dst[p0] = mm(forward_weight(local_ref[level, p0], 0), stacked)
            dst[p1] = mm(forward_weight(local_ref[level, p1], 0), stacked)
        src, dst = dst, src
    write_split(lambda p: src[p], count, next_bit, sc_ref[1], stay_ref, leave_ref)


def forward_cross_kernel(sc_ref, kept_ref, arrived_ref, blocks_ref, *rest, count, bit, next_bit, last, prior=False):
    if last:
        spread_ref, out_ref, buf = (rest[0],) + rest[1 + prior:]
    else:
        stay_ref, leave_ref, buf = rest
    own = sc_ref[0]
    for r in range(count // 2):
        stacked = jnp.concatenate([kept_ref[r], arrived_ref[r]], axis=0)
        for j in range(2):
            p = expand(r, bit, j)
            buf[p] = mm(forward_weight(blocks_ref[p], own), stacked)
    if last:
        for p in range(count):
            out_ref[p] = mm(embed_tile(spread_ref[p]), buf[p])
    else:
        write_split(lambda p: buf[p], count, next_bit, sc_ref[1], stay_ref, leave_ref)


def adjoint_first_kernel(sc_ref, echoes_ref, spread_ref, blocks_ref, kept_ref, leave_ref, buf, *, count, bit):
    for p in range(count):
        buf[p] = mm_t(embed_tile(spread_ref[p]), echoes_ref[p])
    own = sc_ref[0]
    for r in range(count // 2):
        kept_ref[r], leave_ref[r] = adjoint_pair(lambda p: buf[p], blocks_ref, bit, r, own)


def adjoint_cross_kernel(sc_ref, prev_kept_ref, prev_arrived_ref, blocks_ref, kept_ref, leave_ref,
                         *, count, bit, prev_bit):
    value_of = read_split(prev_kept_ref, prev_arrived_ref, prev_bit, sc_ref[1])
    own = sc_ref[0]
    for r in range(count // 2):
        kept_ref[r], leave_ref[r] = adjoint_pair(value_of, blocks_ref, bit, r, own)


def adjoint_local_kernel(sc_ref, prev_kept_ref, prev_arrived_ref, local_ref, leaf_ref, *rest,
                         count, levels, prev_bit, prior=False):
    out_ref, buf_a, buf_b = rest[prior:]
    value_of = read_split(prev_kept_ref, prev_arrived_ref, prev_bit, sc_ref[1])
    for p in range(count):
        buf_a[p] = value_of(p)
    src, dst = buf_a, buf_b
    for level in reversed(range(levels)):
        for r in range(count // 2):
            first, second = adjoint_pair(lambda p: src[p], local_ref.at[level], level, r, 0)
            dst[expand(r, level, 0)] = first
            dst[expand(r, level, 1)] = second
        src, dst = dst, src
    for p in range(count):
        out_ref[p] = mm_t(embed_tile(leaf_ref[p]), src[p])


def whole(shape):
    return pl.BlockSpec(shape, lambda i, sc, n=len(shape): (0,) * n)


def column_block(shape, chunk):
    return pl.BlockSpec(shape, lambda i, sc, c=chunk: (0, 0, c))


def level_block(shape, level, count, grouped):
    if grouped:
        return pl.BlockSpec((None, count) + tuple(shape[2:]), lambda i, sc, v=level: (v, sc[2], 0, 0))
    return pl.BlockSpec((None, count) + tuple(shape[2:]), lambda i, sc, v=level: (v, 0, 0, 0))


def call(kernel, scalars, inputs, in_specs, out_shapes, scratch, out_specs=None, aliases=None):
    grid_spec = pltpu.PrefetchScalarGridSpec(
        num_scalar_prefetch=1,
        grid=(1,),
        in_specs=in_specs,
        out_specs=out_specs or [whole(s.shape) for s in out_shapes],
        scratch_shapes=scratch,
    )
    return pl.pallas_call(
        kernel,
        grid_spec=grid_spec,
        out_shape=out_shapes,
        input_output_aliases=aliases or {},
        compiler_params=pltpu.CompilerParams(vmem_limit_bytes=48 * 1024 * 1024),
    )(scalars, *inputs)


def into_columns(kernel, scalars, inputs, in_specs, scratch, full, part, chunk, prior):
    if prior is None:
        return call(kernel, scalars, inputs, in_specs, [full], scratch,
                    out_specs=[column_block(part.shape, chunk)])
    return call(functools.partial(kernel, prior=True), scalars, inputs[:len(in_specs)] + [prior],
                in_specs + [pl.BlockSpec(memory_space=pl.ANY)], [full], scratch,
                out_specs=[column_block(part.shape, chunk)], aliases={1 + len(in_specs): 0})


def per_device(samples, echoes, leaf_maps, local_blocks, cross_blocks, outer_blocks, spread_maps):
    levels_local = local_blocks.shape[0]
    inner_bits = cross_blocks.shape[0]
    outer_bits = outer_blocks.shape[0]
    count, rows, columns = samples.shape
    width = columns // CHUNKS
    tgt_index = lax.axis_index("tgt")
    src_index = lax.axis_index("src")
    bits = [m for m in range(inner_bits)] + [m for m in range(outer_bits)]
    axes = ["tgt"] * inner_bits + ["src"] * outer_bits
    own_bits = [tgt_index >> m & 1 for m in range(inner_bits)] + [src_index >> m & 1 for m in range(outer_bits)]
    sources = [(cross_blocks, m, True) for m in range(inner_bits)] + [(outer_blocks, m, False) for m in range(outer_bits)]
    n_cross = len(bits)

    def scalars(first, second):
        return jnp.stack([first, second, tgt_index]).astype(jnp.int32)

    def blocks_spec(index):
        array, level, grouped = sources[index]
        return level_block(array.shape, level, count, grouped)

    block = jax.ShapeDtypeStruct((count, rows, width), jnp.bfloat16)
    half = jax.ShapeDtypeStruct((count // 2, rows, width), jnp.bfloat16)
    half_spec = whole(half.shape)
    zero = tgt_index * 0

    def in_order(leave, earlier):
        if earlier is None:
            return leave
        leave, _ = lax.optimization_barrier((leave, earlier))
        return leave

    fwd = []
    for chunk in range(CHUNKS):
        fwd.append(call(
            functools.partial(forward_local_kernel, count=count, levels=levels_local, next_bit=bits[0]),
            scalars(zero, own_bits[0]),
            [samples, leaf_maps, local_blocks],
            [column_block((count, rows, width), chunk), whole(leaf_maps.shape), whole(local_blocks.shape)],
            [half, half],
            [pltpu.VMEM(block.shape, jnp.bfloat16), pltpu.VMEM(block.shape, jnp.bfloat16)],
        ))
    top = n_cross - 1
    adj = []
    for chunk in range(CHUNKS):
        adj.append(call(
            functools.partial(adjoint_first_kernel, count=count, bit=bits[top]),
            scalars(own_bits[top], zero),
            [echoes, spread_maps, sources[top][0]],
            [column_block((count, rows, width), chunk), whole(spread_maps.shape), blocks_spec(top)],
            [half, half],
            [pltpu.VMEM(block.shape, jnp.bfloat16)],
        ))

    full = jax.ShapeDtypeStruct(samples.shape, jnp.bfloat16)
    image_field = None
    for step in range(n_cross):
        index = step
        bit, axis = bits[index], axes[index]
        last = index == n_cross - 1
        next_bit = 0 if last else bits[index + 1]
        earlier = None
        for chunk in range(CHUNKS):
            stay, leave = fwd[chunk]
            arrived = from_partner(in_order(leave, earlier if axis == "src" and bit > 0 else None), axis, bit)
            earlier = arrived
            inputs = [stay, arrived, sources[index][0]]
            specs = [half_spec, half_spec, blocks_spec(index)]
            if last:
                inputs.append(spread_maps)
                specs.append(whole(spread_maps.shape))
            kernel = functools.partial(forward_cross_kernel, count=count, bit=bit, next_bit=next_bit, last=last)
            if last:
                (image_field,) = into_columns(
                    kernel, scalars(own_bits[index], zero), inputs, specs,
                    [pltpu.VMEM(block.shape, jnp.bfloat16)], full, block, chunk, image_field)
            else:
                fwd[chunk] = tuple(call(
                    kernel,
                    scalars(own_bits[index], own_bits[index + 1]),
                    inputs,
                    specs,
                    [half, half],
                    [pltpu.VMEM(block.shape, jnp.bfloat16)],
                ))

        index = top - step
        earlier = None
        for chunk in range(CHUNKS):
            kept, leave = adj[chunk]
            queued = (axes[index] == "src" and bits[index] > 0) or index == 0
            arrived = from_partner(in_order(leave, earlier if queued else None),
                                   axes[index], bits[index])
            earlier = arrived
            if index > 0:
                adj[chunk] = tuple(call(
                    functools.partial(adjoint_cross_kernel, count=count, bit=bits[index - 1], prev_bit=bits[index]),
                    scalars(own_bits[index - 1], own_bits[index]),
                    [kept, arrived, sources[index - 1][0]],
                    [half_spec, half_spec, blocks_spec(index - 1)],
                    [half, half],
                    [],
                ))
            else:
                adj[chunk] = (kept, arrived)

    aperture_field = None
    for chunk in range(CHUNKS):
        kept, arrived = adj[chunk]
        (aperture_field,) = into_columns(
            functools.partial(adjoint_local_kernel, count=count, levels=levels_local, prev_bit=bits[0]),
            scalars(zero, own_bits[0]),
            [kept, arrived, local_blocks, leaf_maps],
            [half_spec, half_spec, whole(local_blocks.shape), whole(leaf_maps.shape)],
            [pltpu.VMEM(block.shape, jnp.bfloat16), pltpu.VMEM(block.shape, jnp.bfloat16)],
            full, block, chunk, aperture_field)
    return (image_field, aperture_field)


def solution(mesh):
    return jax.shard_map(
        per_device,
        mesh=mesh,
        in_specs=(
            P(("src", "tgt"), None, None),
            P(("src", "tgt"), None, None),
            P(("src", "tgt"), None, None),
            P(None, ("src", "tgt"), None, None),
            P(None, "src", None, None),
            P(None, ("src", "tgt"), None, None),
            P(("src", "tgt"), None, None),
        ),
        out_specs=(P(("src", "tgt"), None, None), P(("src", "tgt"), None, None)),
        check_vma=False,
    )
```

```python
import functools

import jax
import jax.numpy as jnp
from jax import lax
from jax.experimental import pallas as pl
from jax.experimental.pallas import tpu as pltpu
from jax.sharding import PartitionSpec as P

CHUNKS = 2


def from_partner(x, axis, apart):
    return lax.ppermute(x, axis, [(i, i ^ 1 << apart) for i in range(lax.axis_size(axis))])


def expand(r, bit, j):
    return ((r >> bit) << (bit + 1)) | (j << bit) | (r & ((1 << bit) - 1))


def compress(p, bit):
    return ((p >> (bit + 1)) << bit) | (p & ((1 << bit) - 1))


def mm(w, x):
    return jnp.dot(w, x, preferred_element_type=jnp.float32).astype(jnp.bfloat16)


def mm_t(w, x):
    product = lax.dot_general(w, x, (((0,), (0,)), ((), ())), preferred_element_type=jnp.float32)
    return product.astype(jnp.bfloat16)


def embed_tile(stored):
    half = stored.shape[-1] // 2
    lane = lax.broadcasted_iota(jnp.int32, stored.shape, 1)
    top = jnp.where(lane < half, stored, -stored)
    bottom = pltpu.roll(stored, half, 1)
    return jnp.concatenate([top, bottom], axis=0)


def block_pair(stored, own):
    width = stored.shape[-1] // 2
    first = embed_tile(stored[:, :width])
    second = embed_tile(stored[:, width:])
    if isinstance(own, int) and own == 0:
        return first, second
    return jnp.where(own == 0, first, second), jnp.where(own == 0, second, first)


def forward_weight(stored, own):
    first, second = block_pair(stored, own)
    return jnp.concatenate([first, second], axis=1)


def write_split(value_of, count, bit, own, stay_ref, leave_ref):
    for p in range(count):
        r = compress(p, bit)
        here = ((p >> bit) & 1) == own

        @pl.when(here)
        def _():
            stay_ref[r] = value_of(p)

        @pl.when(jnp.logical_not(here))
        def _():
            leave_ref[r] = value_of(p)


def read_split(kept_ref, arrived_ref, bit, own):
    def value_of(p):
        r = compress(p, bit)
        return jnp.where(((p >> bit) & 1) == own, kept_ref[r], arrived_ref[r])

    return value_of


def adjoint_pair(value_of, blocks_ref, bit, r, own):
    lower, upper = expand(r, bit, 0), expand(r, bit, 1)
    stacked = jnp.concatenate([value_of(lower), value_of(upper)], axis=0)
    first_lower, second_lower = block_pair(blocks_ref[lower], own)
    first_upper, second_upper = block_pair(blocks_ref[upper], own)
    kept = mm_t(jnp.concatenate([first_lower, first_upper], axis=0), stacked)
    leave = mm_t(jnp.concatenate([second_lower, second_upper], axis=0), stacked)
    return kept, leave


def forward_local_kernel(sc_ref, samples_ref, leaf_ref, local_ref, stay_ref, leave_ref, buf_a, buf_b,
                         *, count, levels, next_bit):
    for p in range(count):
        buf_a[p] = mm(embed_tile(leaf_ref[p]), samples_ref[p])
    src, dst = buf_a, buf_b
    for level in range(levels):
        for r in range(count // 2):
            p0, p1 = expand(r, level, 0), expand(r, level, 1)
            stacked = jnp.concatenate([src[p0], src[p1]], axis=0)
            dst[p0] = mm(forward_weight(local_ref[level, p0], 0), stacked)
            dst[p1] = mm(forward_weight(local_ref[level, p1], 0), stacked)
        src, dst = dst, src
    write_split(lambda p: src[p], count, next_bit, sc_ref[1], stay_ref, leave_ref)


def forward_cross_kernel(sc_ref, kept_ref, arrived_ref, blocks_ref, *rest, count, bit, next_bit, last, prior=False):
    if last:
        spread_ref, out_ref, buf = (rest[0],) + rest[1 + prior:]
    else:
        stay_ref, leave_ref, buf = rest
    own = sc_ref[0]
    for r in range(count // 2):
        stacked = jnp.concatenate([kept_ref[r], arrived_ref[r]], axis=0)
        for j in range(2):
            p = expand(r, bit, j)
            buf[p] = mm(forward_weight(blocks_ref[p], own), stacked)
    if last:
        for p in range(count):
            out_ref[p] = mm(embed_tile(spread_ref[p]), buf[p])
    else:
        write_split(lambda p: buf[p], count, next_bit, sc_ref[1], stay_ref, leave_ref)


def adjoint_first_kernel(sc_ref, echoes_ref, spread_ref, blocks_ref, kept_ref, leave_ref, buf, *, count, bit):
    for p in range(count):
        buf[p] = mm_t(embed_tile(spread_ref[p]), echoes_ref[p])
    own = sc_ref[0]
    for r in range(count // 2):
        kept_ref[r], leave_ref[r] = adjoint_pair(lambda p: buf[p], blocks_ref, bit, r, own)


def adjoint_cross_kernel(sc_ref, prev_kept_ref, prev_arrived_ref, blocks_ref, kept_ref, leave_ref,
                         *, count, bit, prev_bit):
    value_of = read_split(prev_kept_ref, prev_arrived_ref, prev_bit, sc_ref[1])
    own = sc_ref[0]
    for r in range(count // 2):
        kept_ref[r], leave_ref[r] = adjoint_pair(value_of, blocks_ref, bit, r, own)


def adjoint_local_kernel(sc_ref, prev_kept_ref, prev_arrived_ref, local_ref, leaf_ref, *rest,
                         count, levels, prev_bit, prior=False):
    out_ref, buf_a, buf_b = rest[prior:]
    value_of = read_split(prev_kept_ref, prev_arrived_ref, prev_bit, sc_ref[1])
    for p in range(count):
        buf_a[p] = value_of(p)
    src, dst = buf_a, buf_b
    for level in reversed(range(levels)):
        for r in range(count // 2):
            first, second = adjoint_pair(lambda p: src[p], local_ref.at[level], level, r, 0)
            dst[expand(r, level, 0)] = first
            dst[expand(r, level, 1)] = second
        src, dst = dst, src
    for p in range(count):
        out_ref[p] = mm_t(embed_tile(leaf_ref[p]), src[p])


def whole(shape):
    return pl.BlockSpec(shape, lambda i, sc, n=len(shape): (0,) * n)


def column_block(shape, chunk):
    return pl.BlockSpec(shape, lambda i, sc, c=chunk: (0, 0, c))


def level_block(shape, level, count, grouped):
    if grouped:
        return pl.BlockSpec((None, count) + tuple(shape[2:]), lambda i, sc, v=level: (v, sc[2], 0, 0))
    return pl.BlockSpec((None, count) + tuple(shape[2:]), lambda i, sc, v=level: (v, 0, 0, 0))


def call(kernel, scalars, inputs, in_specs, out_shapes, scratch, out_specs=None, aliases=None):
    grid_spec = pltpu.PrefetchScalarGridSpec(
        num_scalar_prefetch=1,
        grid=(1,),
        in_specs=in_specs,
        out_specs=out_specs or [whole(s.shape) for s in out_shapes],
        scratch_shapes=scratch,
    )
    return pl.pallas_call(
        kernel,
        grid_spec=grid_spec,
        out_shape=out_shapes,
        input_output_aliases=aliases or {},
        compiler_params=pltpu.CompilerParams(vmem_limit_bytes=48 * 1024 * 1024),
    )(scalars, *inputs)


def into_columns(kernel, scalars, inputs, in_specs, scratch, full, part, chunk, prior):
    if prior is None:
        return call(kernel, scalars, inputs, in_specs, [full], scratch,
                    out_specs=[column_block(part.shape, chunk)])
    return call(functools.partial(kernel, prior=True), scalars, inputs[:len(in_specs)] + [prior],
                in_specs + [pl.BlockSpec(memory_space=pl.ANY)], [full], scratch,
                out_specs=[column_block(part.shape, chunk)], aliases={1 + len(in_specs): 0})


def per_device(samples, echoes, leaf_maps, local_blocks, cross_blocks, outer_blocks, spread_maps):
    levels_local = local_blocks.shape[0]
    inner_bits = cross_blocks.shape[0]
    outer_bits = outer_blocks.shape[0]
    count, rows, columns = samples.shape
    width = columns // CHUNKS
    tgt_index = lax.axis_index("tgt")
    src_index = lax.axis_index("src")
    bits = [m for m in range(inner_bits)] + [m for m in range(outer_bits)]
    axes = ["tgt"] * inner_bits + ["src"] * outer_bits
    own_bits = [tgt_index >> m & 1 for m in range(inner_bits)] + [src_index >> m & 1 for m in range(outer_bits)]
    sources = [(cross_blocks, m, True) for m in range(inner_bits)] + [(outer_blocks, m, False) for m in range(outer_bits)]
    n_cross = len(bits)

    def scalars(first, second):
        return jnp.stack([first, second, tgt_index]).astype(jnp.int32)

    def blocks_spec(index):
        array, level, grouped = sources[index]
        return level_block(array.shape, level, count, grouped)

    block = jax.ShapeDtypeStruct((count, rows, width), jnp.bfloat16)
    half = jax.ShapeDtypeStruct((count // 2, rows, width), jnp.bfloat16)
    half_spec = whole(half.shape)
    zero = tgt_index * 0

    def in_order(leave, earlier):
        if earlier is None:
            return leave
        leave, _ = lax.optimization_barrier((leave, earlier))
        return leave

    fwd = []
    for chunk in range(CHUNKS):
        fwd.append(call(
            functools.partial(forward_local_kernel, count=count, levels=levels_local, next_bit=bits[0]),
            scalars(zero, own_bits[0]),
            [samples, leaf_maps, local_blocks],
            [column_block((count, rows, width), chunk), whole(leaf_maps.shape), whole(local_blocks.shape)],
            [half, half],
            [pltpu.VMEM(block.shape, jnp.bfloat16), pltpu.VMEM(block.shape, jnp.bfloat16)],
        ))
    top = n_cross - 1
    adj = []
    for chunk in range(CHUNKS):
        adj.append(call(
            functools.partial(adjoint_first_kernel, count=count, bit=bits[top]),
            scalars(own_bits[top], zero),
            [echoes, spread_maps, sources[top][0]],
            [column_block((count, rows, width), chunk), whole(spread_maps.shape), blocks_spec(top)],
            [half, half],
            [pltpu.VMEM(block.shape, jnp.bfloat16)],
        ))

    full = jax.ShapeDtypeStruct(samples.shape, jnp.bfloat16)
    image_field = None
    for step in range(n_cross):
        index = step
        bit, axis = bits[index], axes[index]
        last = index == n_cross - 1
        next_bit = 0 if last else bits[index + 1]
        earlier = None
        for chunk in range(CHUNKS):
            stay, leave = fwd[chunk]
            queued = axis == "src" and bit > 0 and not last
            arrived = from_partner(in_order(leave, earlier if queued else None), axis, bit)
            earlier = arrived
            inputs = [stay, arrived, sources[index][0]]
            specs = [half_spec, half_spec, blocks_spec(index)]
            if last:
                inputs.append(spread_maps)
                specs.append(whole(spread_maps.shape))
            kernel = functools.partial(forward_cross_kernel, count=count, bit=bit, next_bit=next_bit, last=last)
            if last:
                (image_field,) = into_columns(
                    kernel, scalars(own_bits[index], zero), inputs, specs,
                    [pltpu.VMEM(block.shape, jnp.bfloat16)], full, block, chunk, image_field)
            else:
                fwd[chunk] = tuple(call(
                    kernel,
                    scalars(own_bits[index], own_bits[index + 1]),
                    inputs,
                    specs,
                    [half, half],
                    [pltpu.VMEM(block.shape, jnp.bfloat16)],
                ))

        index = top - step
        earlier = None
        for chunk in range(CHUNKS):
            kept, leave = adj[chunk]
            arrived = from_partner(in_order(leave, earlier if axes[index] == "src" and bits[index] > 0 else None),
                                   axes[index], bits[index])
            earlier = arrived
            if index > 0:
                adj[chunk] = tuple(call(
                    functools.partial(adjoint_cross_kernel, count=count, bit=bits[index - 1], prev_bit=bits[index]),
                    scalars(own_bits[index - 1], own_bits[index]),
                    [kept, arrived, sources[index - 1][0]],
                    [half_spec, half_spec, blocks_spec(index - 1)],
                    [half, half],
                    [],
                ))
            else:
                adj[chunk] = (kept, arrived)

    aperture_field = None
    for chunk in range(CHUNKS):
        kept, arrived = adj[chunk]
        (aperture_field,) = into_columns(
            functools.partial(adjoint_local_kernel, count=count, levels=levels_local, prev_bit=bits[0]),
            scalars(zero, own_bits[0]),
            [kept, arrived, local_blocks, leaf_maps],
            [half_spec, half_spec, whole(local_blocks.shape), whole(leaf_maps.shape)],
            [pltpu.VMEM(block.shape, jnp.bfloat16), pltpu.VMEM(block.shape, jnp.bfloat16)],
            full, block, chunk, aperture_field)
    return (image_field, aperture_field)


def solution(mesh):
    return jax.shard_map(
        per_device,
        mesh=mesh,
        in_specs=(
            P(("src", "tgt"), None, None),
            P(("src", "tgt"), None, None),
            P(("src", "tgt"), None, None),
            P(None, ("src", "tgt"), None, None),
            P(None, "src", None, None),
            P(None, ("src", "tgt"), None, None),
            P(("src", "tgt"), None, None),
        ),
        out_specs=(P(("src", "tgt"), None, None), P(("src", "tgt"), None, None)),
        check_vma=False,
    )
```

```python
import functools

import jax
import jax.numpy as jnp
from jax import lax
from jax.experimental import pallas as pl
from jax.experimental.pallas import tpu as pltpu
from jax.sharding import PartitionSpec as P

CHUNKS = 2


def from_partner(x, axis, apart):
    return lax.ppermute(x, axis, [(i, i ^ 1 << apart) for i in range(lax.axis_size(axis))])


def expand(r, bit, j):
    return ((r >> bit) << (bit + 1)) | (j << bit) | (r & ((1 << bit) - 1))


def compress(p, bit):
    return ((p >> (bit + 1)) << bit) | (p & ((1 << bit) - 1))


def mm(w, x):
    return jnp.dot(w, x, preferred_element_type=jnp.float32).astype(jnp.bfloat16)


def mm_t(w, x):
    return mm(w.astype(jnp.float32).T.astype(jnp.bfloat16), x)


def embed_tile(stored):
    half = stored.shape[-1] // 2
    lane = lax.broadcasted_iota(jnp.int32, stored.shape, 1)
    top = jnp.where(lane < half, stored, -stored)
    bottom = pltpu.roll(stored, half, 1)
    return jnp.concatenate([top, bottom], axis=0)


def block_pair(stored, own):
    width = stored.shape[-1] // 2
    first = embed_tile(stored[:, :width])
    second = embed_tile(stored[:, width:])
    if isinstance(own, int) and own == 0:
        return first, second
    return jnp.where(own == 0, first, second), jnp.where(own == 0, second, first)


def forward_weight(stored, own):
    first, second = block_pair(stored, own)
    return jnp.concatenate([first, second], axis=1)


def write_split(value_of, count, bit, own, stay_ref, leave_ref):
    for p in range(count):
        r = compress(p, bit)
        here = ((p >> bit) & 1) == own

        @pl.when(here)
        def _():
            stay_ref[r] = value_of(p)

        @pl.when(jnp.logical_not(here))
        def _():
            leave_ref[r] = value_of(p)


def read_split(kept_ref, arrived_ref, bit, own):
    def value_of(p):
        r = compress(p, bit)
        return jnp.where(((p >> bit) & 1) == own, kept_ref[r], arrived_ref[r])

    return value_of


def adjoint_pair(value_of, blocks_ref, bit, r, own):
    lower, upper = expand(r, bit, 0), expand(r, bit, 1)
    stacked = jnp.concatenate([value_of(lower), value_of(upper)], axis=0)
    first_lower, second_lower = block_pair(blocks_ref[lower], own)
    first_upper, second_upper = block_pair(blocks_ref[upper], own)
    kept = mm_t(jnp.concatenate([first_lower, first_upper], axis=0), stacked)
    leave = mm_t(jnp.concatenate([second_lower, second_upper], axis=0), stacked)
    return kept, leave


def forward_local_kernel(sc_ref, samples_ref, leaf_ref, local_ref, stay_ref, leave_ref, buf_a, buf_b,
                         *, count, levels, next_bit):
    for p in range(count):
        buf_a[p] = mm(embed_tile(leaf_ref[p]), samples_ref[p])
    src, dst = buf_a, buf_b
    for level in range(levels):
        for r in range(count // 2):
            p0, p1 = expand(r, level, 0), expand(r, level, 1)
            stacked = jnp.concatenate([src[p0], src[p1]], axis=0)
            dst[p0] = mm(forward_weight(local_ref[level, p0], 0), stacked)
            dst[p1] = mm(forward_weight(local_ref[level, p1], 0), stacked)
        src, dst = dst, src
    write_split(lambda p: src[p], count, next_bit, sc_ref[1], stay_ref, leave_ref)


def forward_cross_kernel(sc_ref, kept_ref, arrived_ref, blocks_ref, *rest, count, bit, next_bit, last, prior=False):
    if last:
        spread_ref, out_ref, buf = (rest[0],) + rest[1 + prior:]
    else:
        stay_ref, leave_ref, buf = rest
    own = sc_ref[0]
    for r in range(count // 2):
        stacked = jnp.concatenate([kept_ref[r], arrived_ref[r]], axis=0)
        for j in range(2):
            p = expand(r, bit, j)
            buf[p] = mm(forward_weight(blocks_ref[p], own), stacked)
    if last:
        for p in range(count):
            out_ref[p] = mm(embed_tile(spread_ref[p]), buf[p])
    else:
        write_split(lambda p: buf[p], count, next_bit, sc_ref[1], stay_ref, leave_ref)


def adjoint_first_kernel(sc_ref, echoes_ref, spread_ref, blocks_ref, kept_ref, leave_ref, buf, *, count, bit):
    for p in range(count):
        buf[p] = mm_t(embed_tile(spread_ref[p]), echoes_ref[p])
    own = sc_ref[0]
    for r in range(count // 2):
        kept_ref[r], leave_ref[r] = adjoint_pair(lambda p: buf[p], blocks_ref, bit, r, own)


def adjoint_cross_kernel(sc_ref, prev_kept_ref, prev_arrived_ref, blocks_ref, kept_ref, leave_ref,
                         *, count, bit, prev_bit):
    value_of = read_split(prev_kept_ref, prev_arrived_ref, prev_bit, sc_ref[1])
    own = sc_ref[0]
    for r in range(count // 2):
        kept_ref[r], leave_ref[r] = adjoint_pair(value_of, blocks_ref, bit, r, own)


def adjoint_local_kernel(sc_ref, prev_kept_ref, prev_arrived_ref, local_ref, leaf_ref, *rest,
                         count, levels, prev_bit, prior=False):
    out_ref, buf_a, buf_b = rest[prior:]
    value_of = read_split(prev_kept_ref, prev_arrived_ref, prev_bit, sc_ref[1])
    for p in range(count):
        buf_a[p] = value_of(p)
    src, dst = buf_a, buf_b
    for level in reversed(range(levels)):
        for r in range(count // 2):
            first, second = adjoint_pair(lambda p: src[p], local_ref.at[level], level, r, 0)
            dst[expand(r, level, 0)] = first
            dst[expand(r, level, 1)] = second
        src, dst = dst, src
    for p in range(count):
        out_ref[p] = mm_t(embed_tile(leaf_ref[p]), src[p])


def whole(shape):
    return pl.BlockSpec(shape, lambda i, sc, n=len(shape): (0,) * n)


def column_block(shape, chunk):
    return pl.BlockSpec(shape, lambda i, sc, c=chunk: (0, 0, c))


def level_block(shape, level, count, grouped):
    if grouped:
        return pl.BlockSpec((None, count) + tuple(shape[2:]), lambda i, sc, v=level: (v, sc[2], 0, 0))
    return pl.BlockSpec((None, count) + tuple(shape[2:]), lambda i, sc, v=level: (v, 0, 0, 0))


def call(kernel, scalars, inputs, in_specs, out_shapes, scratch, out_specs=None, aliases=None):
    grid_spec = pltpu.PrefetchScalarGridSpec(
        num_scalar_prefetch=1,
        grid=(1,),
        in_specs=in_specs,
        out_specs=out_specs or [whole(s.shape) for s in out_shapes],
        scratch_shapes=scratch,
    )
    return pl.pallas_call(
        kernel,
        grid_spec=grid_spec,
        out_shape=out_shapes,
        input_output_aliases=aliases or {},
        compiler_params=pltpu.CompilerParams(vmem_limit_bytes=48 * 1024 * 1024),
    )(scalars, *inputs)


def into_columns(kernel, scalars, inputs, in_specs, scratch, full, part, chunk, prior):
    if prior is None:
        return call(kernel, scalars, inputs, in_specs, [full], scratch,
                    out_specs=[column_block(part.shape, chunk)])
    return call(functools.partial(kernel, prior=True), scalars, inputs[:len(in_specs)] + [prior],
                in_specs + [pl.BlockSpec(memory_space=pl.ANY)], [full], scratch,
                out_specs=[column_block(part.shape, chunk)], aliases={1 + len(in_specs): 0})


def per_device(samples, echoes, leaf_maps, local_blocks, cross_blocks, outer_blocks, spread_maps):
    levels_local = local_blocks.shape[0]
    inner_bits = cross_blocks.shape[0]
    outer_bits = outer_blocks.shape[0]
    count, rows, columns = samples.shape
    width = columns // CHUNKS
    tgt_index = lax.axis_index("tgt")
    src_index = lax.axis_index("src")
    bits = [m for m in range(inner_bits)] + [m for m in range(outer_bits)]
    axes = ["tgt"] * inner_bits + ["src"] * outer_bits
    own_bits = [tgt_index >> m & 1 for m in range(inner_bits)] + [src_index >> m & 1 for m in range(outer_bits)]
    sources = [(cross_blocks, m, True) for m in range(inner_bits)] + [(outer_blocks, m, False) for m in range(outer_bits)]
    n_cross = len(bits)

    def scalars(first, second):
        return jnp.stack([first, second, tgt_index]).astype(jnp.int32)

    def blocks_spec(index):
        array, level, grouped = sources[index]
        return level_block(array.shape, level, count, grouped)

    block = jax.ShapeDtypeStruct((count, rows, width), jnp.bfloat16)
    half = jax.ShapeDtypeStruct((count // 2, rows, width), jnp.bfloat16)
    half_spec = whole(half.shape)
    zero = tgt_index * 0

    def in_order(leave, earlier):
        if earlier is None:
            return leave
        leave, _ = lax.optimization_barrier((leave, earlier))
        return leave

    fwd = []
    for chunk in range(CHUNKS):
        fwd.append(call(
            functools.partial(forward_local_kernel, count=count, levels=levels_local, next_bit=bits[0]),
            scalars(zero, own_bits[0]),
            [samples, leaf_maps, local_blocks],
            [column_block((count, rows, width), chunk), whole(leaf_maps.shape), whole(local_blocks.shape)],
            [half, half],
            [pltpu.VMEM(block.shape, jnp.bfloat16), pltpu.VMEM(block.shape, jnp.bfloat16)],
        ))
    top = n_cross - 1
    adj = []
    for chunk in range(CHUNKS):
        adj.append(call(
            functools.partial(adjoint_first_kernel, count=count, bit=bits[top]),
            scalars(own_bits[top], zero),
            [echoes, spread_maps, sources[top][0]],
            [column_block((count, rows, width), chunk), whole(spread_maps.shape), blocks_spec(top)],
            [half, half],
            [pltpu.VMEM(block.shape, jnp.bfloat16)],
        ))

    full = jax.ShapeDtypeStruct(samples.shape, jnp.bfloat16)
    image_field = None
    for step in range(n_cross):
        index = step
        bit, axis = bits[index], axes[index]
        last = index == n_cross - 1
        next_bit = 0 if last else bits[index + 1]
        earlier = None
        for chunk in range(CHUNKS):
            stay, leave = fwd[chunk]
            arrived = from_partner(in_order(leave, earlier if axis == "src" and bit > 0 else None), axis, bit)
            earlier = arrived
            inputs = [stay, arrived, sources[index][0]]
            specs = [half_spec, half_spec, blocks_spec(index)]
            if last:
                inputs.append(spread_maps)
                specs.append(whole(spread_maps.shape))
            kernel = functools.partial(forward_cross_kernel, count=count, bit=bit, next_bit=next_bit, last=last)
            if last:
                (image_field,) = into_columns(
                    kernel, scalars(own_bits[index], zero), inputs, specs,
                    [pltpu.VMEM(block.shape, jnp.bfloat16)], full, block, chunk, image_field)
            else:
                fwd[chunk] = tuple(call(
                    kernel,
                    scalars(own_bits[index], own_bits[index + 1]),
                    inputs,
                    specs,
                    [half, half],
                    [pltpu.VMEM(block.shape, jnp.bfloat16)],
                ))

        index = top - step
        earlier = None
        for chunk in range(CHUNKS):
            kept, leave = adj[chunk]
            arrived = from_partner(in_order(leave, earlier if axes[index] == "src" and bits[index] > 0 else None),
                                   axes[index], bits[index])
            earlier = arrived
            if index > 0:
                adj[chunk] = tuple(call(
                    functools.partial(adjoint_cross_kernel, count=count, bit=bits[index - 1], prev_bit=bits[index]),
                    scalars(own_bits[index - 1], own_bits[index]),
                    [kept, arrived, sources[index - 1][0]],
                    [half_spec, half_spec, blocks_spec(index - 1)],
                    [half, half],
                    [],
                ))
            else:
                adj[chunk] = (kept, arrived)

    aperture_field = None
    for chunk in range(CHUNKS):
        kept, arrived = adj[chunk]
        (aperture_field,) = into_columns(
            functools.partial(adjoint_local_kernel, count=count, levels=levels_local, prev_bit=bits[0]),
            scalars(zero, own_bits[0]),
            [kept, arrived, local_blocks, leaf_maps],
            [half_spec, half_spec, whole(local_blocks.shape), whole(leaf_maps.shape)],
            [pltpu.VMEM(block.shape, jnp.bfloat16), pltpu.VMEM(block.shape, jnp.bfloat16)],
            full, block, chunk, aperture_field)
    return (image_field, aperture_field)


def solution(mesh):
    return jax.shard_map(
        per_device,
        mesh=mesh,
        in_specs=(
            P(("src", "tgt"), None, None),
            P(("src", "tgt"), None, None),
            P(("src", "tgt"), None, None),
            P(None, ("src", "tgt"), None, None),
            P(None, "src", None, None),
            P(None, ("src", "tgt"), None, None),
            P(("src", "tgt"), None, None),
        ),
        out_specs=(P(("src", "tgt"), None, None), P(("src", "tgt"), None, None)),
        check_vma=False,
    )
```

```python
import functools

import jax
import jax.numpy as jnp
from jax import lax
from jax.experimental import pallas as pl
from jax.experimental.pallas import tpu as pltpu
from jax.sharding import PartitionSpec as P

CHUNKS = 2


def from_partner(x, axis, apart):
    return lax.ppermute(x, axis, [(i, i ^ 1 << apart) for i in range(lax.axis_size(axis))])


def expand(r, bit, j):
    return ((r >> bit) << (bit + 1)) | (j << bit) | (r & ((1 << bit) - 1))


def compress(p, bit):
    return ((p >> (bit + 1)) << bit) | (p & ((1 << bit) - 1))


def mm(w, x):
    return jnp.dot(w, x, preferred_element_type=jnp.float32).astype(jnp.bfloat16)


def mm_t(w, x):
    return mm(w.astype(jnp.float32).T.astype(jnp.bfloat16), x)


def embed_tile(stored):
    half = stored.shape[-1] // 2
    lane = lax.broadcasted_iota(jnp.int32, stored.shape, 1)
    top = jnp.where(lane < half, stored, -stored)
    bottom = pltpu.roll(stored, half, 1)
    return jnp.concatenate([top, bottom], axis=0)


def block_pair(stored, own):
    width = stored.shape[-1] // 2
    first = embed_tile(stored[:, :width])
    second = embed_tile(stored[:, width:])
    if isinstance(own, int) and own == 0:
        return first, second
    return jnp.where(own == 0, first, second), jnp.where(own == 0, second, first)


def forward_weight(stored, own):
    first, second = block_pair(stored, own)
    return jnp.concatenate([first, second], axis=1)


def write_split(value_of, count, bit, own, stay_ref, leave_ref):
    for p in range(count):
        r = compress(p, bit)
        here = ((p >> bit) & 1) == own

        @pl.when(here)
        def _():
            stay_ref[r] = value_of(p)

        @pl.when(jnp.logical_not(here))
        def _():
            leave_ref[r] = value_of(p)


def read_split(kept_ref, arrived_ref, bit, own):
    def value_of(p):
        r = compress(p, bit)
        return jnp.where(((p >> bit) & 1) == own, kept_ref[r], arrived_ref[r])

    return value_of


def adjoint_pair(value_of, blocks_ref, bit, r, own):
    lower, upper = expand(r, bit, 0), expand(r, bit, 1)
    stacked = jnp.concatenate([value_of(lower), value_of(upper)], axis=0)
    first_lower, second_lower = block_pair(blocks_ref[lower], 0)
    first_upper, second_upper = block_pair(blocks_ref[upper], 0)
    first = mm_t(jnp.concatenate([first_lower, first_upper], axis=0), stacked)
    second = mm_t(jnp.concatenate([second_lower, second_upper], axis=0), stacked)
    if isinstance(own, int) and own == 0:
        return first, second
    return jnp.where(own == 0, first, second), jnp.where(own == 0, second, first)


def forward_local_kernel(sc_ref, samples_ref, leaf_ref, local_ref, stay_ref, leave_ref, buf_a, buf_b,
                         *, count, levels, next_bit):
    for p in range(count):
        buf_a[p] = mm(embed_tile(leaf_ref[p]), samples_ref[p])
    src, dst = buf_a, buf_b
    for level in range(levels):
        for r in range(count // 2):
            p0, p1 = expand(r, level, 0), expand(r, level, 1)
            stacked = jnp.concatenate([src[p0], src[p1]], axis=0)
            dst[p0] = mm(forward_weight(local_ref[level, p0], 0), stacked)
            dst[p1] = mm(forward_weight(local_ref[level, p1], 0), stacked)
        src, dst = dst, src
    write_split(lambda p: src[p], count, next_bit, sc_ref[1], stay_ref, leave_ref)


def forward_cross_kernel(sc_ref, kept_ref, arrived_ref, blocks_ref, *rest, count, bit, next_bit, last, prior=False):
    if last:
        spread_ref, out_ref, buf = (rest[0],) + rest[1 + prior:]
    else:
        stay_ref, leave_ref, buf = rest
    own = sc_ref[0]
    for r in range(count // 2):
        stacked = jnp.concatenate([kept_ref[r], arrived_ref[r]], axis=0)
        for j in range(2):
            p = expand(r, bit, j)
            buf[p] = mm(forward_weight(blocks_ref[p], own), stacked)
    if last:
        for p in range(count):
            out_ref[p] = mm(embed_tile(spread_ref[p]), buf[p])
    else:
        write_split(lambda p: buf[p], count, next_bit, sc_ref[1], stay_ref, leave_ref)


def adjoint_first_kernel(sc_ref, echoes_ref, spread_ref, blocks_ref, kept_ref, leave_ref, buf, *, count, bit):
    for p in range(count):
        buf[p] = mm_t(embed_tile(spread_ref[p]), echoes_ref[p])
    own = sc_ref[0]
    for r in range(count // 2):
        kept_ref[r], leave_ref[r] = adjoint_pair(lambda p: buf[p], blocks_ref, bit, r, own)


def adjoint_cross_kernel(sc_ref, prev_kept_ref, prev_arrived_ref, blocks_ref, kept_ref, leave_ref,
                         *, count, bit, prev_bit):
    value_of = read_split(prev_kept_ref, prev_arrived_ref, prev_bit, sc_ref[1])
    own = sc_ref[0]
    for r in range(count // 2):
        kept_ref[r], leave_ref[r] = adjoint_pair(value_of, blocks_ref, bit, r, own)


def adjoint_local_kernel(sc_ref, prev_kept_ref, prev_arrived_ref, local_ref, leaf_ref, *rest,
                         count, levels, prev_bit, prior=False):
    out_ref, buf_a, buf_b = rest[prior:]
    value_of = read_split(prev_kept_ref, prev_arrived_ref, prev_bit, sc_ref[1])
    for p in range(count):
        buf_a[p] = value_of(p)
    src, dst = buf_a, buf_b
    for level in reversed(range(levels)):
        for r in range(count // 2):
            first, second = adjoint_pair(lambda p: src[p], local_ref.at[level], level, r, 0)
            dst[expand(r, level, 0)] = first
            dst[expand(r, level, 1)] = second
        src, dst = dst, src
    for p in range(count):
        out_ref[p] = mm_t(embed_tile(leaf_ref[p]), src[p])


def whole(shape):
    return pl.BlockSpec(shape, lambda i, sc, n=len(shape): (0,) * n)


def column_block(shape, chunk):
    return pl.BlockSpec(shape, lambda i, sc, c=chunk: (0, 0, c))


def level_block(shape, level, count, grouped):
    if grouped:
        return pl.BlockSpec((None, count) + tuple(shape[2:]), lambda i, sc, v=level: (v, sc[2], 0, 0))
    return pl.BlockSpec((None, count) + tuple(shape[2:]), lambda i, sc, v=level: (v, 0, 0, 0))


def call(kernel, scalars, inputs, in_specs, out_shapes, scratch, out_specs=None, aliases=None):
    grid_spec = pltpu.PrefetchScalarGridSpec(
        num_scalar_prefetch=1,
        grid=(1,),
        in_specs=in_specs,
        out_specs=out_specs or [whole(s.shape) for s in out_shapes],
        scratch_shapes=scratch,
    )
    return pl.pallas_call(
        kernel,
        grid_spec=grid_spec,
        out_shape=out_shapes,
        input_output_aliases=aliases or {},
        compiler_params=pltpu.CompilerParams(vmem_limit_bytes=48 * 1024 * 1024),
    )(scalars, *inputs)


def into_columns(kernel, scalars, inputs, in_specs, scratch, full, part, chunk, prior):
    if prior is None:
        return call(kernel, scalars, inputs, in_specs, [full], scratch,
                    out_specs=[column_block(part.shape, chunk)])
    return call(functools.partial(kernel, prior=True), scalars, inputs[:len(in_specs)] + [prior],
                in_specs + [pl.BlockSpec(memory_space=pl.ANY)], [full], scratch,
                out_specs=[column_block(part.shape, chunk)], aliases={1 + len(in_specs): 0})


def per_device(samples, echoes, leaf_maps, local_blocks, cross_blocks, outer_blocks, spread_maps):
    levels_local = local_blocks.shape[0]
    inner_bits = cross_blocks.shape[0]
    outer_bits = outer_blocks.shape[0]
    count, rows, columns = samples.shape
    width = columns // CHUNKS
    tgt_index = lax.axis_index("tgt")
    src_index = lax.axis_index("src")
    bits = [m for m in range(inner_bits)] + [m for m in range(outer_bits)]
    axes = ["tgt"] * inner_bits + ["src"] * outer_bits
    own_bits = [tgt_index >> m & 1 for m in range(inner_bits)] + [src_index >> m & 1 for m in range(outer_bits)]
    sources = [(cross_blocks, m, True) for m in range(inner_bits)] + [(outer_blocks, m, False) for m in range(outer_bits)]
    n_cross = len(bits)

    def scalars(first, second):
        return jnp.stack([first, second, tgt_index]).astype(jnp.int32)

    def blocks_spec(index):
        array, level, grouped = sources[index]
        return level_block(array.shape, level, count, grouped)

    block = jax.ShapeDtypeStruct((count, rows, width), jnp.bfloat16)
    half = jax.ShapeDtypeStruct((count // 2, rows, width), jnp.bfloat16)
    half_spec = whole(half.shape)
    zero = tgt_index * 0

    def in_order(leave, earlier):
        if earlier is None:
            return leave
        leave, _ = lax.optimization_barrier((leave, earlier))
        return leave

    fwd = []
    for chunk in range(CHUNKS):
        fwd.append(call(
            functools.partial(forward_local_kernel, count=count, levels=levels_local, next_bit=bits[0]),
            scalars(zero, own_bits[0]),
            [samples, leaf_maps, local_blocks],
            [column_block((count, rows, width), chunk), whole(leaf_maps.shape), whole(local_blocks.shape)],
            [half, half],
            [pltpu.VMEM(block.shape, jnp.bfloat16), pltpu.VMEM(block.shape, jnp.bfloat16)],
        ))
    top = n_cross - 1
    adj = []
    for chunk in range(CHUNKS):
        adj.append(call(
            functools.partial(adjoint_first_kernel, count=count, bit=bits[top]),
            scalars(own_bits[top], zero),
            [echoes, spread_maps, sources[top][0]],
            [column_block((count, rows, width), chunk), whole(spread_maps.shape), blocks_spec(top)],
            [half, half],
            [pltpu.VMEM(block.shape, jnp.bfloat16)],
        ))

    full = jax.ShapeDtypeStruct(samples.shape, jnp.bfloat16)
    image_field = None
    for step in range(n_cross):
        index = step
        bit, axis = bits[index], axes[index]
        last = index == n_cross - 1
        next_bit = 0 if last else bits[index + 1]
        earlier = None
        for chunk in range(CHUNKS):
            stay, leave = fwd[chunk]
            arrived = from_partner(in_order(leave, earlier if axis == "src" and bit > 0 else None), axis, bit)
            earlier = arrived
            inputs = [stay, arrived, sources[index][0]]
            specs = [half_spec, half_spec, blocks_spec(index)]
            if last:
                inputs.append(spread_maps)
                specs.append(whole(spread_maps.shape))
            kernel = functools.partial(forward_cross_kernel, count=count, bit=bit, next_bit=next_bit, last=last)
            if last:
                (image_field,) = into_columns(
                    kernel, scalars(own_bits[index], zero), inputs, specs,
                    [pltpu.VMEM(block.shape, jnp.bfloat16)], full, block, chunk, image_field)
            else:
                fwd[chunk] = tuple(call(
                    kernel,
                    scalars(own_bits[index], own_bits[index + 1]),
                    inputs,
                    specs,
                    [half, half],
                    [pltpu.VMEM(block.shape, jnp.bfloat16)],
                ))

        index = top - step
        earlier = None
        for chunk in range(CHUNKS):
            kept, leave = adj[chunk]
            arrived = from_partner(in_order(leave, earlier if axes[index] == "src" and bits[index] > 0 else None),
                                   axes[index], bits[index])
            earlier = arrived
            if index > 0:
                adj[chunk] = tuple(call(
                    functools.partial(adjoint_cross_kernel, count=count, bit=bits[index - 1], prev_bit=bits[index]),
                    scalars(own_bits[index - 1], own_bits[index]),
                    [kept, arrived, sources[index - 1][0]],
                    [half_spec, half_spec, blocks_spec(index - 1)],
                    [half, half],
                    [],
                ))
            else:
                adj[chunk] = (kept, arrived)

    aperture_field = None
    for chunk in range(CHUNKS):
        kept, arrived = adj[chunk]
        (aperture_field,) = into_columns(
            functools.partial(adjoint_local_kernel, count=count, levels=levels_local, prev_bit=bits[0]),
            scalars(zero, own_bits[0]),
            [kept, arrived, local_blocks, leaf_maps],
            [half_spec, half_spec, whole(local_blocks.shape), whole(leaf_maps.shape)],
            [pltpu.VMEM(block.shape, jnp.bfloat16), pltpu.VMEM(block.shape, jnp.bfloat16)],
            full, block, chunk, aperture_field)
    return (image_field, aperture_field)


def solution(mesh):
    return jax.shard_map(
        per_device,
        mesh=mesh,
        in_specs=(
            P(("src", "tgt"), None, None),
            P(("src", "tgt"), None, None),
            P(("src", "tgt"), None, None),
            P(None, ("src", "tgt"), None, None),
            P(None, "src", None, None),
            P(None, ("src", "tgt"), None, None),
            P(("src", "tgt"), None, None),
        ),
        out_specs=(P(("src", "tgt"), None, None), P(("src", "tgt"), None, None)),
        check_vma=False,
    )
```
